32 devices in a mesh: groups: 2 (over x), shard: 16 (over z, y, core).
Axes of the slice: x: 2, y: 2, z: 4, core: 2. Of those that a mesh axis runs over, the one named last changes fastest.
Arguments:
- particles: float32 [64, 64, 4096], P(('groups', 'shard')), parts along dimension 0, may hold values from -6 to 6
- slot_target: int32 [64], P('groups'), parts along dimension 0, may hold values from -1 to 15, as said below
- slot_defocus_level: int32 [64], P('groups'), parts along dimension 0, may hold values from 0 to 15
- defocus: float32 [32], P('groups'), parts along dimension 0, may hold values from 2 to 20
- ref_library: bfloat16 [16, 16, 65536], P('groups', None, 'shard'), parts along dimension 0, may hold values from -6 to 6
- rotation_list: int32 [16, 8], P('groups'), parts along dimension 0, may hold values from 0 to 15
Outputs:
- scores: float32 [64, 8, 8], P(('groups', 'shard')), parts along dimension 0
- best_scores: float32 [64, 8], P(('groups', 'shard')), parts along dimension 0
The draws below stay inside these ranges and needn't reach their ends.
There are 2 independent parts, one for each index of `groups`. The reference program is written for one: setup_inputs(seed, part) draws one part's arguments, and reference() takes and returns one part's arrays. A program takes and returns all parts, laid end to end along the dimension named above; each array names one. Nothing has to cross between parts.
Inputs may be any that keep to these rules, and one draw needn't show every extreme that they name: `slot_target`: every position 0 to 15 is held by exactly one slot; the other slots hold -1. A device holds 0 to 2 occupied slots of its own, and some device holds 2.
All inputs are finite; a program needn't handle non-finite values.
Results may differ from the reference program's by a relative error of at most 0.0049.
Values may be sent and summed in bfloat16 or wider, within the bound.
No kernel may reach another device: no remote copies, remote signals or barrier semaphores. Data moves between devices by JAX's collectives and lax.ppermute only.
A program may use at most 128 MiB of HBM per device.

```python
import math
import jax
import jax.numpy as jnp
from jax import lax

BOX = 64
BAND = 32
SHIFTS = 8
CLASSES = 8
LIB = 16
ROT = 8
BINS = 16
PART_DEV = 1
CAP = 2
SLOTS = 32
PARTICLES = 16


def draw_slot_target(key, part):
    devices = SLOTS // CAP
    total_count = devices * PART_DEV
    key_order, key_offsets, key_slots, key_shuffle = jax.random.split(key, 4)
    device_order = jax.random.permutation(key_order, devices)
    half_count = devices // 2
    offsets = jax.random.randint(key_offsets, (half_count,), -PART_DEV, PART_DEV + 1)
    offsets = offsets.at[0].set(PART_DEV)
    paired = jnp.concatenate([PART_DEV + offsets, PART_DEV - offsets]).astype(jnp.int32)
    counts = jnp.zeros((devices,), jnp.int32).at[device_order].set(paired)
    slot_ranks = jax.vmap(lambda one_key: jax.random.permutation(one_key, CAP))(jax.random.split(key_slots, devices))
    occupied = (slot_ranks < counts[:, None]).reshape(-1)
    running = jnp.cumsum(occupied.astype(jnp.int32)) - 1
    shuffle = jax.random.permutation(key_shuffle, total_count)
    return jnp.where(occupied, shuffle[jnp.clip(running, 0, total_count - 1)], -1).astype(jnp.int32)


def plant(result, stream_key, least, top_value):
    longest = result.shape.index(max(result.shape))
    spots = []
    for shift in (0, 1):
        where = [jax.random.randint(jax.random.fold_in(stream_key, axis), (), 0, length) for axis, length in enumerate(result.shape)]
        where[longest] = (where[longest] + shift) % result.shape[longest]
        spots.append(tuple(where))
    return result.at[spots[0]].set(least).at[spots[1]].set(top_value)


def steps_of(rng, shape, pieces, smallest, largest):
    gain, own = 1.0, jax.random.fold_in(rng, 6)
    for axis_at, shards_of in pieces:
        heights = jnp.exp(jax.random.uniform(jax.random.fold_in(own, axis_at), (shards_of,), jnp.float32, smallest / len(pieces), largest / len(pieces)))
        gain = gain * jnp.repeat(heights, shape[axis_at] // shards_of).reshape([-1 if axis == axis_at else 1 for axis in range(len(shape))])
    return gain


def centred(stream_key, extent, scale, reach, cuts=(), kind=jnp.bfloat16):
    result = scale * jax.random.normal(stream_key, extent, jnp.float32)
    if cuts:
        result = result * steps_of(stream_key, extent, cuts, -0.22, 0.18)
    return jnp.clip(result, -reach, reach).astype(kind)


def setup_inputs(seed: int = 0, part: int = 0) -> dict:
    keys = jax.random.split(jax.random.key(seed), 7)
    part_splits = jax.random.split(jax.random.fold_in(keys[6], part), 7)
    particles = centred(part_splits[0], (SLOTS, BOX, BOX * BOX), 1.0, 6.0, ((0, 16),), jnp.float32)
    slot_target = draw_slot_target(jax.random.fold_in(jax.random.fold_in(keys[6], part), 71), part)
    slot_defocus_level = plant(jax.random.randint(part_splits[2], (SLOTS,), 0, BINS), jax.random.fold_in(part_splits[2], 1), 0, BINS - 1).astype(jnp.int32)
    defocus = jnp.clip(jnp.exp(jax.random.uniform(part_splits[3], (BINS,), jnp.float32, math.log(2.0), math.log(20.0))), 2.0, 20.0)
    ref_library = centred(part_splits[4], (CLASSES, LIB, 2 * BAND * BAND * BAND), 1.0, 6.0, ((2, 16),))
    rotation_list = plant(jax.random.randint(part_splits[5], (CLASSES, ROT), 0, LIB), jax.random.fold_in(part_splits[5], 1), 0, LIB - 1).astype(jnp.int32)
    return {"particles": particles, "slot_target": slot_target, "slot_defocus_level": slot_defocus_level, "defocus": defocus, "ref_library": ref_library, "rotation_list": rotation_list}


def signed_band(band_size):
    return jnp.arange(band_size, dtype=jnp.int32) - band_size // 2

def table_pair(outer_loop_index, inner_index, box_edge):
    phase_index = outer_loop_index[:, None] * inner_index[None, :] % box_edge
    angles = phase_index.astype(jnp.float32) * (2.0 * jnp.pi / box_edge)
    return (jnp.cos(angles).astype(jnp.bfloat16), jnp.sin(angles).astype(jnp.bfloat16))

def spectral_product(form, left, right):
    return jnp.einsum(form, left.astype(jnp.float32), right.astype(jnp.float32))

def forward_spectra(volumes):
    batch_size, box_edge = (volumes.shape[0], volumes.shape[1])
    cosine_forward, sine_forward = table_pair(signed_band(BAND), jnp.arange(box_edge, dtype=jnp.int32), box_edge)
    density_volume = volumes.astype(jnp.bfloat16)
    leading_real = spectral_product('qw,rwl->rql', cosine_forward, density_volume).astype(jnp.bfloat16)
    leading_imaginary = (-spectral_product('qw,rwl->rql', sine_forward, density_volume)).astype(jnp.bfloat16)
    leading_real = leading_real.reshape(batch_size, BAND, box_edge, box_edge)
    leading_imaginary = leading_imaginary.reshape(batch_size, BAND, box_edge, box_edge)
    second_real = (spectral_product('jy,nkyz->nkjz', cosine_forward, leading_real) + spectral_product('jy,nkyz->nkjz', sine_forward, leading_imaginary)).astype(jnp.bfloat16)
    second_imag = (spectral_product('jy,nkyz->nkjz', cosine_forward, leading_imaginary) - spectral_product('jy,nkyz->nkjz', sine_forward, leading_real)).astype(jnp.bfloat16)
    third_real = spectral_product('nkjz,lz->nkjl', second_real, cosine_forward) + spectral_product('nkjz,lz->nkjl', second_imag, sine_forward)
    third_imag = spectral_product('nkjz,lz->nkjl', second_imag, cosine_forward) - spectral_product('nkjz,lz->nkjl', second_real, sine_forward)
    spectrum = jnp.stack([third_real, third_imag], axis=1).astype(jnp.bfloat16)
    return spectrum.reshape(batch_size, 2, BAND * BAND * BAND)

def score_rows(spectra, bin_ids, defocus, fetch_class):
    batch_size = spectra.shape[0]
    volume_size = BAND * BAND * BAND
    band_index = signed_band(BAND).astype(jnp.float32)
    radius = (band_index[:, None, None] ** 2 + band_index[None, :, None] ** 2 + band_index[None, None, :] ** 2).reshape(-1) / (BAND / 2) ** 2
    chosen_defocus = lax.optimization_barrier(jnp.sum(jnp.where(bin_ids[:, None] == jnp.arange(defocus.shape[0], dtype=jnp.int32)[None, :], defocus[None, :], jnp.float32(0.0)), axis=1))
    contrast = -jnp.sin(chosen_defocus[:, None] * radius[None, :] + 0.07)
    spec_real = spectra[:, 0].astype(jnp.float32)
    spec_imag = spectra[:, 1].astype(jnp.float32)
    weight_real, weight_imag = lax.optimization_barrier(((contrast * spec_real).astype(jnp.bfloat16), (-contrast * spec_imag).astype(jnp.bfloat16)))
    weight_real = weight_real.astype(jnp.float32)[:, None, :]
    weight_imag = weight_imag.astype(jnp.float32)[:, None, :]
    energy_particle = lax.optimization_barrier(jnp.sum(spec_real * spec_real + spec_imag * spec_imag, axis=1))
    cos_inv, sin_inv = table_pair(signed_band(SHIFTS), signed_band(BAND), BOX)
    score_scale = float(BAND) ** 1.5
    results = []
    for class_id in range(CLASSES):
        references = fetch_class(class_id)
        ref_real = references[:, :volume_size].astype(jnp.float32)
        ref_imag = references[:, volume_size:].astype(jnp.float32)
        magnitude = ref_real * ref_real + ref_imag * ref_imag
        energy_ref = lax.dot_general(contrast * contrast, magnitude, (((1,), (1,)), ((), ())), precision=lax.Precision.HIGHEST)
        prod_real = (weight_real * ref_real[None] - weight_imag * ref_imag[None]).astype(jnp.bfloat16)
        prod_imag = (weight_real * ref_imag[None] + weight_imag * ref_real[None]).astype(jnp.bfloat16)
        prod_real = prod_real.reshape(batch_size, ROT, BAND, BAND, BAND)
        prod_imag = prod_imag.reshape(batch_size, ROT, BAND, BAND, BAND)
        rows_real = (spectral_product('sk,nrkjl->nrsjl', cos_inv, prod_real) - spectral_product('sk,nrkjl->nrsjl', sin_inv, prod_imag)).astype(jnp.bfloat16)
        rows_imag = (spectral_product('sk,nrkjl->nrsjl', cos_inv, prod_imag) + spectral_product('sk,nrkjl->nrsjl', sin_inv, prod_real)).astype(jnp.bfloat16)
        cols_real = (spectral_product('tj,nrsjl->nrstl', cos_inv, rows_real) - spectral_product('tj,nrsjl->nrstl', sin_inv, rows_imag)).astype(jnp.bfloat16)
        cols_imag = (spectral_product('tj,nrsjl->nrstl', cos_inv, rows_imag) + spectral_product('tj,nrsjl->nrstl', sin_inv, rows_real)).astype(jnp.bfloat16)
        correlation = spectral_product('nrstl,ul->nrstu', cols_real, cos_inv) - spectral_product('nrstl,ul->nrstu', cols_imag, sin_inv)
        peak_value = lax.optimization_barrier(jnp.max(correlation.reshape(batch_size, ROT, -1), axis=2))
        results.append(score_scale * peak_value * lax.rsqrt(energy_particle[:, None] * energy_ref + 1e-06))
    return jnp.stack(results, axis=1)

def pick_rows(library, listed):
    return library[listed]

def reference(particles, slot_target, slot_defocus_level, defocus, ref_library, rotation_list):
    occupied = slot_target >= 0
    source = jnp.zeros((PARTICLES,), jnp.int32).at[jnp.where(occupied, slot_target, PARTICLES)].set(jnp.arange(SLOTS, dtype=jnp.int32), mode='drop')
    chosen = jax.vmap(pick_rows)(ref_library, rotation_list)

    def fetch_class(class_id):
        return chosen[class_id]

    def score_one(slot_index):
        density_volume = lax.dynamic_slice_in_dim(particles, slot_index.astype(jnp.int32), 1, 0)
        bin_ids = lax.dynamic_slice_in_dim(slot_defocus_level, slot_index.astype(jnp.int32), 1, 0)
        return score_rows(forward_spectra(density_volume), bin_ids, defocus, fetch_class)[0]
    balanced = lax.map(score_one, source)
    picked = balanced[jnp.maximum(slot_target, 0)]
    scores = jnp.where(occupied[:, None, None], picked, jnp.float32(0.0))
    return (scores, lax.optimization_barrier(jnp.max(scores, axis=2)))
```

```python
import numpy as np
import jax
import jax.numpy as jnp
from jax import lax
from jax.sharding import PartitionSpec as P

BOX = 64
BAND = 32
SHIFTS = 8
PART_DEV = 1


def signed_band(band_size):
    return jnp.arange(band_size, dtype=jnp.int32) - band_size // 2


def table_pair(outer_loop_index, inner_index, box_edge):
    phase_index = outer_loop_index[:, None] * inner_index[None, :] % box_edge
    angles = phase_index.astype(jnp.float32) * (2.0 * jnp.pi / box_edge)
    return (jnp.cos(angles).astype(jnp.bfloat16), jnp.sin(angles).astype(jnp.bfloat16))


def spectral_product(form, left, right):
    return jnp.einsum(form, left, right, preferred_element_type=jnp.float32)


def forward_spectra(volumes):
    batch_size, box_edge = (volumes.shape[0], volumes.shape[1])
    cosine_forward, sine_forward = table_pair(
        signed_band(BAND), jnp.arange(box_edge, dtype=jnp.int32), box_edge
    )
    density_volume = volumes.astype(jnp.bfloat16)
    leading_real = spectral_product("qw,rwl->rql", cosine_forward, density_volume).astype(
        jnp.bfloat16
    )
    leading_imaginary = (-spectral_product("qw,rwl->rql", sine_forward, density_volume)).astype(
        jnp.bfloat16
    )
    leading_real = leading_real.reshape(batch_size, BAND, box_edge, box_edge)
    leading_imaginary = leading_imaginary.reshape(batch_size, BAND, box_edge, box_edge)
    second_real = (
        spectral_product("jy,nkyz->nkjz", cosine_forward, leading_real)
        + spectral_product("jy,nkyz->nkjz", sine_forward, leading_imaginary)
    ).astype(jnp.bfloat16)
    second_imag = (
        spectral_product("jy,nkyz->nkjz", cosine_forward, leading_imaginary)
        - spectral_product("jy,nkyz->nkjz", sine_forward, leading_real)
    ).astype(jnp.bfloat16)
    third_real = spectral_product("nkjz,lz->nkjl", second_real, cosine_forward) + spectral_product(
        "nkjz,lz->nkjl", second_imag, sine_forward
    )
    third_imag = spectral_product("nkjz,lz->nkjl", second_imag, cosine_forward) - spectral_product(
        "nkjz,lz->nkjl", second_real, sine_forward
    )
    spectrum = jnp.stack([third_real, third_imag], axis=1).astype(jnp.bfloat16)
    return spectrum.reshape(batch_size, 2, BAND * BAND * BAND)


def plane_table():
    k = signed_band(BAND)
    t = signed_band(SHIFTS)
    phase = (
        t[None, None, :, None] * k[:, None, None, None]
        + t[None, None, None, :] * k[None, :, None, None]
    ) % BOX
    angles = phase.astype(jnp.float32) * (2.0 * jnp.pi / BOX)
    shape = (BAND * BAND, SHIFTS * SHIFTS)
    return jnp.concatenate(
        [jnp.cos(angles).reshape(shape), jnp.sin(angles).reshape(shape)], axis=1
    ).astype(jnp.bfloat16)


def score_block(spectra, bin_ids, defocus, refs):
    n_part = spectra.shape[0]
    n_ref = refs.shape[0]
    volume_size = BAND * BAND * BAND
    band_index = signed_band(BAND).astype(jnp.float32)
    radius = (
        band_index[:, None, None] ** 2
        + band_index[None, :, None] ** 2
        + band_index[None, None, :] ** 2
    ).reshape(-1) / (BAND / 2) ** 2
    chosen_defocus = jnp.sum(
        jnp.where(
            bin_ids[:, None] == jnp.arange(defocus.shape[0], dtype=jnp.int32)[None, :],
            defocus[None, :],
            jnp.float32(0.0),
        ),
        axis=1,
    )
    contrast = -jnp.sin(chosen_defocus[:, None] * radius[None, :] + 0.07)
    spec_real = spectra[:, 0].astype(jnp.float32)
    spec_imag = spectra[:, 1].astype(jnp.float32)
    weight_real = (contrast * spec_real).astype(jnp.bfloat16).astype(jnp.float32)
    weight_imag = (-contrast * spec_imag).astype(jnp.bfloat16).astype(jnp.float32)
    energy_particle = jnp.sum(spec_real * spec_real + spec_imag * spec_imag, axis=1)
    ref_real = refs[:, :volume_size].astype(jnp.float32)
    ref_imag = refs[:, volume_size:].astype(jnp.float32)
    magnitude = ref_real * ref_real + ref_imag * ref_imag
    energy_ref = lax.dot_general(
        contrast * contrast, magnitude, (((1,), (1,)), ((), ())), precision=lax.Precision.HIGHEST
    )
    wr = weight_real[:, None, :]
    wi = weight_imag[:, None, :]
    prod_real = (wr * ref_real[None] - wi * ref_imag[None]).astype(jnp.bfloat16)
    prod_imag = (wr * ref_imag[None] + wi * ref_real[None]).astype(jnp.bfloat16)
    product = jnp.stack([prod_real, prod_imag], axis=2).reshape(
        n_part, n_ref, 2, BAND, BAND * BAND
    )
    planes = spectral_product("ijakl,lm->ijakm", product, plane_table())
    half = SHIFTS * SHIFTS
    plane_real = planes[:, :, 0, :, :half] - planes[:, :, 1, :, half:]
    plane_imag = planes[:, :, 0, :, half:] + planes[:, :, 1, :, :half]
    cos_inv, sin_inv = table_pair(signed_band(SHIFTS), signed_band(BAND), BOX)
    correlation = jnp.einsum(
        "tk,ijkm->ijtm", cos_inv.astype(jnp.float32), plane_real,
        precision=lax.Precision.HIGHEST,
    ) - jnp.einsum(
        "tk,ijkm->ijtm", sin_inv.astype(jnp.float32), plane_imag,
        precision=lax.Precision.HIGHEST,
    )
    peak_value = jnp.max(correlation.reshape(n_part, n_ref, -1), axis=2)
    score_scale = float(BAND) ** 1.5
    return score_scale * peak_value * lax.rsqrt(energy_particle[:, None] * energy_ref + 1e-06)


def pick_rows(library, listed):
    return library[listed]


def ref_groups(shards, particles, refs):
    best = None
    for groups in range(1, shards + 1):
        if shards % groups or refs % groups or particles % (shards // groups):
            continue
        cost = particles * groups // shards + refs // groups
        if best is None or cost < best[0]:
            best = (cost, groups)
    return best[1]


def per_device(particles, slot_target, slot_defocus_level, defocus, ref_library, rotation_list):
    shards = lax.axis_size("shard")
    my_index = lax.axis_index("shard")
    slots_here = particles.shape[0]
    positions = PART_DEV * shards
    every_slot = slot_target.shape[0]
    classes, rotations = rotation_list.shape
    n_refs = classes * rotations
    r_groups = ref_groups(shards, positions, n_refs)
    p_groups = shards // r_groups
    part_block = positions // p_groups
    ref_block = n_refs // r_groups
    my_pblock = my_index // r_groups
    dest_rblock = np.arange(shards) % r_groups
    dest_pblock = np.arange(shards) // r_groups

    own_target = lax.dynamic_slice_in_dim(slot_target, my_index * slots_here, slots_here, 0)
    occupied = own_target >= 0

    chosen = jax.vmap(pick_rows)(ref_library, rotation_list)
    piece = chosen.shape[-1]
    ref_send = chosen.reshape(r_groups, ref_block, piece)[dest_rblock]
    ref_got = lax.all_to_all(ref_send, "shard", 0, 0, tiled=True)
    refs = ref_got.transpose(1, 0, 2).reshape(ref_block, shards * piece)

    source = (
        jnp.zeros((positions,), jnp.int32)
        .at[jnp.where(slot_target >= 0, slot_target, positions)]
        .set(jnp.arange(every_slot, dtype=jnp.int32), mode="drop")
    )
    flattened = forward_spectra(particles).reshape(slots_here, -1)
    pieces = lax.all_to_all(flattened, "shard", split_axis=1, concat_axis=0, tiled=True)
    part_send = pieces[source].reshape(p_groups, part_block, piece)[dest_pblock]
    part_got = lax.all_to_all(part_send, "shard", 0, 0, tiled=True)
    spectra = part_got.transpose(1, 0, 2).reshape(part_block, 2, -1)

    my_sources = lax.dynamic_slice_in_dim(source, my_pblock * part_block, part_block, 0)
    block_scores = score_block(spectra, slot_defocus_level[my_sources], defocus, refs)
    all_scores = lax.all_gather(block_scores, "shard", axis=0, tiled=False)
    all_scores = (
        all_scores.reshape(p_groups, r_groups, part_block, ref_block)
        .transpose(0, 2, 1, 3)
        .reshape(positions, classes, rotations)
    )
    scores = jnp.where(
        occupied[:, None, None], all_scores[jnp.maximum(own_target, 0)], jnp.float32(0.0)
    )
    return (scores, jnp.max(scores, axis=2))


def solution(mesh):
    in_specs = (
        P(("groups", "shard"), None, None),
        P("groups"),
        P("groups"),
        P("groups"),
        P("groups", None, "shard"),
        P("groups", None),
    )
    out_specs = (P(("groups", "shard"), None, None), P(("groups", "shard"), None))
    return jax.shard_map(
        per_device, mesh=mesh, in_specs=in_specs, out_specs=out_specs, check_vma=False
    )
```

```python
import numpy as np
import jax
import jax.numpy as jnp
from jax import lax
from jax.sharding import PartitionSpec as P

BOX = 64
BAND = 32
SHIFTS = 8
PART_DEV = 1


def signed_band(band_size):
    return jnp.arange(band_size, dtype=jnp.int32) - band_size // 2


def table_pair(outer_loop_index, inner_index, box_edge):
    phase_index = outer_loop_index[:, None] * inner_index[None, :] % box_edge
    angles = phase_index.astype(jnp.float32) * (2.0 * jnp.pi / box_edge)
    return (jnp.cos(angles).astype(jnp.bfloat16), jnp.sin(angles).astype(jnp.bfloat16))


def spectral_product(form, left, right):
    return jnp.einsum(form, left, right, preferred_element_type=jnp.float32)


def forward_spectra(volumes):
    batch_size, box_edge = (volumes.shape[0], volumes.shape[1])
    cosine_forward, sine_forward = table_pair(
        signed_band(BAND), jnp.arange(box_edge, dtype=jnp.int32), box_edge
    )
    density_volume = volumes.astype(jnp.bfloat16)
    leading_real = spectral_product("qw,rwl->rql", cosine_forward, density_volume).astype(
        jnp.bfloat16
    )
    leading_imaginary = (-spectral_product("qw,rwl->rql", sine_forward, density_volume)).astype(
        jnp.bfloat16
    )
    leading_real = leading_real.reshape(batch_size, BAND, box_edge, box_edge)
    leading_imaginary = leading_imaginary.reshape(batch_size, BAND, box_edge, box_edge)
    second_real = (
        spectral_product("jy,nkyz->nkjz", cosine_forward, leading_real)
        + spectral_product("jy,nkyz->nkjz", sine_forward, leading_imaginary)
    ).astype(jnp.bfloat16)
    second_imag = (
        spectral_product("jy,nkyz->nkjz", cosine_forward, leading_imaginary)
        - spectral_product("jy,nkyz->nkjz", sine_forward, leading_real)
    ).astype(jnp.bfloat16)
    third_real = spectral_product("nkjz,lz->nkjl", second_real, cosine_forward) + spectral_product(
        "nkjz,lz->nkjl", second_imag, sine_forward
    )
    third_imag = spectral_product("nkjz,lz->nkjl", second_imag, cosine_forward) - spectral_product(
        "nkjz,lz->nkjl", second_real, sine_forward
    )
    spectrum = jnp.stack([third_real, third_imag], axis=1).astype(jnp.bfloat16)
    return spectrum.reshape(batch_size, 2, BAND * BAND * BAND)


def plane_table():
    k = signed_band(BAND)
    t = signed_band(SHIFTS)
    phase = (
        t[None, None, :, None] * k[:, None, None, None]
        + t[None, None, None, :] * k[None, :, None, None]
    ) % BOX
    angles = phase.astype(jnp.float32) * (2.0 * jnp.pi / BOX)
    shape = (BAND * BAND, SHIFTS * SHIFTS)
    return jnp.concatenate(
        [jnp.cos(angles).reshape(shape), jnp.sin(angles).reshape(shape)], axis=1
    ).astype(jnp.bfloat16)


def score_block(spectra, bin_ids, defocus, refs):
    n_part = spectra.shape[0]
    n_ref = refs.shape[0]
    volume_size = BAND * BAND * BAND
    band_index = signed_band(BAND).astype(jnp.float32)
    radius = (
        band_index[:, None, None] ** 2
        + band_index[None, :, None] ** 2
        + band_index[None, None, :] ** 2
    ).reshape(-1) / (BAND / 2) ** 2
    chosen_defocus = jnp.sum(
        jnp.where(
            bin_ids[:, None] == jnp.arange(defocus.shape[0], dtype=jnp.int32)[None, :],
            defocus[None, :],
            jnp.float32(0.0),
        ),
        axis=1,
    )
    contrast = -jnp.sin(chosen_defocus[:, None] * radius[None, :] + 0.07)
    spec_real = spectra[:, 0].astype(jnp.float32)
    spec_imag = spectra[:, 1].astype(jnp.float32)
    weight_real = (contrast * spec_real).astype(jnp.bfloat16).astype(jnp.float32)
    weight_imag = (-contrast * spec_imag).astype(jnp.bfloat16).astype(jnp.float32)
    energy_particle = jnp.sum(spec_real * spec_real + spec_imag * spec_imag, axis=1)
    ref_real = refs[:, :volume_size].astype(jnp.float32)
    ref_imag = refs[:, volume_size:].astype(jnp.float32)
    magnitude = ref_real * ref_real + ref_imag * ref_imag
    energy_ref = lax.dot_general(
        contrast * contrast, magnitude, (((1,), (1,)), ((), ())), precision=lax.Precision.HIGH
    )
    wr = weight_real[:, None, :]
    wi = weight_imag[:, None, :]
    prod_real = (wr * ref_real[None] - wi * ref_imag[None]).astype(jnp.bfloat16)
    prod_imag = (wr * ref_imag[None] + wi * ref_real[None]).astype(jnp.bfloat16)
    product = jnp.stack([prod_real, prod_imag], axis=2).reshape(
        n_part, n_ref, 2, BAND, BAND * BAND
    )
    planes = spectral_product("ijakl,lm->ijakm", product, plane_table())
    half = SHIFTS * SHIFTS
    plane_real = planes[:, :, 0, :, :half] - planes[:, :, 1, :, half:]
    plane_imag = planes[:, :, 0, :, half:] + planes[:, :, 1, :, :half]
    cos_inv, sin_inv = table_pair(signed_band(SHIFTS), signed_band(BAND), BOX)
    correlation = jnp.einsum(
        "tk,ijkm->ijtm", cos_inv.astype(jnp.float32), plane_real,
        precision=lax.Precision.HIGHEST,
    ) - jnp.einsum(
        "tk,ijkm->ijtm", sin_inv.astype(jnp.float32), plane_imag,
        precision=lax.Precision.HIGHEST,
    )
    peak_value = jnp.max(correlation.reshape(n_part, n_ref, -1), axis=2)
    score_scale = float(BAND) ** 1.5
    return score_scale * peak_value * lax.rsqrt(energy_particle[:, None] * energy_ref + 1e-06)


def pick_rows(library, listed):
    return library[listed]


def ref_groups(shards, particles, refs):
    best = None
    for groups in range(1, shards + 1):
        if shards % groups or refs % groups or particles % (shards // groups):
            continue
        cost = particles * groups // shards + refs // groups
        if best is None or cost < best[0]:
            best = (cost, groups)
    return best[1]


def per_device(particles, slot_target, slot_defocus_level, defocus, ref_library, rotation_list):
    shards = lax.axis_size("shard")
    my_index = lax.axis_index("shard")
    slots_here = particles.shape[0]
    positions = PART_DEV * shards
    every_slot = slot_target.shape[0]
    classes, rotations = rotation_list.shape
    n_refs = classes * rotations
    r_groups = ref_groups(shards, positions, n_refs)
    p_groups = shards // r_groups
    part_block = positions // p_groups
    ref_block = n_refs // r_groups
    my_pblock = my_index // r_groups
    dest_rblock = np.arange(shards) % r_groups
    dest_pblock = np.arange(shards) // r_groups

    chosen = jax.vmap(pick_rows)(ref_library, rotation_list)
    piece = chosen.shape[-1]
    ref_send = chosen.reshape(r_groups, ref_block, piece)[dest_rblock]
    flattened = forward_spectra(particles).reshape(slots_here, shards, piece)
    first_send = jnp.concatenate([flattened.transpose(1, 0, 2), ref_send], axis=1)
    first_got = lax.all_to_all(first_send, "shard", 0, 0, tiled=True)
    pieces = first_got[:, :slots_here].reshape(shards * slots_here, piece)
    refs = first_got[:, slots_here:].transpose(1, 0, 2).reshape(ref_block, shards * piece)

    source = (
        jnp.zeros((positions,), jnp.int32)
        .at[jnp.where(slot_target >= 0, slot_target, positions)]
        .set(jnp.arange(every_slot, dtype=jnp.int32), mode="drop")
    )
    part_send = pieces[source].reshape(p_groups, part_block, piece)[dest_pblock]
    part_got = lax.all_to_all(part_send, "shard", 0, 0, tiled=True)
    spectra = part_got.transpose(1, 0, 2).reshape(part_block, 2, -1)

    my_sources = lax.dynamic_slice_in_dim(source, my_pblock * part_block, part_block, 0)
    block_scores = score_block(spectra, slot_defocus_level[my_sources], defocus, refs)

    targets = slot_target.reshape(shards, slots_here)
    in_block = (targets >= 0) & (targets // part_block == my_pblock)
    rows = block_scores[jnp.clip(targets - my_pblock * part_block, 0, part_block - 1)]
    back_send = jnp.where(in_block[:, :, None], rows, jnp.float32(0.0))
    back_got = lax.all_to_all(back_send, "shard", 0, 0, tiled=True)
    scores = (
        back_got.reshape(p_groups, r_groups, slots_here, ref_block)
        .sum(axis=0)
        .transpose(1, 0, 2)
        .reshape(slots_here, classes, rotations)
    )
    return (scores, jnp.max(scores, axis=2))


def solution(mesh):
    in_specs = (
        P(("groups", "shard"), None, None),
        P("groups"),
        P("groups"),
        P("groups"),
        P("groups", None, "shard"),
        P("groups", None),
    )
    out_specs = (P(("groups", "shard"), None, None), P(("groups", "shard"), None))
    return jax.shard_map(
        per_device, mesh=mesh, in_specs=in_specs, out_specs=out_specs, check_vma=False
    )
```

```python
import numpy as np
import jax
import jax.numpy as jnp
from jax import lax
from jax.sharding import PartitionSpec as P

BOX = 64
BAND = 32
SHIFTS = 8
PART_DEV = 1


def signed_band(band_size):
    return jnp.arange(band_size, dtype=jnp.int32) - band_size // 2


def table_pair(outer_loop_index, inner_index, box_edge):
    phase_index = outer_loop_index[:, None] * inner_index[None, :] % box_edge
    angles = phase_index.astype(jnp.float32) * (2.0 * jnp.pi / box_edge)
    return (jnp.cos(angles).astype(jnp.bfloat16), jnp.sin(angles).astype(jnp.bfloat16))


def spectral_product(form, left, right):
    return jnp.einsum(form, left, right, preferred_element_type=jnp.float32)


def forward_spectra(volumes):
    batch_size, box_edge = (volumes.shape[0], volumes.shape[1])
    cosine_forward, sine_forward = table_pair(
        signed_band(BAND), jnp.arange(box_edge, dtype=jnp.int32), box_edge
    )
    density_volume = volumes.astype(jnp.bfloat16)
    leading_real = spectral_product("qw,rwl->rql", cosine_forward, density_volume).astype(
        jnp.bfloat16
    )
    leading_imaginary = (-spectral_product("qw,rwl->rql", sine_forward, density_volume)).astype(
        jnp.bfloat16
    )
    leading_real = leading_real.reshape(batch_size, BAND, box_edge, box_edge)
    leading_imaginary = leading_imaginary.reshape(batch_size, BAND, box_edge, box_edge)
    second_real = (
        spectral_product("jy,nkyz->nkjz", cosine_forward, leading_real)
        + spectral_product("jy,nkyz->nkjz", sine_forward, leading_imaginary)
    ).astype(jnp.bfloat16)
    second_imag = (
        spectral_product("jy,nkyz->nkjz", cosine_forward, leading_imaginary)
        - spectral_product("jy,nkyz->nkjz", sine_forward, leading_real)
    ).astype(jnp.bfloat16)
    third_real = spectral_product("nkjz,lz->nkjl", second_real, cosine_forward) + spectral_product(
        "nkjz,lz->nkjl", second_imag, sine_forward
    )
    third_imag = spectral_product("nkjz,lz->nkjl", second_imag, cosine_forward) - spectral_product(
        "nkjz,lz->nkjl", second_real, sine_forward
    )
    spectrum = jnp.stack([third_real, third_imag], axis=1).astype(jnp.bfloat16)
    return spectrum.reshape(batch_size, 2, BAND * BAND * BAND)


def plane_table():
    k = signed_band(BAND)
    t = signed_band(SHIFTS)
    phase = (
        t[None, None, :, None] * k[:, None, None, None]
        + t[None, None, None, :] * k[None, :, None, None]
    ) % BOX
    angles = phase.astype(jnp.float32) * (2.0 * jnp.pi / BOX)
    shape = (BAND * BAND, SHIFTS * SHIFTS)
    return jnp.concatenate(
        [jnp.cos(angles).reshape(shape), jnp.sin(angles).reshape(shape)], axis=1
    ).astype(jnp.bfloat16)


def score_block(spectra, bin_ids, defocus, refs):
    n_part = spectra.shape[0]
    n_ref = refs.shape[0]
    volume_size = BAND * BAND * BAND
    band_index = signed_band(BAND).astype(jnp.float32)
    radius = (
        band_index[:, None, None] ** 2
        + band_index[None, :, None] ** 2
        + band_index[None, None, :] ** 2
    ).reshape(-1) / (BAND / 2) ** 2
    chosen_defocus = jnp.sum(
        jnp.where(
            bin_ids[:, None] == jnp.arange(defocus.shape[0], dtype=jnp.int32)[None, :],
            defocus[None, :],
            jnp.float32(0.0),
        ),
        axis=1,
    )
    contrast = -jnp.sin(chosen_defocus[:, None] * radius[None, :] + 0.07)
    spec_real = spectra[:, 0].astype(jnp.float32)
    spec_imag = spectra[:, 1].astype(jnp.float32)
    weight_real = (contrast * spec_real).astype(jnp.bfloat16).astype(jnp.float32)
    weight_imag = (-contrast * spec_imag).astype(jnp.bfloat16).astype(jnp.float32)
    energy_particle = jnp.sum(spec_real * spec_real + spec_imag * spec_imag, axis=1)
    ref_real = refs[:, :volume_size].astype(jnp.float32)
    ref_imag = refs[:, volume_size:].astype(jnp.float32)
    magnitude = ref_real * ref_real + ref_imag * ref_imag
    energy_ref = lax.dot_general(
        contrast * contrast, magnitude, (((1,), (1,)), ((), ())), precision=lax.Precision.HIGH
    )
    wr = weight_real[:, None, :]
    wi = weight_imag[:, None, :]
    prod_real = (wr * ref_real[None] - wi * ref_imag[None]).astype(jnp.bfloat16)
    prod_imag = (wr * ref_imag[None] + wi * ref_real[None]).astype(jnp.bfloat16)
    product = jnp.stack([prod_real, prod_imag], axis=2).reshape(
        n_part, n_ref, 2, BAND, BAND * BAND
    )
    planes = spectral_product("ijakl,lm->ijakm", product, plane_table())
    half = SHIFTS * SHIFTS
    plane_real = planes[:, :, 0, :, :half] - planes[:, :, 1, :, half:]
    plane_imag = planes[:, :, 0, :, half:] + planes[:, :, 1, :, :half]
    cos_inv, sin_inv = table_pair(signed_band(SHIFTS), signed_band(BAND), BOX)
    correlation = jnp.einsum(
        "tk,ijkm->ijtm", cos_inv.astype(jnp.float32), plane_real,
        precision=lax.Precision.HIGHEST,
    ) - jnp.einsum(
        "tk,ijkm->ijtm", sin_inv.astype(jnp.float32), plane_imag,
        precision=lax.Precision.HIGHEST,
    )
    peak_value = jnp.max(correlation.reshape(n_part, n_ref, -1), axis=2)
    score_scale = float(BAND) ** 1.5
    return score_scale * peak_value * lax.rsqrt(energy_particle[:, None] * energy_ref + 1e-06)


def pick_rows(library, listed):
    return library[listed]


def ref_groups(shards, particles, refs):
    best = None
    for groups in range(1, shards + 1):
        if shards % groups or refs % groups or particles % (shards // groups):
            continue
        cost = particles * groups // shards + refs // groups
        if best is None or cost < best[0]:
            best = (cost, groups)
    return best[1]


def per_device(particles, slot_target, slot_defocus_level, defocus, ref_library, rotation_list):
    shards = lax.axis_size("shard")
    my_index = lax.axis_index("shard")
    slots_here = particles.shape[0]
    positions = PART_DEV * shards
    every_slot = slot_target.shape[0]
    classes, rotations = rotation_list.shape
    n_refs = classes * rotations
    r_groups = ref_groups(shards, positions, n_refs)
    p_groups = shards // r_groups
    part_block = positions // p_groups
    ref_block = n_refs // r_groups
    my_pblock = my_index // r_groups
    dest_rblock = np.arange(shards) % r_groups
    dest_pblock = np.arange(shards) // r_groups

    chosen = jax.vmap(pick_rows)(ref_library, rotation_list)
    piece = chosen.shape[-1]
    ref_send = chosen.reshape(r_groups, ref_block, piece)[dest_rblock]
    ref_got = lax.all_to_all(ref_send, "shard", 0, 0, tiled=True)
    flattened = forward_spectra(particles).reshape(slots_here, -1)
    flattened, ref_got = lax.optimization_barrier((flattened, ref_got))
    refs = ref_got.transpose(1, 0, 2).reshape(ref_block, shards * piece)
    pieces = lax.all_to_all(flattened, "shard", split_axis=1, concat_axis=0, tiled=True)

    source = (
        jnp.zeros((positions,), jnp.int32)
        .at[jnp.where(slot_target >= 0, slot_target, positions)]
        .set(jnp.arange(every_slot, dtype=jnp.int32), mode="drop")
    )
    part_send = pieces[source].reshape(p_groups, part_block, piece)[dest_pblock]
    part_got = lax.all_to_all(part_send, "shard", 0, 0, tiled=True)
    spectra = part_got.transpose(1, 0, 2).reshape(part_block, 2, -1)

    my_sources = lax.dynamic_slice_in_dim(source, my_pblock * part_block, part_block, 0)
    block_scores = score_block(spectra, slot_defocus_level[my_sources], defocus, refs)

    targets = slot_target.reshape(shards, slots_here)
    in_block = (targets >= 0) & (targets // part_block == my_pblock)
    rows = block_scores[jnp.clip(targets - my_pblock * part_block, 0, part_block - 1)]
    back_send = jnp.where(in_block[:, :, None], rows, jnp.float32(0.0))
    back_got = lax.all_to_all(back_send, "shard", 0, 0, tiled=True)
    scores = (
        back_got.reshape(p_groups, r_groups, slots_here, ref_block)
        .sum(axis=0)
        .transpose(1, 0, 2)
        .reshape(slots_here, classes, rotations)
    )
    return (scores, jnp.max(scores, axis=2))


def solution(mesh):
    in_specs = (
        P(("groups", "shard"), None, None),
        P("groups"),
        P("groups"),
        P("groups"),
        P("groups", None, "shard"),
        P("groups", None),
    )
    out_specs = (P(("groups", "shard"), None, None), P(("groups", "shard"), None))
    return jax.shard_map(
        per_device, mesh=mesh, in_specs=in_specs, out_specs=out_specs, check_vma=False
    )
```

```python
import jax
import jax.numpy as jnp
from jax import lax
from jax.experimental import pallas as pl
from jax.experimental.pallas import tpu as pltpu
from jax.sharding import PartitionSpec as P

BOX = 64
BAND = 32
SHIFTS = 8
PART_DEV = 1


def signed_band(band_size):
    return jnp.arange(band_size, dtype=jnp.int32) - band_size // 2


def table_pair(outer_loop_index, inner_index, box_edge):
    phase_index = outer_loop_index[:, None] * inner_index[None, :] % box_edge
    angles = phase_index.astype(jnp.float32) * (2.0 * jnp.pi / box_edge)
    return (jnp.cos(angles).astype(jnp.bfloat16), jnp.sin(angles).astype(jnp.bfloat16))


def spectral_product(form, left, right):
    return jnp.einsum(form, left, right, preferred_element_type=jnp.float32)


def forward_spectra(volumes):
    batch_size, box_edge = (volumes.shape[0], volumes.shape[1])
    cosine_forward, sine_forward = table_pair(
        signed_band(BAND), jnp.arange(box_edge, dtype=jnp.int32), box_edge
    )
    density_volume = volumes.astype(jnp.bfloat16)
    leading_real = spectral_product("qw,rwl->rql", cosine_forward, density_volume).astype(
        jnp.bfloat16
    )
    leading_imaginary = (-spectral_product("qw,rwl->rql", sine_forward, density_volume)).astype(
        jnp.bfloat16
    )
    leading_real = leading_real.reshape(batch_size, BAND, box_edge, box_edge)
    leading_imaginary = leading_imaginary.reshape(batch_size, BAND, box_edge, box_edge)
    second_real = (
        spectral_product("jy,nkyz->nkjz", cosine_forward, leading_real)
        + spectral_product("jy,nkyz->nkjz", sine_forward, leading_imaginary)
    ).astype(jnp.bfloat16)
    second_imag = (
        spectral_product("jy,nkyz->nkjz", cosine_forward, leading_imaginary)
        - spectral_product("jy,nkyz->nkjz", sine_forward, leading_real)
    ).astype(jnp.bfloat16)
    third_real = spectral_product("nkjz,lz->nkjl", second_real, cosine_forward) + spectral_product(
        "nkjz,lz->nkjl", second_imag, sine_forward
    )
    third_imag = spectral_product("nkjz,lz->nkjl", second_imag, cosine_forward) - spectral_product(
        "nkjz,lz->nkjl", second_real, sine_forward
    )
    spectrum = jnp.stack([third_real, third_imag], axis=1).astype(jnp.bfloat16)
    return spectrum.reshape(batch_size, 2, BAND * BAND * BAND)


def plane_table():
    k = signed_band(BAND)
    t = signed_band(SHIFTS)
    phase = (
        t[None, None, :, None] * k[:, None, None, None]
        + t[None, None, None, :] * k[None, :, None, None]
    ) % BOX
    angles = phase.astype(jnp.float32) * (2.0 * jnp.pi / BOX)
    shape = (BAND * BAND, SHIFTS * SHIFTS)
    cosine = jnp.cos(angles).reshape(shape)
    sine = jnp.sin(angles).reshape(shape)
    upper = jnp.concatenate([cosine, sine], axis=1)
    lower = jnp.concatenate([-sine, cosine], axis=1)
    return jnp.concatenate([upper, lower], axis=0).astype(jnp.bfloat16)


def correlation_kernel(w_ref, c_ref, t_ref, ec_ref, es_ref, o_ref, p_s):
    n_ref = c_ref.shape[0]
    plane = BAND * BAND
    w_real = w_ref[0, 0].astype(jnp.float32)
    w_imag = w_ref[0, 1].astype(jnp.float32)
    for j in range(n_ref):
        c_real = c_ref[j, 0].astype(jnp.float32)
        c_imag = c_ref[j, 1].astype(jnp.float32)
        rows = slice(j * BAND, (j + 1) * BAND)
        p_s[rows, :plane] = (w_real * c_real - w_imag * c_imag).astype(jnp.bfloat16)
        p_s[rows, plane:] = (w_real * c_imag + w_imag * c_real).astype(jnp.bfloat16)
    planes = jnp.dot(p_s[...], t_ref[...], preferred_element_type=jnp.float32)
    first = jnp.dot(ec_ref[...], planes, preferred_element_type=jnp.float32,
                    precision=lax.Precision.HIGHEST)
    second = jnp.dot(es_ref[...], planes, preferred_element_type=jnp.float32,
                     precision=lax.Precision.HIGHEST)
    half = SHIFTS * SHIFTS
    correlation = first - pltpu.roll(second, half, 1)
    lane = lax.broadcasted_iota(jnp.int32, correlation.shape, 1)
    correlation = jnp.where(lane < half, correlation, -jnp.inf)
    per_row = jnp.max(correlation.reshape(n_ref, SHIFTS, 2 * half), axis=1)
    peak = jnp.max(per_row, axis=1, keepdims=True)
    o_ref[0] = jnp.broadcast_to(peak, (n_ref, 2 * half))


def peak_correlations(weighted, refs):
    n_part = weighted.shape[0]
    n_ref = refs.shape[0]
    plane = BAND * BAND
    cos_inv, sin_inv = table_pair(signed_band(SHIFTS), signed_band(BAND), BOX)
    eye = jnp.eye(n_ref, dtype=jnp.float32)
    e_cos = jnp.kron(eye, cos_inv.astype(jnp.float32))
    e_sin = jnp.kron(eye, sin_inv.astype(jnp.float32))
    table = plane_table()
    width = 2 * SHIFTS * SHIFTS
    out = pl.pallas_call(
        correlation_kernel,
        grid=(n_part,),
        in_specs=[
            pl.BlockSpec((1, 2, BAND, plane), lambda i: (i, 0, 0, 0)),
            pl.BlockSpec((n_ref, 2, BAND, plane), lambda i: (0, 0, 0, 0)),
            pl.BlockSpec((2 * plane, width), lambda i: (0, 0)),
            pl.BlockSpec((n_ref * SHIFTS, n_ref * BAND), lambda i: (0, 0)),
            pl.BlockSpec((n_ref * SHIFTS, n_ref * BAND), lambda i: (0, 0)),
        ],
        out_specs=pl.BlockSpec((1, n_ref, width), lambda i: (i, 0, 0)),
        out_shape=jax.ShapeDtypeStruct((n_part, n_ref, width), jnp.float32),
        scratch_shapes=[pltpu.VMEM((n_ref * BAND, 2 * plane), jnp.bfloat16)],
        cost_estimate=pl.CostEstimate(
            flops=n_part * n_ref * (2 * BAND * 2 * plane * width + 8 * BAND * plane),
            transcendentals=0,
            bytes_accessed=(n_part + n_ref) * 4 * BAND * plane,
        ),
    )(weighted, refs, table, e_cos, e_sin)
    return out[:, :, 0]


def score_block(spectra, bin_ids, defocus, refs):
    n_part = spectra.shape[0]
    n_ref = refs.shape[0]
    volume_size = BAND * BAND * BAND
    band_index = signed_band(BAND).astype(jnp.float32)
    radius = (
        band_index[:, None, None] ** 2
        + band_index[None, :, None] ** 2
        + band_index[None, None, :] ** 2
    ).reshape(-1) / (BAND / 2) ** 2
    chosen_defocus = jnp.sum(
        jnp.where(
            bin_ids[:, None] == jnp.arange(defocus.shape[0], dtype=jnp.int32)[None, :],
            defocus[None, :],
            jnp.float32(0.0),
        ),
        axis=1,
    )
    contrast = -jnp.sin(chosen_defocus[:, None] * radius[None, :] + 0.07)
    ref_real = refs[:, :volume_size].astype(jnp.float32)
    ref_imag = refs[:, volume_size:].astype(jnp.float32)
    magnitude = ref_real * ref_real + ref_imag * ref_imag
    energy_ref = jnp.sum((contrast * contrast)[:, None, :] * magnitude[None, :, :], axis=2)
    spec_real = spectra[:, 0].astype(jnp.float32)
    spec_imag = spectra[:, 1].astype(jnp.float32)
    weight_real = (contrast * spec_real).astype(jnp.bfloat16)
    weight_imag = (-contrast * spec_imag).astype(jnp.bfloat16)
    energy_particle = jnp.sum(spec_real * spec_real + spec_imag * spec_imag, axis=1)
    shape = (BAND, BAND * BAND)
    weighted = jnp.stack([weight_real, weight_imag], axis=1).reshape(n_part, 2, *shape)
    peak_value = peak_correlations(weighted, refs.reshape(n_ref, 2, *shape))
    score_scale = float(BAND) ** 1.5
    return score_scale * peak_value * lax.rsqrt(energy_particle[:, None] * energy_ref + 1e-06)


def ref_groups(shards, particles, refs):
    best = None
    for groups in range(1, shards + 1):
        if shards % groups or refs % groups or particles % (shards // groups):
            continue
        cost = particles * groups // shards + refs // groups
        if best is None or cost < best[0]:
            best = (cost, groups)
    return best[1]


def per_device(particles, slot_target, slot_defocus_level, defocus, ref_library, rotation_list):
    shards = lax.axis_size("shard")
    my_index = lax.axis_index("shard")
    slots_here = particles.shape[0]
    positions = PART_DEV * shards
    every_slot = slot_target.shape[0]
    classes, rotations = rotation_list.shape
    n_refs = classes * rotations
    r_groups = ref_groups(shards, positions, n_refs)
    p_groups = shards // r_groups
    part_block = positions // p_groups
    ref_block = n_refs // r_groups
    my_pblock = my_index // r_groups

    library = ref_library.shape[1]
    listed = (rotation_list[:, :, None] == jnp.arange(library, dtype=jnp.int32)).astype(jnp.bfloat16)
    chosen = jnp.einsum(
        "crl,clk->crk", listed, ref_library, preferred_element_type=jnp.float32
    ).astype(jnp.bfloat16)
    piece = chosen.shape[-1]
    ref_send = jnp.broadcast_to(
        chosen.reshape(1, r_groups, ref_block, piece), (p_groups, r_groups, ref_block, piece)
    ).reshape(shards, ref_block, piece)
    ref_got = lax.all_to_all(ref_send, "shard", 0, 0, tiled=True)
    flattened = forward_spectra(particles).reshape(slots_here, -1)
    flattened, ref_got = lax.optimization_barrier((flattened, ref_got))
    refs = ref_got.transpose(1, 0, 2).reshape(ref_block, shards * piece)
    pieces = lax.all_to_all(flattened, "shard", split_axis=1, concat_axis=0, tiled=True)

    source = (
        jnp.zeros((positions,), jnp.int32)
        .at[jnp.where(slot_target >= 0, slot_target, positions)]
        .set(jnp.arange(every_slot, dtype=jnp.int32), mode="drop")
    )
    part_send = jnp.broadcast_to(
        pieces[source].reshape(p_groups, 1, part_block, piece),
        (p_groups, r_groups, part_block, piece),
    ).reshape(shards, part_block, piece)
    part_got = lax.all_to_all(part_send, "shard", 0, 0, tiled=True)
    spectra = part_got.transpose(1, 0, 2).reshape(part_block, 2, -1)

    my_sources = lax.dynamic_slice_in_dim(source, my_pblock * part_block, part_block, 0)
    block_scores = score_block(spectra, slot_defocus_level[my_sources], defocus, refs)

    targets = slot_target.reshape(shards, slots_here)
    in_block = (targets >= 0) & (targets // part_block == my_pblock)
    rows = block_scores[jnp.clip(targets - my_pblock * part_block, 0, part_block - 1)]
    back_send = jnp.where(in_block[:, :, None], rows, jnp.float32(0.0))
    back_got = lax.all_to_all(back_send, "shard", 0, 0, tiled=True)
    scores = (
        back_got.reshape(p_groups, r_groups, slots_here, ref_block)
        .sum(axis=0)
        .transpose(1, 0, 2)
        .reshape(slots_here, classes, rotations)
    )
    return (scores, jnp.max(scores, axis=2))


def solution(mesh):
    in_specs = (
        P(("groups", "shard"), None, None),
        P("groups"),
        P("groups"),
        P("groups"),
        P("groups", None, "shard"),
        P("groups", None),
    )
    out_specs = (P(("groups", "shard"), None, None), P(("groups", "shard"), None))
    return jax.shard_map(
        per_device, mesh=mesh, in_specs=in_specs, out_specs=out_specs, check_vma=False
    )
```

```python
import numpy as np
import jax
import jax.numpy as jnp
from jax import lax
from jax.experimental import pallas as pl
from jax.experimental.pallas import tpu as pltpu
from jax.sharding import PartitionSpec as P

BOX = 64
BAND = 32
SHIFTS = 8
PART_DEV = 1


def signed_band(band_size):
    return jnp.arange(band_size, dtype=jnp.int32) - band_size // 2


def table_pair(outer_loop_index, inner_index, box_edge):
    phase_index = outer_loop_index[:, None] * inner_index[None, :] % box_edge
    angles = phase_index.astype(jnp.float32) * (2.0 * jnp.pi / box_edge)
    return (jnp.cos(angles).astype(jnp.bfloat16), jnp.sin(angles).astype(jnp.bfloat16))


def spectral_product(form, left, right):
    return jnp.einsum(form, left, right, preferred_element_type=jnp.float32)


def forward_spectra(volumes):
    batch_size, box_edge = (volumes.shape[0], volumes.shape[1])
    cosine_forward, sine_forward = table_pair(
        signed_band(BAND), jnp.arange(box_edge, dtype=jnp.int32), box_edge
    )
    density_volume = volumes.astype(jnp.bfloat16)
    leading_real = spectral_product("qw,rwl->rql", cosine_forward, density_volume).astype(
        jnp.bfloat16
    )
    leading_imaginary = (-spectral_product("qw,rwl->rql", sine_forward, density_volume)).astype(
        jnp.bfloat16
    )
    leading_real = leading_real.reshape(batch_size, BAND, box_edge, box_edge)
    leading_imaginary = leading_imaginary.reshape(batch_size, BAND, box_edge, box_edge)
    second_real = (
        spectral_product("jy,nkyz->nkjz", cosine_forward, leading_real)
        + spectral_product("jy,nkyz->nkjz", sine_forward, leading_imaginary)
    ).astype(jnp.bfloat16)
    second_imag = (
        spectral_product("jy,nkyz->nkjz", cosine_forward, leading_imaginary)
        - spectral_product("jy,nkyz->nkjz", sine_forward, leading_real)
    ).astype(jnp.bfloat16)
    third_real = spectral_product("nkjz,lz->nkjl", second_real, cosine_forward) + spectral_product(
        "nkjz,lz->nkjl", second_imag, sine_forward
    )
    third_imag = spectral_product("nkjz,lz->nkjl", second_imag, cosine_forward) - spectral_product(
        "nkjz,lz->nkjl", second_real, sine_forward
    )
    spectrum = jnp.stack([third_real, third_imag], axis=1).astype(jnp.bfloat16)
    return spectrum.reshape(batch_size, 2, BAND * BAND * BAND)


def plane_table():
    k = np.arange(BAND) - BAND // 2
    t = np.arange(SHIFTS) - SHIFTS // 2
    phase = (
        t[None, None, :, None] * k[:, None, None, None]
        + t[None, None, None, :] * k[None, :, None, None]
    ) % BOX
    angles = phase.astype(np.float32) * np.float32(2.0 * np.pi / BOX)
    shape = (BAND * BAND, SHIFTS * SHIFTS)
    cosine = np.cos(angles).reshape(shape)
    sine = np.sin(angles).reshape(shape)
    upper = np.concatenate([cosine, sine], axis=1)
    lower = np.concatenate([-sine, cosine], axis=1)
    return jnp.asarray(np.concatenate([upper, lower], axis=0), dtype=jnp.bfloat16)


def shift_tables(n_ref):
    k = np.arange(BAND) - BAND // 2
    t = np.arange(SHIFTS) - SHIFTS // 2
    angles = ((t[:, None] * k[None, :]) % BOX).astype(np.float32) * np.float32(2.0 * np.pi / BOX)
    eye = np.eye(n_ref, dtype=np.float32)
    def rounded(x):
        return jnp.asarray(x, dtype=jnp.bfloat16).astype(jnp.float32)
    return rounded(np.kron(eye, np.cos(angles))), rounded(np.kron(eye, np.sin(angles)))


def correlation_kernel(s_ref, g_ref, c_ref, t_ref, ec_ref, es_ref, o_ref, e_ref, p_s):
    n_ref = c_ref.shape[0]
    plane = BAND * BAND
    contrast = g_ref[0]
    s_real = s_ref[0, 0].astype(jnp.float32)
    s_imag = s_ref[0, 1].astype(jnp.float32)
    w_real = (contrast * s_real).astype(jnp.bfloat16).astype(jnp.float32)
    w_imag = (-(contrast * s_imag)).astype(jnp.bfloat16).astype(jnp.float32)
    for j in range(n_ref):
        c_real = c_ref[j, 0]
        c_imag = c_ref[j, 1]
        rows = slice(j * BAND, (j + 1) * BAND)
        p_s[rows, :plane] = (w_real * c_real - w_imag * c_imag).astype(jnp.bfloat16)
        p_s[rows, plane:] = (w_real * c_imag + w_imag * c_real).astype(jnp.bfloat16)
    planes = jnp.dot(p_s[...], t_ref[...], preferred_element_type=jnp.float32)
    first = jnp.dot(ec_ref[...], planes, preferred_element_type=jnp.float32,
                    precision=lax.Precision.HIGHEST)
    second = jnp.dot(es_ref[...], planes, preferred_element_type=jnp.float32,
                     precision=lax.Precision.HIGHEST)
    half = SHIFTS * SHIFTS
    correlation = first - pltpu.roll(second, half, 1)
    lane = lax.broadcasted_iota(jnp.int32, correlation.shape, 1)
    correlation = jnp.where(lane < half, correlation, -jnp.inf)
    per_row = jnp.max(correlation.reshape(n_ref, SHIFTS, 2 * half), axis=1)
    peak = jnp.max(per_row, axis=1, keepdims=True)
    o_ref[0] = jnp.broadcast_to(peak, (n_ref, 2 * half))
    power = jnp.sum(s_real * s_real + s_imag * s_imag, axis=0, keepdims=True)
    e_ref[0] = jnp.broadcast_to(jnp.sum(power, axis=1, keepdims=True), (8, 2 * half))


def peak_correlations(spectra, contrast, refs):
    n_part = spectra.shape[0]
    n_ref = refs.shape[0]
    plane = BAND * BAND
    e_cos, e_sin = shift_tables(n_ref)
    width = 2 * SHIFTS * SHIFTS
    peak, energy = pl.pallas_call(
        correlation_kernel,
        grid=(n_part,),
        in_specs=[
            pl.BlockSpec((1, 2, BAND, plane), lambda i: (i, 0, 0, 0)),
            pl.BlockSpec((1, BAND, plane), lambda i: (i, 0, 0)),
            pl.BlockSpec((n_ref, 2, BAND, plane), lambda i: (0, 0, 0, 0)),
            pl.BlockSpec((2 * plane, width), lambda i: (0, 0)),
            pl.BlockSpec((n_ref * SHIFTS, n_ref * BAND), lambda i: (0, 0)),
            pl.BlockSpec((n_ref * SHIFTS, n_ref * BAND), lambda i: (0, 0)),
        ],
        out_specs=[
            pl.BlockSpec((1, n_ref, width), lambda i: (i, 0, 0)),
            pl.BlockSpec((1, 8, width), lambda i: (i, 0, 0)),
        ],
        out_shape=[
            jax.ShapeDtypeStruct((n_part, n_ref, width), jnp.float32),
            jax.ShapeDtypeStruct((n_part, 8, width), jnp.float32),
        ],
        scratch_shapes=[pltpu.VMEM((n_ref * BAND, 2 * plane), jnp.bfloat16)],
        cost_estimate=pl.CostEstimate(
            flops=n_part * n_ref * (2 * BAND * 2 * plane * width + 8 * BAND * plane),
            transcendentals=0,
            bytes_accessed=n_part * 8 * BAND * plane + n_ref * 8 * BAND * plane,
        ),
    )(spectra, contrast, refs, plane_table(), e_cos, e_sin)
    return peak[:, :, 0], energy[:, 0, 0]


def particle_contrast(bin_ids, defocus):
    band_index = signed_band(BAND).astype(jnp.float32)
    radius = (
        band_index[:, None, None] ** 2
        + band_index[None, :, None] ** 2
        + band_index[None, None, :] ** 2
    ).reshape(-1) / (BAND / 2) ** 2
    chosen_defocus = jnp.sum(
        jnp.where(
            bin_ids[:, None] == jnp.arange(defocus.shape[0], dtype=jnp.int32)[None, :],
            defocus[None, :],
            jnp.float32(0.0),
        ),
        axis=1,
    )
    return -jnp.sin(chosen_defocus[:, None] * radius[None, :] + 0.07)


def reference_energy(contrast, refs):
    volume_size = BAND * BAND * BAND
    ref_real = refs[:, :volume_size].astype(jnp.float32)
    ref_imag = refs[:, volume_size:].astype(jnp.float32)
    magnitude = ref_real * ref_real + ref_imag * ref_imag
    return jnp.sum((contrast * contrast)[:, None, :] * magnitude[None, :, :], axis=2)


def score_block(spectra, contrast, energy_ref, refs):
    n_part = spectra.shape[0]
    n_ref = refs.shape[0]
    shape = (BAND, BAND * BAND)
    peak_value, energy_particle = peak_correlations(
        spectra.reshape(n_part, 2, *shape),
        contrast.reshape(n_part, *shape),
        refs.reshape(n_ref, 2, *shape).astype(jnp.float32),
    )
    score_scale = float(BAND) ** 1.5
    return score_scale * peak_value * lax.rsqrt(energy_particle[:, None] * energy_ref + 1e-06)


def ref_groups(shards, particles, refs):
    best = None
    for groups in range(1, shards + 1):
        if shards % groups or refs % groups or particles % (shards // groups):
            continue
        cost = particles * groups // shards + refs // groups
        if best is None or cost < best[0]:
            best = (cost, groups)
    return best[1]


def per_device(particles, slot_target, slot_defocus_level, defocus, ref_library, rotation_list):
    shards = lax.axis_size("shard")
    my_index = lax.axis_index("shard")
    slots_here = particles.shape[0]
    positions = PART_DEV * shards
    every_slot = slot_target.shape[0]
    classes, rotations = rotation_list.shape
    n_refs = classes * rotations
    r_groups = ref_groups(shards, positions, n_refs)
    p_groups = shards // r_groups
    part_block = positions // p_groups
    ref_block = n_refs // r_groups
    my_pblock = my_index // r_groups

    library = ref_library.shape[1]
    listed = (rotation_list[:, :, None] == jnp.arange(library, dtype=jnp.int32)).astype(jnp.bfloat16)
    chosen = jnp.einsum(
        "crl,clk->crk", listed, ref_library, preferred_element_type=jnp.float32
    ).astype(jnp.bfloat16)
    piece = chosen.shape[-1]
    ref_send = jnp.broadcast_to(
        chosen.reshape(1, r_groups, ref_block, piece), (p_groups, r_groups, ref_block, piece)
    ).reshape(shards, ref_block, piece)
    ref_got = lax.all_to_all(ref_send, "shard", 0, 0, tiled=True)
    flattened = forward_spectra(particles).reshape(slots_here, -1)
    flattened, ref_got = lax.optimization_barrier((flattened, ref_got))
    refs = ref_got.transpose(1, 0, 2).reshape(ref_block, shards * piece)
    pieces = lax.all_to_all(flattened, "shard", split_axis=1, concat_axis=0, tiled=True)

    source = (
        jnp.zeros((positions,), jnp.int32)
        .at[jnp.where(slot_target >= 0, slot_target, positions)]
        .set(jnp.arange(every_slot, dtype=jnp.int32), mode="drop")
    )
    my_sources = lax.dynamic_slice_in_dim(source, my_pblock * part_block, part_block, 0)
    bin_ids, pieces = lax.optimization_barrier((slot_defocus_level[my_sources], pieces))
    contrast = particle_contrast(bin_ids, defocus)
    energy_ref = reference_energy(contrast, refs)
    part_send = jnp.broadcast_to(
        pieces[source].reshape(p_groups, 1, part_block, piece),
        (p_groups, r_groups, part_block, piece),
    ).reshape(shards, part_block, piece)
    part_got = lax.all_to_all(part_send, "shard", 0, 0, tiled=True)
    spectra = part_got.transpose(1, 0, 2).reshape(part_block, -1)
    block_scores = score_block(spectra, contrast, energy_ref, refs)

    targets = slot_target.reshape(shards, slots_here)
    in_block = (targets >= 0) & (targets // part_block == my_pblock)
    rows = block_scores[jnp.clip(targets - my_pblock * part_block, 0, part_block - 1)]
    back_send = jnp.where(in_block[:, :, None], rows, jnp.float32(0.0))
    back_got = lax.all_to_all(back_send, "shard", 0, 0, tiled=True)
    scores = (
        back_got.reshape(p_groups, r_groups, slots_here, ref_block)
        .sum(axis=0)
        .transpose(1, 0, 2)
        .reshape(slots_here, classes, rotations)
    )
    return (scores, jnp.max(scores, axis=2))


def solution(mesh):
    in_specs = (
        P(("groups", "shard"), None, None),
        P("groups"),
        P("groups"),
        P("groups"),
        P("groups", None, "shard"),
        P("groups", None),
    )
    out_specs = (P(("groups", "shard"), None, None), P(("groups", "shard"), None))
    return jax.shard_map(
        per_device, mesh=mesh, in_specs=in_specs, out_specs=out_specs, check_vma=False
    )
```

```python
import numpy as np
import jax
import jax.numpy as jnp
from jax import lax
from jax.experimental import pallas as pl
from jax.experimental.pallas import tpu as pltpu
from jax.sharding import PartitionSpec as P

BOX = 64
BAND = 32
SHIFTS = 8
PART_DEV = 1


def signed_band(band_size):
    return jnp.arange(band_size, dtype=jnp.int32) - band_size // 2


def table_pair(outer_loop_index, inner_index, box_edge):
    phase_index = outer_loop_index[:, None] * inner_index[None, :] % box_edge
    angles = phase_index.astype(jnp.float32) * (2.0 * jnp.pi / box_edge)
    return (jnp.cos(angles).astype(jnp.bfloat16), jnp.sin(angles).astype(jnp.bfloat16))


def spectral_product(form, left, right):
    return jnp.einsum(form, left, right, preferred_element_type=jnp.float32)


def forward_spectra(volumes):
    batch_size, box_edge = (volumes.shape[0], volumes.shape[1])
    cosine_forward, sine_forward = table_pair(
        signed_band(BAND), jnp.arange(box_edge, dtype=jnp.int32), box_edge
    )
    density_volume = volumes.astype(jnp.bfloat16)
    leading_real = spectral_product("qw,rwl->rql", cosine_forward, density_volume).astype(
        jnp.bfloat16
    )
    leading_imaginary = (-spectral_product("qw,rwl->rql", sine_forward, density_volume)).astype(
        jnp.bfloat16
    )
    leading_real = leading_real.reshape(batch_size, BAND, box_edge, box_edge)
    leading_imaginary = leading_imaginary.reshape(batch_size, BAND, box_edge, box_edge)
    second_real = (
        spectral_product("jy,nkyz->nkjz", cosine_forward, leading_real)
        + spectral_product("jy,nkyz->nkjz", sine_forward, leading_imaginary)
    ).astype(jnp.bfloat16)
    second_imag = (
        spectral_product("jy,nkyz->nkjz", cosine_forward, leading_imaginary)
        - spectral_product("jy,nkyz->nkjz", sine_forward, leading_real)
    ).astype(jnp.bfloat16)
    third_real = spectral_product("nkjz,lz->nkjl", second_real, cosine_forward) + spectral_product(
        "nkjz,lz->nkjl", second_imag, sine_forward
    )
    third_imag = spectral_product("nkjz,lz->nkjl", second_imag, cosine_forward) - spectral_product(
        "nkjz,lz->nkjl", second_real, sine_forward
    )
    spectrum = jnp.stack([third_real, third_imag], axis=1).astype(jnp.bfloat16)
    return spectrum.reshape(batch_size, 2, BAND * BAND * BAND)


def plane_table():
    k = np.arange(BAND) - BAND // 2
    t = np.arange(SHIFTS) - SHIFTS // 2
    phase = (
        t[None, None, :, None] * k[:, None, None, None]
        + t[None, None, None, :] * k[None, :, None, None]
    ) % BOX
    angles = phase.astype(np.float32) * np.float32(2.0 * np.pi / BOX)
    shape = (BAND * BAND, SHIFTS * SHIFTS)
    cosine = np.cos(angles).reshape(shape)
    sine = np.sin(angles).reshape(shape)
    upper = np.concatenate([cosine, sine], axis=1)
    lower = np.concatenate([-sine, cosine], axis=1)
    return jnp.asarray(np.concatenate([upper, lower], axis=0), dtype=jnp.bfloat16)


def shift_tables(n_ref):
    k = np.arange(BAND) - BAND // 2
    t = np.arange(SHIFTS) - SHIFTS // 2
    angles = ((t[:, None] * k[None, :]) % BOX).astype(np.float32) * np.float32(2.0 * np.pi / BOX)
    eye = np.eye(n_ref, dtype=np.float32)
    def rounded(x):
        return jnp.asarray(x, dtype=jnp.bfloat16).astype(jnp.float32)
    return rounded(np.kron(eye, np.cos(angles))), rounded(np.kron(eye, np.sin(angles)))


def correlation_kernel(s_ref, g_ref, c_ref, t_ref, ec_ref, es_ref, o_ref, e_ref, p_s):
    n_ref = c_ref.shape[0]
    plane = BAND * BAND
    contrast = g_ref[0]
    s_real = s_ref[0, 0].astype(jnp.float32)
    s_imag = s_ref[0, 1].astype(jnp.float32)
    w_real = (contrast * s_real).astype(jnp.bfloat16).astype(jnp.float32)
    w_imag = (-(contrast * s_imag)).astype(jnp.bfloat16).astype(jnp.float32)
    for j in range(n_ref):
        c_real = c_ref[j, 0]
        c_imag = c_ref[j, 1]
        rows = slice(j * BAND, (j + 1) * BAND)
        p_s[rows, :plane] = (w_real * c_real - w_imag * c_imag).astype(jnp.bfloat16)
        p_s[rows, plane:] = (w_real * c_imag + w_imag * c_real).astype(jnp.bfloat16)
    planes = jnp.dot(p_s[...], t_ref[...], preferred_element_type=jnp.float32)
    first = jnp.dot(ec_ref[...], planes, preferred_element_type=jnp.float32,
                    precision=lax.Precision.HIGHEST)
    second = jnp.dot(es_ref[...], planes, preferred_element_type=jnp.float32,
                     precision=lax.Precision.HIGHEST)
    half = SHIFTS * SHIFTS
    correlation = first - pltpu.roll(second, half, 1)
    lane = lax.broadcasted_iota(jnp.int32, correlation.shape, 1)
    correlation = jnp.where(lane < half, correlation, -jnp.inf)
    per_row = jnp.max(correlation.reshape(n_ref, SHIFTS, 2 * half), axis=1)
    peak = jnp.max(per_row, axis=1, keepdims=True)
    o_ref[0] = jnp.broadcast_to(peak, (n_ref, 2 * half))
    power = jnp.sum(s_real * s_real + s_imag * s_imag, axis=0, keepdims=True)
    e_ref[0] = jnp.broadcast_to(jnp.sum(power, axis=1, keepdims=True), (8, 2 * half))


def peak_correlations(spectra, contrast, refs):
    n_part = spectra.shape[0]
    n_ref = refs.shape[0]
    plane = BAND * BAND
    e_cos, e_sin = shift_tables(n_ref)
    width = 2 * SHIFTS * SHIFTS
    peak, energy = pl.pallas_call(
        correlation_kernel,
        grid=(n_part,),
        in_specs=[
            pl.BlockSpec((1, 2, BAND, plane), lambda i: (i, 0, 0, 0)),
            pl.BlockSpec((1, BAND, plane), lambda i: (i, 0, 0)),
            pl.BlockSpec((n_ref, 2, BAND, plane), lambda i: (0, 0, 0, 0)),
            pl.BlockSpec((2 * plane, width), lambda i: (0, 0)),
            pl.BlockSpec((n_ref * SHIFTS, n_ref * BAND), lambda i: (0, 0)),
            pl.BlockSpec((n_ref * SHIFTS, n_ref * BAND), lambda i: (0, 0)),
        ],
        out_specs=[
            pl.BlockSpec((1, n_ref, width), lambda i: (i, 0, 0)),
            pl.BlockSpec((1, 8, width), lambda i: (i, 0, 0)),
        ],
        out_shape=[
            jax.ShapeDtypeStruct((n_part, n_ref, width), jnp.float32),
            jax.ShapeDtypeStruct((n_part, 8, width), jnp.float32),
        ],
        scratch_shapes=[pltpu.VMEM((n_ref * BAND, 2 * plane), jnp.bfloat16)],
        cost_estimate=pl.CostEstimate(
            flops=n_part * n_ref * (2 * BAND * 2 * plane * width + 8 * BAND * plane),
            transcendentals=0,
            bytes_accessed=n_part * 8 * BAND * plane + n_ref * 8 * BAND * plane,
        ),
    )(spectra, contrast, refs, plane_table(), e_cos, e_sin)
    return peak[:, :, 0], energy[:, 0, 0]


def particle_contrast(bin_ids, defocus):
    band_index = signed_band(BAND).astype(jnp.float32)
    radius = (
        band_index[:, None, None] ** 2
        + band_index[None, :, None] ** 2
        + band_index[None, None, :] ** 2
    ).reshape(-1) / (BAND / 2) ** 2
    chosen_defocus = jnp.sum(
        jnp.where(
            bin_ids[:, None] == jnp.arange(defocus.shape[0], dtype=jnp.int32)[None, :],
            defocus[None, :],
            jnp.float32(0.0),
        ),
        axis=1,
    )
    return -jnp.sin(chosen_defocus[:, None] * radius[None, :] + 0.07)


def reference_energy(contrast, refs):
    volume_size = BAND * BAND * BAND
    ref_real = refs[:, :volume_size].astype(jnp.float32)
    ref_imag = refs[:, volume_size:].astype(jnp.float32)
    magnitude = ref_real * ref_real + ref_imag * ref_imag
    return jnp.sum((contrast * contrast)[:, None, :] * magnitude[None, :, :], axis=2)


def score_block(spectra, contrast, energy_ref, refs):
    n_part = spectra.shape[0]
    n_ref = refs.shape[0]
    shape = (BAND, BAND * BAND)
    peak_value, energy_particle = peak_correlations(
        spectra.reshape(n_part, 2, *shape),
        contrast.reshape(n_part, *shape),
        refs.reshape(n_ref, 2, *shape).astype(jnp.float32),
    )
    score_scale = float(BAND) ** 1.5
    return score_scale * peak_value * lax.rsqrt(energy_particle[:, None] * energy_ref + 1e-06)


def ref_groups(shards, particles, refs):
    best = None
    for groups in range(1, shards + 1):
        if shards % groups or refs % groups or particles % (shards // groups):
            continue
        cost = particles * groups // shards + refs // groups
        if best is None or cost < best[0]:
            best = (cost, groups)
    return best[1]


def per_device(particles, slot_target, slot_defocus_level, defocus, ref_library, rotation_list):
    shards = lax.axis_size("shard")
    my_index = lax.axis_index("shard")
    slots_here = particles.shape[0]
    positions = PART_DEV * shards
    every_slot = slot_target.shape[0]
    classes, rotations = rotation_list.shape
    n_refs = classes * rotations
    r_groups = ref_groups(shards, positions, n_refs)
    p_groups = shards // r_groups
    part_block = positions // p_groups
    ref_block = n_refs // r_groups
    my_pblock = my_index // r_groups

    library = ref_library.shape[1]
    listed = (rotation_list[:, :, None] == jnp.arange(library, dtype=jnp.int32)).astype(jnp.bfloat16)
    chosen = jnp.einsum(
        "crl,clk->crk", listed, ref_library, preferred_element_type=jnp.float32
    ).astype(jnp.bfloat16)
    piece = chosen.shape[-1]
    ref_send = jnp.broadcast_to(
        chosen.reshape(1, r_groups, ref_block, piece), (p_groups, r_groups, ref_block, piece)
    ).reshape(shards, ref_block, piece)
    ref_got = lax.all_to_all(ref_send, "shard", 0, 0, tiled=True)
    flattened = forward_spectra(particles).reshape(slots_here, -1)
    flattened, ref_got = lax.optimization_barrier((flattened, ref_got))
    refs = ref_got.transpose(1, 0, 2).reshape(ref_block, shards * piece)
    pieces = lax.all_to_all(flattened, "shard", split_axis=1, concat_axis=0, tiled=True)

    source = (
        jnp.zeros((positions,), jnp.int32)
        .at[jnp.where(slot_target >= 0, slot_target, positions)]
        .set(jnp.arange(every_slot, dtype=jnp.int32), mode="drop")
    )
    my_sources = lax.dynamic_slice_in_dim(source, my_pblock * part_block, part_block, 0)
    bin_ids, pieces = lax.optimization_barrier((slot_defocus_level[my_sources], pieces))
    contrast = particle_contrast(bin_ids, defocus)
    energy_ref = reference_energy(contrast, refs)
    if r_groups % 2 == 0:
        half = shards // 2
        core = my_index % 2
        groups = [[2 * m + q for m in range(half)] for q in range(2)]
        picked = pieces[source].reshape(p_groups, 1, part_block, piece)
        part_send = jnp.broadcast_to(
            picked, (p_groups, r_groups // 2, part_block, piece)
        ).reshape(half, part_block, piece)
        mine = lax.all_to_all(part_send, "shard", 0, 0, tiled=True, axis_index_groups=groups)
        other = lax.ppermute(mine, "shard", [(d, d ^ 1) for d in range(shards)])
        even = jnp.where(core == 0, mine, other)
        odd = jnp.where(core == 0, other, mine)
        part_got = jnp.stack([even, odd], axis=1).reshape(shards, part_block, piece)
    else:
        part_send = jnp.broadcast_to(
            pieces[source].reshape(p_groups, 1, part_block, piece),
            (p_groups, r_groups, part_block, piece),
        ).reshape(shards, part_block, piece)
        part_got = lax.all_to_all(part_send, "shard", 0, 0, tiled=True)
    spectra = part_got.transpose(1, 0, 2).reshape(part_block, -1)
    block_scores = score_block(spectra, contrast, energy_ref, refs)

    targets = slot_target.reshape(shards, slots_here)
    in_block = (targets >= 0) & (targets // part_block == my_pblock)
    rows = block_scores[jnp.clip(targets - my_pblock * part_block, 0, part_block - 1)]
    back_send = jnp.where(in_block[:, :, None], rows, jnp.float32(0.0))
    back_got = lax.all_to_all(back_send, "shard", 0, 0, tiled=True)
    scores = (
        back_got.reshape(p_groups, r_groups, slots_here, ref_block)
        .sum(axis=0)
        .transpose(1, 0, 2)
        .reshape(slots_here, classes, rotations)
    )
    return (scores, jnp.max(scores, axis=2))


def solution(mesh):
    in_specs = (
        P(("groups", "shard"), None, None),
        P("groups"),
        P("groups"),
        P("groups"),
        P("groups", None, "shard"),
        P("groups", None),
    )
    out_specs = (P(("groups", "shard"), None, None), P(("groups", "shard"), None))
    return jax.shard_map(
        per_device, mesh=mesh, in_specs=in_specs, out_specs=out_specs, check_vma=False
    )
```

```python
import numpy as np
import jax
import jax.numpy as jnp
from jax import lax
from jax.experimental import pallas as pl
from jax.experimental.pallas import tpu as pltpu
from jax.sharding import PartitionSpec as P

BOX = 64
BAND = 32
SHIFTS = 8
PART_DEV = 1


def signed_band(band_size):
    return jnp.arange(band_size, dtype=jnp.int32) - band_size // 2


def table_pair(outer_loop_index, inner_index, box_edge):
    phase_index = outer_loop_index[:, None] * inner_index[None, :] % box_edge
    angles = phase_index.astype(jnp.float32) * (2.0 * jnp.pi / box_edge)
    return (jnp.cos(angles).astype(jnp.bfloat16), jnp.sin(angles).astype(jnp.bfloat16))


def spectral_product(form, left, right):
    return jnp.einsum(form, left, right, preferred_element_type=jnp.float32)


def forward_spectra(volumes):
    batch_size, box_edge = (volumes.shape[0], volumes.shape[1])
    cosine_forward, sine_forward = table_pair(
        signed_band(BAND), jnp.arange(box_edge, dtype=jnp.int32), box_edge
    )
    density_volume = volumes.astype(jnp.bfloat16)
    leading_real = spectral_product("qw,rwl->rql", cosine_forward, density_volume).astype(
        jnp.bfloat16
    )
    leading_imaginary = (-spectral_product("qw,rwl->rql", sine_forward, density_volume)).astype(
        jnp.bfloat16
    )
    leading_real = leading_real.reshape(batch_size, BAND, box_edge, box_edge)
    leading_imaginary = leading_imaginary.reshape(batch_size, BAND, box_edge, box_edge)
    second_real = (
        spectral_product("jy,nkyz->nkjz", cosine_forward, leading_real)
        + spectral_product("jy,nkyz->nkjz", sine_forward, leading_imaginary)
    ).astype(jnp.bfloat16)
    second_imag = (
        spectral_product("jy,nkyz->nkjz", cosine_forward, leading_imaginary)
        - spectral_product("jy,nkyz->nkjz", sine_forward, leading_real)
    ).astype(jnp.bfloat16)
    third_real = spectral_product("nkjz,lz->nkjl", second_real, cosine_forward) + spectral_product(
        "nkjz,lz->nkjl", second_imag, sine_forward
    )
    third_imag = spectral_product("nkjz,lz->nkjl", second_imag, cosine_forward) - spectral_product(
        "nkjz,lz->nkjl", second_real, sine_forward
    )
    spectrum = jnp.stack([third_real, third_imag], axis=1).astype(jnp.bfloat16)
    return spectrum.reshape(batch_size, 2, BAND * BAND * BAND)


def plane_table():
    k = np.arange(BAND) - BAND // 2
    t = np.arange(SHIFTS) - SHIFTS // 2
    phase = (
        t[None, None, :, None] * k[:, None, None, None]
        + t[None, None, None, :] * k[None, :, None, None]
    ) % BOX
    angles = phase.astype(np.float32) * np.float32(2.0 * np.pi / BOX)
    shape = (BAND * BAND, SHIFTS * SHIFTS)
    cosine = np.cos(angles).reshape(shape)
    sine = np.sin(angles).reshape(shape)
    upper = np.concatenate([cosine, sine], axis=1)
    lower = np.concatenate([-sine, cosine], axis=1)
    return jnp.asarray(np.concatenate([upper, lower], axis=0), dtype=jnp.bfloat16)


def shift_tables(n_ref):
    k = np.arange(BAND) - BAND // 2
    t = np.arange(SHIFTS) - SHIFTS // 2
    angles = ((t[:, None] * k[None, :]) % BOX).astype(np.float32) * np.float32(2.0 * np.pi / BOX)
    eye = np.eye(n_ref, dtype=np.float32)
    def rounded(x):
        return jnp.asarray(x, dtype=jnp.bfloat16).astype(jnp.float32)
    return rounded(np.kron(eye, np.cos(angles))), rounded(np.kron(eye, np.sin(angles)))


def correlation_kernel(s_ref, g_ref, c_ref, t_ref, ec_ref, es_ref, o_ref, e_ref, p_s):
    n_ref = c_ref.shape[0]
    plane = BAND * BAND
    contrast = g_ref[0]
    s_real = s_ref[0, 0].astype(jnp.float32)
    s_imag = s_ref[0, 1].astype(jnp.float32)
    w_real = (contrast * s_real).astype(jnp.bfloat16).astype(jnp.float32)
    w_imag = (-(contrast * s_imag)).astype(jnp.bfloat16).astype(jnp.float32)
    for j in range(n_ref):
        c_real = c_ref[j, 0]
        c_imag = c_ref[j, 1]
        rows = slice(j * BAND, (j + 1) * BAND)
        p_s[rows, :plane] = (w_real * c_real - w_imag * c_imag).astype(jnp.bfloat16)
        p_s[rows, plane:] = (w_real * c_imag + w_imag * c_real).astype(jnp.bfloat16)
    planes = jnp.dot(p_s[...], t_ref[...], preferred_element_type=jnp.float32)
    first = jnp.dot(ec_ref[...], planes, preferred_element_type=jnp.float32,
                    precision=lax.Precision.HIGHEST)
    second = jnp.dot(es_ref[...], planes, preferred_element_type=jnp.float32,
                     precision=lax.Precision.HIGHEST)
    half = SHIFTS * SHIFTS
    correlation = first - pltpu.roll(second, half, 1)
    lane = lax.broadcasted_iota(jnp.int32, correlation.shape, 1)
    correlation = jnp.where(lane < half, correlation, -jnp.inf)
    per_row = jnp.max(correlation.reshape(n_ref, SHIFTS, 2 * half), axis=1)
    peak = jnp.max(per_row, axis=1, keepdims=True)
    o_ref[0] = jnp.broadcast_to(peak, (n_ref, 2 * half))
    power = jnp.sum(s_real * s_real + s_imag * s_imag, axis=0, keepdims=True)
    e_ref[0] = jnp.broadcast_to(jnp.sum(power, axis=1, keepdims=True), (8, 2 * half))


def peak_correlations(spectra, contrast, refs):
    n_part = spectra.shape[0]
    n_ref = refs.shape[0]
    plane = BAND * BAND
    e_cos, e_sin = shift_tables(n_ref)
    width = 2 * SHIFTS * SHIFTS
    peak, energy = pl.pallas_call(
        correlation_kernel,
        grid=(n_part,),
        in_specs=[
            pl.BlockSpec((1, 2, BAND, plane), lambda i: (i, 0, 0, 0)),
            pl.BlockSpec((1, BAND, plane), lambda i: (i, 0, 0)),
            pl.BlockSpec((n_ref, 2, BAND, plane), lambda i: (0, 0, 0, 0)),
            pl.BlockSpec((2 * plane, width), lambda i: (0, 0)),
            pl.BlockSpec((n_ref * SHIFTS, n_ref * BAND), lambda i: (0, 0)),
            pl.BlockSpec((n_ref * SHIFTS, n_ref * BAND), lambda i: (0, 0)),
        ],
        out_specs=[
            pl.BlockSpec((1, n_ref, width), lambda i: (i, 0, 0)),
            pl.BlockSpec((1, 8, width), lambda i: (i, 0, 0)),
        ],
        out_shape=[
            jax.ShapeDtypeStruct((n_part, n_ref, width), jnp.float32),
            jax.ShapeDtypeStruct((n_part, 8, width), jnp.float32),
        ],
        scratch_shapes=[pltpu.VMEM((n_ref * BAND, 2 * plane), jnp.bfloat16)],
        cost_estimate=pl.CostEstimate(
            flops=n_part * n_ref * (2 * BAND * 2 * plane * width + 8 * BAND * plane),
            transcendentals=0,
            bytes_accessed=n_part * 8 * BAND * plane + n_ref * 8 * BAND * plane,
        ),
    )(spectra, contrast, refs, plane_table(), e_cos, e_sin)
    return peak[:, :, 0], energy[:, 0, 0]


def particle_contrast(bin_ids, defocus):
    band_index = signed_band(BAND).astype(jnp.float32)
    radius = (
        band_index[:, None, None] ** 2
        + band_index[None, :, None] ** 2
        + band_index[None, None, :] ** 2
    ).reshape(-1) / (BAND / 2) ** 2
    chosen_defocus = jnp.sum(
        jnp.where(
            bin_ids[:, None] == jnp.arange(defocus.shape[0], dtype=jnp.int32)[None, :],
            defocus[None, :],
            jnp.float32(0.0),
        ),
        axis=1,
    )
    return -jnp.sin(chosen_defocus[:, None] * radius[None, :] + 0.07)


def reference_energy(contrast, refs):
    volume_size = BAND * BAND * BAND
    ref_real = refs[:, :volume_size].astype(jnp.float32)
    ref_imag = refs[:, volume_size:].astype(jnp.float32)
    magnitude = ref_real * ref_real + ref_imag * ref_imag
    return jnp.sum((contrast * contrast)[:, None, :] * magnitude[None, :, :], axis=2)


def score_block(spectra, contrast, energy_ref, refs):
    n_part = spectra.shape[0]
    n_ref = refs.shape[0]
    shape = (BAND, BAND * BAND)
    peak_value, energy_particle = peak_correlations(
        spectra.reshape(n_part, 2, *shape),
        contrast.reshape(n_part, *shape),
        refs,
    )
    score_scale = float(BAND) ** 1.5
    return score_scale * peak_value * lax.rsqrt(energy_particle[:, None] * energy_ref + 1e-06)


def ref_groups(shards, particles, refs):
    best = None
    for groups in range(1, shards + 1):
        if shards % groups or refs % groups or particles % (shards // groups):
            continue
        cost = particles * groups // shards + refs // groups
        if best is None or cost < best[0]:
            best = (cost, groups)
    return best[1]


def per_device(particles, slot_target, slot_defocus_level, defocus, ref_library, rotation_list):
    shards = lax.axis_size("shard")
    my_index = lax.axis_index("shard")
    slots_here = particles.shape[0]
    positions = PART_DEV * shards
    every_slot = slot_target.shape[0]
    classes, rotations = rotation_list.shape
    n_refs = classes * rotations
    r_groups = ref_groups(shards, positions, n_refs)
    p_groups = shards // r_groups
    part_block = positions // p_groups
    ref_block = n_refs // r_groups
    my_pblock = my_index // r_groups

    library = ref_library.shape[1]
    listed = (rotation_list[:, :, None] == jnp.arange(library, dtype=jnp.int32)).astype(jnp.bfloat16)
    chosen = jnp.einsum(
        "crl,clk->crk", listed, ref_library, preferred_element_type=jnp.float32
    ).astype(jnp.bfloat16)
    piece = chosen.shape[-1]
    ref_send = jnp.broadcast_to(
        chosen.reshape(1, r_groups, ref_block, piece), (p_groups, r_groups, ref_block, piece)
    ).reshape(shards, ref_block, piece)
    ref_got = lax.all_to_all(ref_send, "shard", 0, 0, tiled=True)
    flattened = forward_spectra(particles).reshape(slots_here, -1)
    source = (
        jnp.zeros((positions,), jnp.int32)
        .at[jnp.where(slot_target >= 0, slot_target, positions)]
        .set(jnp.arange(every_slot, dtype=jnp.int32), mode="drop")
    )
    my_sources = lax.dynamic_slice_in_dim(source, my_pblock * part_block, part_block, 0)
    flattened, ref_got, bin_ids = lax.optimization_barrier(
        (flattened, ref_got, slot_defocus_level[my_sources])
    )
    contrast = lax.optimization_barrier(particle_contrast(bin_ids, defocus))
    refs = ref_got.transpose(1, 0, 2).reshape(ref_block, shards * piece)
    pieces = lax.all_to_all(flattened, "shard", split_axis=1, concat_axis=0, tiled=True)

    energy_ref = reference_energy(contrast, refs)
    refs_wide = refs.reshape(ref_block, 2, BAND, BAND * BAND).astype(jnp.float32)
    if r_groups % 2 == 0:
        half = shards // 2
        core = my_index % 2
        groups = [[2 * m + q for m in range(half)] for q in range(2)]
        picked = pieces[source].reshape(p_groups, 1, part_block, piece)
        picked, refs_wide, contrast, energy_ref = lax.optimization_barrier(
            (picked, refs_wide, contrast, energy_ref)
        )
        part_send = jnp.broadcast_to(
            picked, (p_groups, r_groups // 2, part_block, piece)
        ).reshape(half, part_block, piece)
        mine = lax.all_to_all(part_send, "shard", 0, 0, tiled=True, axis_index_groups=groups)
        other = lax.ppermute(mine, "shard", [(d, d ^ 1) for d in range(shards)])
        even = jnp.where(core == 0, mine, other)
        odd = jnp.where(core == 0, other, mine)
        part_got = jnp.stack([even, odd], axis=1).reshape(shards, part_block, piece)
    else:
        part_send = jnp.broadcast_to(
            pieces[source].reshape(p_groups, 1, part_block, piece),
            (p_groups, r_groups, part_block, piece),
        ).reshape(shards, part_block, piece)
        part_got = lax.all_to_all(part_send, "shard", 0, 0, tiled=True)
    spectra = part_got.transpose(1, 0, 2).reshape(part_block, -1)
    block_scores = score_block(spectra, contrast, energy_ref, refs_wide)

    targets = slot_target.reshape(shards, slots_here)
    in_block = (targets >= 0) & (targets // part_block == my_pblock)
    rows = block_scores[jnp.clip(targets - my_pblock * part_block, 0, part_block - 1)]
    back_send = jnp.where(in_block[:, :, None], rows, jnp.float32(0.0))
    back_got = lax.all_to_all(back_send, "shard", 0, 0, tiled=True)
    scores = (
        back_got.reshape(p_groups, r_groups, slots_here, ref_block)
        .sum(axis=0)
        .transpose(1, 0, 2)
        .reshape(slots_here, classes, rotations)
    )
    return (scores, jnp.max(scores, axis=2))


def solution(mesh):
    in_specs = (
        P(("groups", "shard"), None, None),
        P("groups"),
        P("groups"),
        P("groups"),
        P("groups", None, "shard"),
        P("groups", None),
    )
    out_specs = (P(("groups", "shard"), None, None), P(("groups", "shard"), None))
    return jax.shard_map(
        per_device, mesh=mesh, in_specs=in_specs, out_specs=out_specs, check_vma=False
    )
```

```python
import numpy as np
import jax
import jax.numpy as jnp
from jax import lax
from jax.experimental import pallas as pl
from jax.experimental.pallas import tpu as pltpu
from jax.sharding import PartitionSpec as P

BOX = 64
BAND = 32
SHIFTS = 8
PART_DEV = 1


def signed_band(band_size):
    return jnp.arange(band_size, dtype=jnp.int32) - band_size // 2


def table_pair(outer_loop_index, inner_index, box_edge):
    phase_index = outer_loop_index[:, None] * inner_index[None, :] % box_edge
    angles = phase_index.astype(jnp.float32) * (2.0 * jnp.pi / box_edge)
    return (jnp.cos(angles).astype(jnp.bfloat16), jnp.sin(angles).astype(jnp.bfloat16))


def spectral_product(form, left, right):
    return jnp.einsum(form, left, right, preferred_element_type=jnp.float32)


def forward_spectra(volumes):
    batch_size, box_edge = (volumes.shape[0], volumes.shape[1])
    cosine_forward, sine_forward = table_pair(
        signed_band(BAND), jnp.arange(box_edge, dtype=jnp.int32), box_edge
    )
    density_volume = volumes.astype(jnp.bfloat16)
    leading_real = spectral_product("qw,rwl->rql", cosine_forward, density_volume).astype(
        jnp.bfloat16
    )
    leading_imaginary = (-spectral_product("qw,rwl->rql", sine_forward, density_volume)).astype(
        jnp.bfloat16
    )
    leading_real = leading_real.reshape(batch_size, BAND, box_edge, box_edge)
    leading_imaginary = leading_imaginary.reshape(batch_size, BAND, box_edge, box_edge)
    second_real = (
        spectral_product("jy,nkyz->nkjz", cosine_forward, leading_real)
        + spectral_product("jy,nkyz->nkjz", sine_forward, leading_imaginary)
    ).astype(jnp.bfloat16)
    second_imag = (
        spectral_product("jy,nkyz->nkjz", cosine_forward, leading_imaginary)
        - spectral_product("jy,nkyz->nkjz", sine_forward, leading_real)
    ).astype(jnp.bfloat16)
    third_real = spectral_product("nkjz,lz->nkjl", second_real, cosine_forward) + spectral_product(
        "nkjz,lz->nkjl", second_imag, sine_forward
    )
    third_imag = spectral_product("nkjz,lz->nkjl", second_imag, cosine_forward) - spectral_product(
        "nkjz,lz->nkjl", second_real, sine_forward
    )
    spectrum = jnp.stack([third_real, third_imag], axis=1).astype(jnp.bfloat16)
    return spectrum.reshape(batch_size, 2, BAND * BAND * BAND)


def plane_table():
    k = np.arange(BAND) - BAND // 2
    t = np.arange(SHIFTS) - SHIFTS // 2
    phase = (
        t[None, None, :, None] * k[:, None, None, None]
        + t[None, None, None, :] * k[None, :, None, None]
    ) % BOX
    angles = phase.astype(np.float32) * np.float32(2.0 * np.pi / BOX)
    shape = (BAND * BAND, SHIFTS * SHIFTS)
    cosine = np.cos(angles).reshape(shape)
    sine = np.sin(angles).reshape(shape)
    upper = np.concatenate([cosine, sine], axis=1)
    lower = np.concatenate([-sine, cosine], axis=1)
    return jnp.asarray(np.concatenate([upper, lower], axis=0), dtype=jnp.bfloat16)


def shift_tables(n_ref):
    k = np.arange(BAND) - BAND // 2
    t = np.arange(SHIFTS) - SHIFTS // 2
    angles = ((t[:, None] * k[None, :]) % BOX).astype(np.float32) * np.float32(2.0 * np.pi / BOX)
    eye = np.eye(n_ref, dtype=np.float32)
    def rounded(x):
        return jnp.asarray(x, dtype=jnp.bfloat16).astype(jnp.float32)
    return rounded(np.kron(eye, np.cos(angles))), rounded(np.kron(eye, np.sin(angles)))


def correlation_kernel(s_ref, g_ref, c_ref, t_ref, ec_ref, es_ref, o_ref, e_ref, p_s):
    n_ref = c_ref.shape[0]
    plane = BAND * BAND
    contrast = g_ref[0]
    s_real = s_ref[0, 0].astype(jnp.float32)
    s_imag = s_ref[0, 1].astype(jnp.float32)
    w_real = (contrast * s_real).astype(jnp.bfloat16).astype(jnp.float32)
    w_imag = (-(contrast * s_imag)).astype(jnp.bfloat16).astype(jnp.float32)
    for j in range(n_ref):
        c_real = c_ref[j, 0]
        c_imag = c_ref[j, 1]
        rows = slice(j * BAND, (j + 1) * BAND)
        p_s[rows, :plane] = (w_real * c_real - w_imag * c_imag).astype(jnp.bfloat16)
        p_s[rows, plane:] = (w_real * c_imag + w_imag * c_real).astype(jnp.bfloat16)
    planes = jnp.dot(p_s[...], t_ref[...], preferred_element_type=jnp.float32)
    first = jnp.dot(ec_ref[...], planes, preferred_element_type=jnp.float32,
                    precision=lax.Precision.HIGHEST)
    second = jnp.dot(es_ref[...], planes, preferred_element_type=jnp.float32,
                     precision=lax.Precision.HIGHEST)
    half = SHIFTS * SHIFTS
    correlation = first - pltpu.roll(second, half, 1)
    lane = lax.broadcasted_iota(jnp.int32, correlation.shape, 1)
    correlation = jnp.where(lane < half, correlation, -jnp.inf)
    per_row = jnp.max(correlation.reshape(n_ref, SHIFTS, 2 * half), axis=1)
    peak = jnp.max(per_row, axis=1, keepdims=True)
    o_ref[0] = jnp.broadcast_to(peak, (n_ref, 2 * half))
    power = jnp.sum(s_real * s_real + s_imag * s_imag, axis=0, keepdims=True)
    e_ref[0] = jnp.broadcast_to(jnp.sum(power, axis=1, keepdims=True), (8, 2 * half))


def peak_correlations(spectra, contrast, refs):
    n_part = spectra.shape[0]
    n_ref = refs.shape[0]
    plane = BAND * BAND
    e_cos, e_sin = shift_tables(n_ref)
    width = 2 * SHIFTS * SHIFTS
    peak, energy = pl.pallas_call(
        correlation_kernel,
        grid=(n_part,),
        in_specs=[
            pl.BlockSpec((1, 2, BAND, plane), lambda i: (i, 0, 0, 0)),
            pl.BlockSpec((1, BAND, plane), lambda i: (i, 0, 0)),
            pl.BlockSpec((n_ref, 2, BAND, plane), lambda i: (0, 0, 0, 0)),
            pl.BlockSpec((2 * plane, width), lambda i: (0, 0)),
            pl.BlockSpec((n_ref * SHIFTS, n_ref * BAND), lambda i: (0, 0)),
            pl.BlockSpec((n_ref * SHIFTS, n_ref * BAND), lambda i: (0, 0)),
        ],
        out_specs=[
            pl.BlockSpec((1, n_ref, width), lambda i: (i, 0, 0)),
            pl.BlockSpec((1, 8, width), lambda i: (i, 0, 0)),
        ],
        out_shape=[
            jax.ShapeDtypeStruct((n_part, n_ref, width), jnp.float32),
            jax.ShapeDtypeStruct((n_part, 8, width), jnp.float32),
        ],
        scratch_shapes=[pltpu.VMEM((n_ref * BAND, 2 * plane), jnp.bfloat16)],
        cost_estimate=pl.CostEstimate(
            flops=n_part * n_ref * (2 * BAND * 2 * plane * width + 8 * BAND * plane),
            transcendentals=0,
            bytes_accessed=n_part * 8 * BAND * plane + n_ref * 8 * BAND * plane,
        ),
    )(spectra, contrast, refs, plane_table(), e_cos, e_sin)
    return peak[:, :, 0], energy[:, 0, 0]


def particle_contrast(bin_ids, defocus):
    band_index = signed_band(BAND).astype(jnp.float32)
    radius = (
        band_index[:, None, None] ** 2
        + band_index[None, :, None] ** 2
        + band_index[None, None, :] ** 2
    ).reshape(-1) / (BAND / 2) ** 2
    chosen_defocus = jnp.sum(
        jnp.where(
            bin_ids[:, None] == jnp.arange(defocus.shape[0], dtype=jnp.int32)[None, :],
            defocus[None, :],
            jnp.float32(0.0),
        ),
        axis=1,
    )
    return -jnp.sin(chosen_defocus[:, None] * radius[None, :] + 0.07)


def reference_energy(contrast, refs):
    volume_size = BAND * BAND * BAND
    ref_real = refs[:, :volume_size].astype(jnp.float32)
    ref_imag = refs[:, volume_size:].astype(jnp.float32)
    magnitude = ref_real * ref_real + ref_imag * ref_imag
    return jnp.sum((contrast * contrast)[:, None, :] * magnitude[None, :, :], axis=2)


def score_block(spectra, contrast, energy_ref, refs):
    n_part = spectra.shape[0]
    n_ref = refs.shape[0]
    shape = (BAND, BAND * BAND)
    peak_value, energy_particle = peak_correlations(
        spectra.reshape(n_part, 2, *shape),
        contrast.reshape(n_part, *shape),
        refs,
    )
    score_scale = float(BAND) ** 1.5
    return score_scale * peak_value * lax.rsqrt(energy_particle[:, None] * energy_ref + 1e-06)


def ref_groups(shards, particles, refs):
    best = None
    for groups in range(1, shards + 1):
        if shards % groups or refs % groups or particles % (shards // groups):
            continue
        cost = particles * groups // shards + refs // groups
        if best is None or cost < best[0]:
            best = (cost, groups)
    return best[1]


def per_device(particles, slot_target, slot_defocus_level, defocus, ref_library, rotation_list):
    shards = lax.axis_size("shard")
    my_index = lax.axis_index("shard")
    slots_here = particles.shape[0]
    positions = PART_DEV * shards
    every_slot = slot_target.shape[0]
    classes, rotations = rotation_list.shape
    n_refs = classes * rotations
    r_groups = ref_groups(shards, positions, n_refs)
    p_groups = shards // r_groups
    part_block = positions // p_groups
    ref_block = n_refs // r_groups
    my_pblock = my_index // r_groups

    library = ref_library.shape[1]
    listed = (rotation_list[:, :, None] == jnp.arange(library, dtype=jnp.int32)).astype(jnp.bfloat16)
    chosen = jnp.einsum(
        "crl,clk->crk", listed, ref_library, preferred_element_type=jnp.float32
    ).astype(jnp.bfloat16)
    piece = chosen.shape[-1]
    ref_send = jnp.broadcast_to(
        chosen.reshape(1, r_groups, ref_block, piece), (p_groups, r_groups, ref_block, piece)
    ).reshape(shards, ref_block, piece)
    ref_got = lax.all_to_all(ref_send, "shard", 0, 0, tiled=True)
    flattened = forward_spectra(particles).reshape(slots_here, -1)
    source = (
        jnp.zeros((positions,), jnp.int32)
        .at[jnp.where(slot_target >= 0, slot_target, positions)]
        .set(jnp.arange(every_slot, dtype=jnp.int32), mode="drop")
    )
    my_sources = lax.dynamic_slice_in_dim(source, my_pblock * part_block, part_block, 0)
    flattened, ref_got, bin_ids = lax.optimization_barrier(
        (flattened, ref_got, slot_defocus_level[my_sources])
    )
    contrast = lax.optimization_barrier(particle_contrast(bin_ids, defocus))
    refs = ref_got.transpose(1, 0, 2).reshape(ref_block, shards * piece)
    pieces = lax.all_to_all(flattened, "shard", split_axis=1, concat_axis=0, tiled=True)

    energy_ref = reference_energy(contrast, refs)
    refs_wide = refs.reshape(ref_block, 2, BAND, BAND * BAND).astype(jnp.float32)
    if r_groups % 2 == 0:
        half = shards // 2
        core = my_index % 2
        groups = [[2 * m + q for m in range(half)] for q in range(2)]
        picked = pieces[source].reshape(p_groups, 1, part_block, piece)
        picked, contrast, energy_ref = lax.optimization_barrier(
            (picked, contrast.reshape(part_block, BAND, BAND * BAND), energy_ref)
        )
        part_send = jnp.broadcast_to(
            picked, (p_groups, r_groups // 2, part_block, piece)
        ).reshape(half, part_block, piece)
        mine = lax.all_to_all(part_send, "shard", 0, 0, tiled=True, axis_index_groups=groups)
        mine, refs_wide = lax.optimization_barrier((mine, refs_wide))
        other = lax.ppermute(mine, "shard", [(d, d ^ 1) for d in range(shards)])
        even = jnp.where(core == 0, mine, other)
        odd = jnp.where(core == 0, other, mine)
        part_got = jnp.stack([even, odd], axis=1).reshape(shards, part_block, piece)
    else:
        part_send = jnp.broadcast_to(
            pieces[source].reshape(p_groups, 1, part_block, piece),
            (p_groups, r_groups, part_block, piece),
        ).reshape(shards, part_block, piece)
        part_got = lax.all_to_all(part_send, "shard", 0, 0, tiled=True)
    spectra = part_got.transpose(1, 0, 2).reshape(part_block, -1)
    block_scores = score_block(spectra, contrast, energy_ref, refs_wide)

    targets = slot_target.reshape(shards, slots_here)
    in_block = (targets >= 0) & (targets // part_block == my_pblock)
    rows = block_scores[jnp.clip(targets - my_pblock * part_block, 0, part_block - 1)]
    back_send = jnp.where(in_block[:, :, None], rows, jnp.float32(0.0))
    back_got = lax.all_to_all(back_send, "shard", 0, 0, tiled=True)
    scores = (
        back_got.reshape(p_groups, r_groups, slots_here, ref_block)
        .sum(axis=0)
        .transpose(1, 0, 2)
        .reshape(slots_here, classes, rotations)
    )
    return (scores, jnp.max(scores, axis=2))


def solution(mesh):
    in_specs = (
        P(("groups", "shard"), None, None),
        P("groups"),
        P("groups"),
        P("groups"),
        P("groups", None, "shard"),
        P("groups", None),
    )
    out_specs = (P(("groups", "shard"), None, None), P(("groups", "shard"), None))
    return jax.shard_map(
        per_device, mesh=mesh, in_specs=in_specs, out_specs=out_specs, check_vma=False
    )
```

```python
import numpy as np
import jax
import jax.numpy as jnp
from jax import lax
from jax.experimental import pallas as pl
from jax.experimental.pallas import tpu as pltpu
from jax.sharding import PartitionSpec as P

BOX = 64
BAND = 32
SHIFTS = 8
PART_DEV = 1


def signed_band(band_size):
    return jnp.arange(band_size, dtype=jnp.int32) - band_size // 2


def table_pair(outer_loop_index, inner_index, box_edge):
    phase_index = outer_loop_index[:, None] * inner_index[None, :] % box_edge
    angles = phase_index.astype(jnp.float32) * (2.0 * jnp.pi / box_edge)
    return (jnp.cos(angles).astype(jnp.bfloat16), jnp.sin(angles).astype(jnp.bfloat16))


def spectral_product(form, left, right):
    return jnp.einsum(form, left, right, preferred_element_type=jnp.float32)


def forward_spectra(volumes):
    batch_size, box_edge = (volumes.shape[0], volumes.shape[1])
    cosine_forward, sine_forward = table_pair(
        signed_band(BAND), jnp.arange(box_edge, dtype=jnp.int32), box_edge
    )
    density_volume = volumes.astype(jnp.bfloat16)
    leading_real = spectral_product("qw,rwl->rql", cosine_forward, density_volume).astype(
        jnp.bfloat16
    )
    leading_imaginary = (-spectral_product("qw,rwl->rql", sine_forward, density_volume)).astype(
        jnp.bfloat16
    )
    leading_real = leading_real.reshape(batch_size, BAND, box_edge, box_edge)
    leading_imaginary = leading_imaginary.reshape(batch_size, BAND, box_edge, box_edge)
    second_real = (
        spectral_product("jy,nkyz->nkjz", cosine_forward, leading_real)
        + spectral_product("jy,nkyz->nkjz", sine_forward, leading_imaginary)
    ).astype(jnp.bfloat16)
    second_imag = (
        spectral_product("jy,nkyz->nkjz", cosine_forward, leading_imaginary)
        - spectral_product("jy,nkyz->nkjz", sine_forward, leading_real)
    ).astype(jnp.bfloat16)
    third_real = spectral_product("nkjz,lz->nkjl", second_real, cosine_forward) + spectral_product(
        "nkjz,lz->nkjl", second_imag, sine_forward
    )
    third_imag = spectral_product("nkjz,lz->nkjl", second_imag, cosine_forward) - spectral_product(
        "nkjz,lz->nkjl", second_real, sine_forward
    )
    spectrum = jnp.stack([third_real, third_imag], axis=1).astype(jnp.bfloat16)
    return spectrum.reshape(batch_size, 2, BAND * BAND * BAND)


def plane_table():
    k = np.arange(BAND) - BAND // 2
    t = np.arange(SHIFTS) - SHIFTS // 2
    phase = (
        t[None, None, :, None] * k[:, None, None, None]
        + t[None, None, None, :] * k[None, :, None, None]
    ) % BOX
    angles = phase.astype(np.float32) * np.float32(2.0 * np.pi / BOX)
    shape = (BAND * BAND, SHIFTS * SHIFTS)
    cosine = np.cos(angles).reshape(shape)
    sine = np.sin(angles).reshape(shape)
    upper = np.concatenate([cosine, sine], axis=1)
    lower = np.concatenate([-sine, cosine], axis=1)
    return jnp.asarray(np.concatenate([upper, lower], axis=0), dtype=jnp.bfloat16)


def shift_tables(n_ref):
    k = np.arange(BAND) - BAND // 2
    t = np.arange(SHIFTS) - SHIFTS // 2
    angles = ((t[:, None] * k[None, :]) % BOX).astype(np.float32) * np.float32(2.0 * np.pi / BOX)
    eye = np.eye(n_ref, dtype=np.float32)
    def rounded(x):
        return jnp.asarray(x, dtype=jnp.bfloat16).astype(jnp.float32)
    return rounded(np.kron(eye, np.cos(angles))), rounded(np.kron(eye, np.sin(angles)))


def correlation_kernel(s_ref, g_ref, c_ref, t_ref, ec_ref, es_ref, o_ref, e_ref, p_s):
    n_part = s_ref.shape[0]
    n_ref = c_ref.shape[0]
    plane = BAND * BAND
    half = SHIFTS * SHIFTS

    def one_particle(i, carry):
        contrast = g_ref[i]
        s_real = s_ref[i, 0].astype(jnp.float32)
        s_imag = s_ref[i, 1].astype(jnp.float32)
        w_real = (contrast * s_real).astype(jnp.bfloat16).astype(jnp.float32)
        w_imag = (-(contrast * s_imag)).astype(jnp.bfloat16).astype(jnp.float32)
        for j in range(n_ref):
            c_real = c_ref[j, 0]
            c_imag = c_ref[j, 1]
            rows = slice(j * BAND, (j + 1) * BAND)
            p_s[rows, :plane] = (w_real * c_real - w_imag * c_imag).astype(jnp.bfloat16)
            p_s[rows, plane:] = (w_real * c_imag + w_imag * c_real).astype(jnp.bfloat16)
        planes = jnp.dot(p_s[...], t_ref[...], preferred_element_type=jnp.float32)
        first = jnp.dot(ec_ref[...], planes, preferred_element_type=jnp.float32,
                        precision=lax.Precision.HIGHEST)
        second = jnp.dot(es_ref[...], planes, preferred_element_type=jnp.float32,
                         precision=lax.Precision.HIGHEST)
        correlation = first - pltpu.roll(second, half, 1)
        lane = lax.broadcasted_iota(jnp.int32, correlation.shape, 1)
        correlation = jnp.where(lane < half, correlation, -jnp.inf)
        per_row = jnp.max(correlation.reshape(n_ref, SHIFTS, 2 * half), axis=1)
        peak = jnp.max(per_row, axis=1, keepdims=True)
        o_ref[i] = jnp.broadcast_to(peak, (n_ref, 2 * half))
        power = jnp.sum(s_real * s_real + s_imag * s_imag, axis=0, keepdims=True)
        e_ref[i] = jnp.broadcast_to(jnp.sum(power, axis=1, keepdims=True), (8, 2 * half))
        return carry

    lax.fori_loop(0, n_part, one_particle, 0)


def peak_correlations(spectra, contrast, refs):
    n_part = spectra.shape[0]
    n_ref = refs.shape[0]
    plane = BAND * BAND
    e_cos, e_sin = shift_tables(n_ref)
    width = 2 * SHIFTS * SHIFTS
    whole = pl.BlockSpec(memory_space=pltpu.VMEM)
    peak, energy = pl.pallas_call(
        correlation_kernel,
        in_specs=[whole] * 6,
        out_specs=[whole, whole],
        out_shape=[
            jax.ShapeDtypeStruct((n_part, n_ref, width), jnp.float32),
            jax.ShapeDtypeStruct((n_part, 8, width), jnp.float32),
        ],
        scratch_shapes=[pltpu.VMEM((n_ref * BAND, 2 * plane), jnp.bfloat16)],
        cost_estimate=pl.CostEstimate(
            flops=n_part * n_ref * (2 * BAND * 2 * plane * width + 8 * BAND * plane),
            transcendentals=0,
            bytes_accessed=n_part * 8 * BAND * plane + n_ref * 8 * BAND * plane,
        ),
    )(spectra, contrast, refs, plane_table(), e_cos, e_sin)
    return peak[:, :, 0], energy[:, 0, 0]


def particle_contrast(bin_ids, defocus):
    band_index = signed_band(BAND).astype(jnp.float32)
    radius = (
        band_index[:, None, None] ** 2
        + band_index[None, :, None] ** 2
        + band_index[None, None, :] ** 2
    ).reshape(-1) / (BAND / 2) ** 2
    chosen_defocus = jnp.sum(
        jnp.where(
            bin_ids[:, None] == jnp.arange(defocus.shape[0], dtype=jnp.int32)[None, :],
            defocus[None, :],
            jnp.float32(0.0),
        ),
        axis=1,
    )
    return -jnp.sin(chosen_defocus[:, None] * radius[None, :] + 0.07)


def reference_energy(contrast, refs):
    volume_size = BAND * BAND * BAND
    ref_real = refs[:, :volume_size].astype(jnp.float32)
    ref_imag = refs[:, volume_size:].astype(jnp.float32)
    magnitude = ref_real * ref_real + ref_imag * ref_imag
    return jnp.sum((contrast * contrast)[:, None, :] * magnitude[None, :, :], axis=2)


def score_block(spectra, contrast, energy_ref, refs):
    n_part = spectra.shape[0]
    n_ref = refs.shape[0]
    shape = (BAND, BAND * BAND)
    peak_value, energy_particle = peak_correlations(
        spectra.reshape(n_part, 2, *shape),
        contrast.reshape(n_part, *shape),
        refs,
    )
    score_scale = float(BAND) ** 1.5
    return score_scale * peak_value * lax.rsqrt(energy_particle[:, None] * energy_ref + 1e-06)


def ref_groups(shards, particles, refs):
    best = None
    for groups in range(1, shards + 1):
        if shards % groups or refs % groups or particles % (shards // groups):
            continue
        cost = particles * groups // shards + refs // groups
        if best is None or cost < best[0]:
            best = (cost, groups)
    return best[1]


def per_device(particles, slot_target, slot_defocus_level, defocus, ref_library, rotation_list):
    shards = lax.axis_size("shard")
    my_index = lax.axis_index("shard")
    slots_here = particles.shape[0]
    positions = PART_DEV * shards
    every_slot = slot_target.shape[0]
    classes, rotations = rotation_list.shape
    n_refs = classes * rotations
    r_groups = ref_groups(shards, positions, n_refs)
    p_groups = shards // r_groups
    part_block = positions // p_groups
    ref_block = n_refs // r_groups
    my_pblock = my_index // r_groups

    library = ref_library.shape[1]
    listed = (rotation_list[:, :, None] == jnp.arange(library, dtype=jnp.int32)).astype(jnp.bfloat16)
    chosen = jnp.einsum(
        "crl,clk->crk", listed, ref_library, preferred_element_type=jnp.float32
    ).astype(jnp.bfloat16)
    piece = chosen.shape[-1]
    ref_send = jnp.broadcast_to(
        chosen.reshape(1, r_groups, ref_block, piece), (p_groups, r_groups, ref_block, piece)
    ).reshape(shards, ref_block, piece)
    ref_got = lax.all_to_all(ref_send, "shard", 0, 0, tiled=True)
    flattened = forward_spectra(particles).reshape(slots_here, -1)
    source = (
        jnp.zeros((positions,), jnp.int32)
        .at[jnp.where(slot_target >= 0, slot_target, positions)]
        .set(jnp.arange(every_slot, dtype=jnp.int32), mode="drop")
    )
    my_sources = lax.dynamic_slice_in_dim(source, my_pblock * part_block, part_block, 0)
    flattened, ref_got, bin_ids = lax.optimization_barrier(
        (flattened, ref_got, slot_defocus_level[my_sources])
    )
    contrast = lax.optimization_barrier(particle_contrast(bin_ids, defocus))
    refs = ref_got.transpose(1, 0, 2).reshape(ref_block, shards * piece)
    pieces = lax.all_to_all(flattened, "shard", split_axis=1, concat_axis=0, tiled=True)

    energy_ref = reference_energy(contrast, refs)
    refs_wide = refs.reshape(ref_block, 2, BAND, BAND * BAND).astype(jnp.float32)
    if r_groups % 2 == 0:
        half = shards // 2
        core = my_index % 2
        groups = [[2 * m + q for m in range(half)] for q in range(2)]
        picked = pieces[source].reshape(p_groups, 1, part_block, piece)
        picked, contrast, energy_ref = lax.optimization_barrier(
            (picked, contrast.reshape(part_block, BAND, BAND * BAND), energy_ref)
        )
        part_send = jnp.broadcast_to(
            picked, (p_groups, r_groups // 2, part_block, piece)
        ).reshape(half, part_block, piece)
        mine = lax.all_to_all(part_send, "shard", 0, 0, tiled=True, axis_index_groups=groups)
        mine, refs_wide = lax.optimization_barrier((mine, refs_wide))
        other = lax.ppermute(mine, "shard", [(d, d ^ 1) for d in range(shards)])
        even = jnp.where(core == 0, mine, other)
        odd = jnp.where(core == 0, other, mine)
        part_got = jnp.stack([even, odd], axis=1).reshape(shards, part_block, piece)
    else:
        part_send = jnp.broadcast_to(
            pieces[source].reshape(p_groups, 1, part_block, piece),
            (p_groups, r_groups, part_block, piece),
        ).reshape(shards, part_block, piece)
        part_got = lax.all_to_all(part_send, "shard", 0, 0, tiled=True)
    spectra = part_got.transpose(1, 0, 2).reshape(part_block, -1)
    block_scores = score_block(spectra, contrast, energy_ref, refs_wide)

    targets = slot_target.reshape(shards, slots_here)
    in_block = (targets >= 0) & (targets // part_block == my_pblock)
    rows = block_scores[jnp.clip(targets - my_pblock * part_block, 0, part_block - 1)]
    back_send = jnp.where(in_block[:, :, None], rows, jnp.float32(0.0))
    back_got = lax.all_to_all(back_send, "shard", 0, 0, tiled=True)
    scores = (
        back_got.reshape(p_groups, r_groups, slots_here, ref_block)
        .sum(axis=0)
        .transpose(1, 0, 2)
        .reshape(slots_here, classes, rotations)
    )
    return (scores, jnp.max(scores, axis=2))


def solution(mesh):
    in_specs = (
        P(("groups", "shard"), None, None),
        P("groups"),
        P("groups"),
        P("groups"),
        P("groups", None, "shard"),
        P("groups", None),
    )
    out_specs = (P(("groups", "shard"), None, None), P(("groups", "shard"), None))
    return jax.shard_map(
        per_device, mesh=mesh, in_specs=in_specs, out_specs=out_specs, check_vma=False
    )
```

```python
import numpy as np
import jax
import jax.numpy as jnp
from jax import lax
from jax.experimental import pallas as pl
from jax.experimental.pallas import tpu as pltpu
from jax.sharding import PartitionSpec as P

BOX = 64
BAND = 32
SHIFTS = 8
PART_DEV = 1


def signed_band(band_size):
    return jnp.arange(band_size, dtype=jnp.int32) - band_size // 2


def table_pair(outer_loop_index, inner_index, box_edge):
    phase_index = outer_loop_index[:, None] * inner_index[None, :] % box_edge
    angles = phase_index.astype(jnp.float32) * (2.0 * jnp.pi / box_edge)
    return (jnp.cos(angles).astype(jnp.bfloat16), jnp.sin(angles).astype(jnp.bfloat16))


def spectral_product(form, left, right):
    return jnp.einsum(form, left, right, preferred_element_type=jnp.float32)


def forward_spectra(volumes):
    batch_size, box_edge = (volumes.shape[0], volumes.shape[1])
    cosine_forward, sine_forward = table_pair(
        signed_band(BAND), jnp.arange(box_edge, dtype=jnp.int32), box_edge
    )
    density_volume = volumes.astype(jnp.bfloat16)
    leading_real = spectral_product("qw,rwl->rql", cosine_forward, density_volume).astype(
        jnp.bfloat16
    )
    leading_imaginary = (-spectral_product("qw,rwl->rql", sine_forward, density_volume)).astype(
        jnp.bfloat16
    )
    leading_real = leading_real.reshape(batch_size, BAND, box_edge, box_edge)
    leading_imaginary = leading_imaginary.reshape(batch_size, BAND, box_edge, box_edge)
    second_real = (
        spectral_product("jy,nkyz->nkjz", cosine_forward, leading_real)
        + spectral_product("jy,nkyz->nkjz", sine_forward, leading_imaginary)
    ).astype(jnp.bfloat16)
    second_imag = (
        spectral_product("jy,nkyz->nkjz", cosine_forward, leading_imaginary)
        - spectral_product("jy,nkyz->nkjz", sine_forward, leading_real)
    ).astype(jnp.bfloat16)
    third_real = spectral_product("nkjz,lz->nkjl", second_real, cosine_forward) + spectral_product(
        "nkjz,lz->nkjl", second_imag, sine_forward
    )
    third_imag = spectral_product("nkjz,lz->nkjl", second_imag, cosine_forward) - spectral_product(
        "nkjz,lz->nkjl", second_real, sine_forward
    )
    spectrum = jnp.stack([third_real, third_imag], axis=1).astype(jnp.bfloat16)
    return spectrum.reshape(batch_size, 2, BAND * BAND * BAND)


def plane_table():
    k = np.arange(BAND) - BAND // 2
    t = np.arange(SHIFTS) - SHIFTS // 2
    phase = (
        t[None, None, :, None] * k[:, None, None, None]
        + t[None, None, None, :] * k[None, :, None, None]
    ) % BOX
    angles = phase.astype(np.float32) * np.float32(2.0 * np.pi / BOX)
    shape = (BAND * BAND, SHIFTS * SHIFTS)
    cosine = np.cos(angles).reshape(shape)
    sine = np.sin(angles).reshape(shape)
    upper = np.concatenate([cosine, sine], axis=1)
    lower = np.concatenate([-sine, cosine], axis=1)
    return jnp.asarray(np.concatenate([upper, lower], axis=0), dtype=jnp.bfloat16)


def shift_tables(n_ref):
    k = np.arange(BAND) - BAND // 2
    t = np.arange(SHIFTS) - SHIFTS // 2
    angles = ((t[:, None] * k[None, :]) % BOX).astype(np.float32) * np.float32(2.0 * np.pi / BOX)
    eye = np.eye(n_ref, dtype=np.float32)
    def rounded(x):
        return jnp.asarray(x, dtype=jnp.bfloat16).astype(jnp.float32)
    return rounded(np.kron(eye, np.cos(angles))), rounded(np.kron(eye, np.sin(angles)))


def correlation_kernel(s_ref, d_ref, r_ref, c_ref, t_ref, ec_ref, es_ref, o_ref, e_ref, p_s):
    n_ref = c_ref.shape[0]
    plane = BAND * BAND
    contrast = -jnp.sin(d_ref[0, 0:1, 0:1] * r_ref[...] + 0.07)
    s_real = s_ref[0, 0].astype(jnp.float32)
    s_imag = s_ref[0, 1].astype(jnp.float32)
    w_real = (contrast * s_real).astype(jnp.bfloat16).astype(jnp.float32)
    w_imag = (-(contrast * s_imag)).astype(jnp.bfloat16).astype(jnp.float32)
    for j in range(n_ref):
        c_real = c_ref[j, 0].astype(jnp.float32)
        c_imag = c_ref[j, 1].astype(jnp.float32)
        rows = slice(j * BAND, (j + 1) * BAND)
        p_s[rows, :plane] = (w_real * c_real - w_imag * c_imag).astype(jnp.bfloat16)
        p_s[rows, plane:] = (w_real * c_imag + w_imag * c_real).astype(jnp.bfloat16)
    planes = jnp.dot(p_s[...], t_ref[...], preferred_element_type=jnp.float32)
    first = jnp.dot(ec_ref[...], planes, preferred_element_type=jnp.float32,
                    precision=lax.Precision.HIGHEST)
    second = jnp.dot(es_ref[...], planes, preferred_element_type=jnp.float32,
                     precision=lax.Precision.HIGHEST)
    half = SHIFTS * SHIFTS
    correlation = first - pltpu.roll(second, half, 1)
    lane = lax.broadcasted_iota(jnp.int32, correlation.shape, 1)
    correlation = jnp.where(lane < half, correlation, -jnp.inf)
    per_row = jnp.max(correlation.reshape(n_ref, SHIFTS, 2 * half), axis=1)
    peak = jnp.max(per_row, axis=1, keepdims=True)
    o_ref[0] = jnp.broadcast_to(peak, (n_ref, 2 * half))
    power = jnp.sum(s_real * s_real + s_imag * s_imag, axis=0, keepdims=True)
    e_ref[0] = jnp.broadcast_to(jnp.sum(power, axis=1, keepdims=True), (8, 2 * half))


def radius_table():
    band_index = np.arange(BAND, dtype=np.float32) - BAND // 2
    radius = (
        band_index[:, None, None] ** 2
        + band_index[None, :, None] ** 2
        + band_index[None, None, :] ** 2
    ) / np.float32((BAND / 2) ** 2)
    return jnp.asarray(radius.reshape(BAND, BAND * BAND), dtype=jnp.float32)


def peak_correlations(spectra, chosen_defocus, refs):
    n_part = spectra.shape[0]
    n_ref = refs.shape[0]
    plane = BAND * BAND
    e_cos, e_sin = shift_tables(n_ref)
    width = 2 * SHIFTS * SHIFTS
    peak, energy = pl.pallas_call(
        correlation_kernel,
        grid=(n_part,),
        in_specs=[
            pl.BlockSpec((1, 2, BAND, plane), lambda i: (i, 0, 0, 0)),
            pl.BlockSpec((1, 8, width), lambda i: (i, 0, 0)),
            pl.BlockSpec((BAND, plane), lambda i: (0, 0)),
            pl.BlockSpec((n_ref, 2, BAND, plane), lambda i: (0, 0, 0, 0)),
            pl.BlockSpec((2 * plane, width), lambda i: (0, 0)),
            pl.BlockSpec((n_ref * SHIFTS, n_ref * BAND), lambda i: (0, 0)),
            pl.BlockSpec((n_ref * SHIFTS, n_ref * BAND), lambda i: (0, 0)),
        ],
        out_specs=[
            pl.BlockSpec((1, n_ref, width), lambda i: (i, 0, 0)),
            pl.BlockSpec((1, 8, width), lambda i: (i, 0, 0)),
        ],
        out_shape=[
            jax.ShapeDtypeStruct((n_part, n_ref, width), jnp.float32),
            jax.ShapeDtypeStruct((n_part, 8, width), jnp.float32),
        ],
        scratch_shapes=[pltpu.VMEM((n_ref * BAND, 2 * plane), jnp.bfloat16)],
        cost_estimate=pl.CostEstimate(
            flops=n_part * n_ref * (2 * BAND * 2 * plane * width + 8 * BAND * plane),
            transcendentals=0,
            bytes_accessed=n_part * 4 * BAND * plane + n_ref * 4 * BAND * plane,
        ),
    )(
        spectra,
        jnp.broadcast_to(chosen_defocus[:, None, None], (n_part, 8, width)),
        radius_table(),
        refs,
        plane_table(),
        e_cos,
        e_sin,
    )
    return peak[:, :, 0], energy[:, 0, 0]


def particle_contrast(bin_ids, defocus):
    band_index = signed_band(BAND).astype(jnp.float32)
    radius = (
        band_index[:, None, None] ** 2
        + band_index[None, :, None] ** 2
        + band_index[None, None, :] ** 2
    ).reshape(-1) / (BAND / 2) ** 2
    chosen_defocus = jnp.sum(
        jnp.where(
            bin_ids[:, None] == jnp.arange(defocus.shape[0], dtype=jnp.int32)[None, :],
            defocus[None, :],
            jnp.float32(0.0),
        ),
        axis=1,
    )
    return -jnp.sin(chosen_defocus[:, None] * radius[None, :] + 0.07), chosen_defocus


def reference_energy(contrast, refs):
    volume_size = BAND * BAND * BAND
    ref_real = refs[:, :volume_size].astype(jnp.float32)
    ref_imag = refs[:, volume_size:].astype(jnp.float32)
    magnitude = ref_real * ref_real + ref_imag * ref_imag
    return jnp.sum((contrast * contrast)[:, None, :] * magnitude[None, :, :], axis=2)


def score_block(spectra, chosen_defocus, energy_ref, refs):
    n_part = spectra.shape[0]
    n_ref = refs.shape[0]
    shape = (BAND, BAND * BAND)
    peak_value, energy_particle = peak_correlations(
        spectra.reshape(n_part, 2, *shape),
        chosen_defocus,
        refs,
    )
    score_scale = float(BAND) ** 1.5
    return score_scale * peak_value * lax.rsqrt(energy_particle[:, None] * energy_ref + 1e-06)


def ref_groups(shards, particles, refs):
    best = None
    for groups in range(1, shards + 1):
        if shards % groups or refs % groups or particles % (shards // groups):
            continue
        cost = particles * groups // shards + refs // groups
        if best is None or cost < best[0]:
            best = (cost, groups)
    return best[1]


def per_device(particles, slot_target, slot_defocus_level, defocus, ref_library, rotation_list):
    shards = lax.axis_size("shard")
    my_index = lax.axis_index("shard")
    slots_here = particles.shape[0]
    positions = PART_DEV * shards
    every_slot = slot_target.shape[0]
    classes, rotations = rotation_list.shape
    n_refs = classes * rotations
    r_groups = ref_groups(shards, positions, n_refs)
    p_groups = shards // r_groups
    part_block = positions // p_groups
    ref_block = n_refs // r_groups
    my_pblock = my_index // r_groups

    library = ref_library.shape[1]
    listed = (rotation_list[:, :, None] == jnp.arange(library, dtype=jnp.int32)).astype(jnp.bfloat16)
    chosen = jnp.einsum(
        "crl,clk->crk", listed, ref_library, preferred_element_type=jnp.float32
    ).astype(jnp.bfloat16)
    piece = chosen.shape[-1]
    ref_send = jnp.broadcast_to(
        chosen.reshape(1, r_groups, ref_block, piece), (p_groups, r_groups, ref_block, piece)
    ).reshape(shards, ref_block, piece)
    ref_got = lax.all_to_all(ref_send, "shard", 0, 0, tiled=True)
    flattened = forward_spectra(particles).reshape(slots_here, -1)
    source = (
        jnp.zeros((positions,), jnp.int32)
        .at[jnp.where(slot_target >= 0, slot_target, positions)]
        .set(jnp.arange(every_slot, dtype=jnp.int32), mode="drop")
    )
    my_sources = lax.dynamic_slice_in_dim(source, my_pblock * part_block, part_block, 0)
    flattened, ref_got, bin_ids = lax.optimization_barrier(
        (flattened, ref_got, slot_defocus_level[my_sources])
    )
    contrast, chosen_defocus = particle_contrast(bin_ids, defocus)
    refs = ref_got.transpose(1, 0, 2).reshape(ref_block, shards * piece)
    pieces = lax.all_to_all(flattened, "shard", split_axis=1, concat_axis=0, tiled=True)

    energy_ref = reference_energy(contrast, refs)
    refs_wide = refs.reshape(ref_block, 2, BAND, BAND * BAND)
    if r_groups % 2 == 0:
        half = shards // 2
        core = my_index % 2
        groups = [[2 * m + q for m in range(half)] for q in range(2)]
        picked = pieces[source].reshape(p_groups, 1, part_block, piece)
        picked, energy_ref = lax.optimization_barrier((picked, energy_ref))
        part_send = jnp.broadcast_to(
            picked, (p_groups, r_groups // 2, part_block, piece)
        ).reshape(half, part_block, piece)
        mine = lax.all_to_all(part_send, "shard", 0, 0, tiled=True, axis_index_groups=groups)
        mine, refs_wide = lax.optimization_barrier((mine, refs_wide))
        other = lax.ppermute(mine, "shard", [(d, d ^ 1) for d in range(shards)])
        even = jnp.where(core == 0, mine, other)
        odd = jnp.where(core == 0, other, mine)
        part_got = jnp.stack([even, odd], axis=1).reshape(shards, part_block, piece)
    else:
        part_send = jnp.broadcast_to(
            pieces[source].reshape(p_groups, 1, part_block, piece),
            (p_groups, r_groups, part_block, piece),
        ).reshape(shards, part_block, piece)
        part_got = lax.all_to_all(part_send, "shard", 0, 0, tiled=True)
    spectra = part_got.transpose(1, 0, 2).reshape(part_block, -1)
    block_scores = score_block(spectra, chosen_defocus, energy_ref, refs_wide)

    targets = slot_target.reshape(shards, slots_here)
    in_block = (targets >= 0) & (targets // part_block == my_pblock)
    rows = block_scores[jnp.clip(targets - my_pblock * part_block, 0, part_block - 1)]
    back_send = jnp.where(in_block[:, :, None], rows, jnp.float32(0.0))
    back_got = lax.all_to_all(back_send, "shard", 0, 0, tiled=True)
    scores = (
        back_got.reshape(p_groups, r_groups, slots_here, ref_block)
        .sum(axis=0)
        .transpose(1, 0, 2)
        .reshape(slots_here, classes, rotations)
    )
    return (scores, jnp.max(scores, axis=2))


def solution(mesh):
    in_specs = (
        P(("groups", "shard"), None, None),
        P("groups"),
        P("groups"),
        P("groups"),
        P("groups", None, "shard"),
        P("groups", None),
    )
    out_specs = (P(("groups", "shard"), None, None), P(("groups", "shard"), None))
    return jax.shard_map(
        per_device, mesh=mesh, in_specs=in_specs, out_specs=out_specs, check_vma=False
    )
```

```python
import numpy as np
import jax
import jax.numpy as jnp
from jax import lax
from jax.experimental import pallas as pl
from jax.experimental.pallas import tpu as pltpu
from jax.sharding import PartitionSpec as P

BOX = 64
BAND = 32
SHIFTS = 8
PART_DEV = 1


def signed_band(band_size):
    return jnp.arange(band_size, dtype=jnp.int32) - band_size // 2


def table_pair(outer_loop_index, inner_index, box_edge):
    phase_index = outer_loop_index[:, None] * inner_index[None, :] % box_edge
    angles = phase_index.astype(jnp.float32) * (2.0 * jnp.pi / box_edge)
    return (jnp.cos(angles).astype(jnp.bfloat16), jnp.sin(angles).astype(jnp.bfloat16))


def spectral_product(form, left, right):
    return jnp.einsum(form, left, right, preferred_element_type=jnp.float32)


def forward_spectra(volumes):
    batch_size, box_edge = (volumes.shape[0], volumes.shape[1])
    cosine_forward, sine_forward = table_pair(
        signed_band(BAND), jnp.arange(box_edge, dtype=jnp.int32), box_edge
    )
    density_volume = volumes.astype(jnp.bfloat16)
    leading_real = spectral_product("qw,rwl->rql", cosine_forward, density_volume).astype(
        jnp.bfloat16
    )
    leading_imaginary = (-spectral_product("qw,rwl->rql", sine_forward, density_volume)).astype(
        jnp.bfloat16
    )
    leading_real = leading_real.reshape(batch_size, BAND, box_edge, box_edge)
    leading_imaginary = leading_imaginary.reshape(batch_size, BAND, box_edge, box_edge)
    second_real = (
        spectral_product("jy,nkyz->nkjz", cosine_forward, leading_real)
        + spectral_product("jy,nkyz->nkjz", sine_forward, leading_imaginary)
    ).astype(jnp.bfloat16)
    second_imag = (
        spectral_product("jy,nkyz->nkjz", cosine_forward, leading_imaginary)
        - spectral_product("jy,nkyz->nkjz", sine_forward, leading_real)
    ).astype(jnp.bfloat16)
    third_real = spectral_product("nkjz,lz->nkjl", second_real, cosine_forward) + spectral_product(
        "nkjz,lz->nkjl", second_imag, sine_forward
    )
    third_imag = spectral_product("nkjz,lz->nkjl", second_imag, cosine_forward) - spectral_product(
        "nkjz,lz->nkjl", second_real, sine_forward
    )
    spectrum = jnp.stack([third_real, third_imag], axis=1).astype(jnp.bfloat16)
    return spectrum.reshape(batch_size, 2, BAND * BAND * BAND)


def plane_table():
    k = np.arange(BAND) - BAND // 2
    t = np.arange(SHIFTS) - SHIFTS // 2
    phase = (
        t[None, None, :, None] * k[:, None, None, None]
        + t[None, None, None, :] * k[None, :, None, None]
    ) % BOX
    angles = phase.astype(np.float32) * np.float32(2.0 * np.pi / BOX)
    shape = (BAND * BAND, SHIFTS * SHIFTS)
    cosine = np.cos(angles).reshape(shape)
    sine = np.sin(angles).reshape(shape)
    upper = np.concatenate([cosine, sine], axis=1)
    lower = np.concatenate([-sine, cosine], axis=1)
    return jnp.asarray(np.concatenate([upper, lower], axis=0), dtype=jnp.bfloat16)


def shift_tables(n_ref):
    k = np.arange(BAND) - BAND // 2
    t = np.arange(SHIFTS) - SHIFTS // 2
    angles = ((t[:, None] * k[None, :]) % BOX).astype(np.float32) * np.float32(2.0 * np.pi / BOX)
    eye = np.eye(n_ref, dtype=np.float32)
    def rounded(x):
        return jnp.asarray(x, dtype=jnp.bfloat16).astype(jnp.float32)
    return rounded(np.kron(eye, np.cos(angles))), rounded(np.kron(eye, np.sin(angles)))


def correlation_kernel(s_ref, g_ref, c_ref, t_ref, ec_ref, es_ref, r_ref, o_ref, p_s):
    n_ref = c_ref.shape[0]
    plane = BAND * BAND
    contrast = g_ref[0]
    s_real = s_ref[0, 0].astype(jnp.float32)
    s_imag = s_ref[0, 1].astype(jnp.float32)
    w_real = (contrast * s_real).astype(jnp.bfloat16).astype(jnp.float32)
    w_imag = (-(contrast * s_imag)).astype(jnp.bfloat16).astype(jnp.float32)
    for j in range(n_ref):
        c_real = c_ref[j, 0]
        c_imag = c_ref[j, 1]
        rows = slice(j * BAND, (j + 1) * BAND)
        p_s[rows, :plane] = (w_real * c_real - w_imag * c_imag).astype(jnp.bfloat16)
        p_s[rows, plane:] = (w_real * c_imag + w_imag * c_real).astype(jnp.bfloat16)
    planes = jnp.dot(p_s[...], t_ref[...], preferred_element_type=jnp.float32)
    first = jnp.dot(ec_ref[...], planes, preferred_element_type=jnp.float32,
                    precision=lax.Precision.HIGHEST)
    second = jnp.dot(es_ref[...], planes, preferred_element_type=jnp.float32,
                     precision=lax.Precision.HIGHEST)
    half = SHIFTS * SHIFTS
    correlation = first - pltpu.roll(second, half, 1)
    lane = lax.broadcasted_iota(jnp.int32, correlation.shape, 1)
    correlation = jnp.where(lane < half, correlation, -jnp.inf)
    per_row = jnp.max(correlation.reshape(n_ref, SHIFTS, 2 * half), axis=1)
    peak = jnp.max(per_row, axis=1, keepdims=True)
    power = jnp.sum(s_real * s_real + s_imag * s_imag, axis=0, keepdims=True)
    energy_particle = jnp.sum(power, axis=1, keepdims=True)
    energy_ref = r_ref[0][:, 0:1]
    score = float(BAND) ** 1.5 * peak * lax.rsqrt(energy_particle * energy_ref + 1e-06)
    o_ref[0] = jnp.broadcast_to(score, (n_ref, 2 * half))


def peak_correlations(spectra, contrast, refs, energy_ref):
    n_part = spectra.shape[0]
    n_ref = refs.shape[0]
    plane = BAND * BAND
    e_cos, e_sin = shift_tables(n_ref)
    width = 2 * SHIFTS * SHIFTS
    scores = pl.pallas_call(
        correlation_kernel,
        grid=(n_part,),
        in_specs=[
            pl.BlockSpec((1, 2, BAND, plane), lambda i: (i, 0, 0, 0)),
            pl.BlockSpec((1, BAND, plane), lambda i: (i, 0, 0)),
            pl.BlockSpec((n_ref, 2, BAND, plane), lambda i: (0, 0, 0, 0)),
            pl.BlockSpec((2 * plane, width), lambda i: (0, 0)),
            pl.BlockSpec((n_ref * SHIFTS, n_ref * BAND), lambda i: (0, 0)),
            pl.BlockSpec((n_ref * SHIFTS, n_ref * BAND), lambda i: (0, 0)),
            pl.BlockSpec((1, n_ref, width), lambda i: (i, 0, 0)),
        ],
        out_specs=pl.BlockSpec((1, n_ref, width), lambda i: (i, 0, 0)),
        out_shape=jax.ShapeDtypeStruct((n_part, n_ref, width), jnp.float32),
        scratch_shapes=[pltpu.VMEM((n_ref * BAND, 2 * plane), jnp.bfloat16)],
        cost_estimate=pl.CostEstimate(
            flops=n_part * n_ref * (2 * BAND * 2 * plane * width + 8 * BAND * plane),
            transcendentals=0,
            bytes_accessed=n_part * 8 * BAND * plane + n_ref * 8 * BAND * plane,
        ),
    )(
        spectra, contrast, refs, plane_table(), e_cos, e_sin,
        jnp.broadcast_to(energy_ref[:, :, None], (n_part, n_ref, width)),
    )
    return scores[:, :, 0]


def particle_contrast(bin_ids, defocus):
    band_index = signed_band(BAND).astype(jnp.float32)
    radius = (
        band_index[:, None, None] ** 2
        + band_index[None, :, None] ** 2
        + band_index[None, None, :] ** 2
    ).reshape(-1) / (BAND / 2) ** 2
    chosen_defocus = jnp.sum(
        jnp.where(
            bin_ids[:, None] == jnp.arange(defocus.shape[0], dtype=jnp.int32)[None, :],
            defocus[None, :],
            jnp.float32(0.0),
        ),
        axis=1,
    )
    return -jnp.sin(chosen_defocus[:, None] * radius[None, :] + 0.07)


def reference_energy(contrast, refs):
    volume_size = BAND * BAND * BAND
    ref_real = refs[:, :volume_size].astype(jnp.float32)
    ref_imag = refs[:, volume_size:].astype(jnp.float32)
    magnitude = ref_real * ref_real + ref_imag * ref_imag
    return jnp.sum((contrast * contrast)[:, None, :] * magnitude[None, :, :], axis=2)


def score_block(spectra, contrast, energy_ref, refs):
    n_part = spectra.shape[0]
    n_ref = refs.shape[0]
    shape = (BAND, BAND * BAND)
    return peak_correlations(
        spectra.reshape(n_part, 2, *shape),
        contrast.reshape(n_part, *shape),
        refs,
        energy_ref,
    )


def ref_groups(shards, particles, refs):
    best = None
    for groups in range(1, shards + 1):
        if shards % groups or refs % groups or particles % (shards // groups):
            continue
        cost = particles * groups // shards + refs // groups
        if best is None or cost < best[0]:
            best = (cost, groups)
    return best[1]


def per_device(particles, slot_target, slot_defocus_level, defocus, ref_library, rotation_list):
    shards = lax.axis_size("shard")
    my_index = lax.axis_index("shard")
    slots_here = particles.shape[0]
    positions = PART_DEV * shards
    every_slot = slot_target.shape[0]
    classes, rotations = rotation_list.shape
    n_refs = classes * rotations
    r_groups = ref_groups(shards, positions, n_refs)
    p_groups = shards // r_groups
    part_block = positions // p_groups
    ref_block = n_refs // r_groups
    my_pblock = my_index // r_groups

    library = ref_library.shape[1]
    listed = (rotation_list[:, :, None] == jnp.arange(library, dtype=jnp.int32)).astype(jnp.bfloat16)
    chosen = jnp.einsum(
        "crl,clk->crk", listed, ref_library, preferred_element_type=jnp.float32
    ).astype(jnp.bfloat16)
    piece = chosen.shape[-1]
    ref_send = jnp.broadcast_to(
        chosen.reshape(1, r_groups, ref_block, piece), (p_groups, r_groups, ref_block, piece)
    ).reshape(shards, ref_block, piece)
    ref_got = lax.all_to_all(ref_send, "shard", 0, 0, tiled=True)
    flattened = forward_spectra(particles).reshape(slots_here, -1)
    source = (
        jnp.zeros((positions,), jnp.int32)
        .at[jnp.where(slot_target >= 0, slot_target, positions)]
        .set(jnp.arange(every_slot, dtype=jnp.int32), mode="drop")
    )
    my_sources = lax.dynamic_slice_in_dim(source, my_pblock * part_block, part_block, 0)
    flattened, ref_got, bin_ids = lax.optimization_barrier(
        (flattened, ref_got, slot_defocus_level[my_sources])
    )
    contrast = lax.optimization_barrier(particle_contrast(bin_ids, defocus))
    refs = ref_got.transpose(1, 0, 2).reshape(ref_block, shards * piece)
    pieces = lax.all_to_all(flattened, "shard", split_axis=1, concat_axis=0, tiled=True)

    energy_ref = reference_energy(contrast, refs)
    refs_wide = refs.reshape(ref_block, 2, BAND, BAND * BAND).astype(jnp.float32)
    if r_groups % 2 == 0:
        half = shards // 2
        core = my_index % 2
        groups = [[2 * m + q for m in range(half)] for q in range(2)]
        picked = pieces[source].reshape(p_groups, 1, part_block, piece)
        picked, contrast, energy_ref = lax.optimization_barrier(
            (picked, contrast.reshape(part_block, BAND, BAND * BAND), energy_ref)
        )
        part_send = jnp.broadcast_to(
            picked, (p_groups, r_groups // 2, part_block, piece)
        ).reshape(half, part_block, piece)
        mine = lax.all_to_all(part_send, "shard", 0, 0, tiled=True, axis_index_groups=groups)
        mine, refs_wide = lax.optimization_barrier((mine, refs_wide))
        other = lax.ppermute(mine, "shard", [(d, d ^ 1) for d in range(shards)])
        even = jnp.where(core == 0, mine, other)
        odd = jnp.where(core == 0, other, mine)
        part_got = jnp.stack([even, odd], axis=1).reshape(shards, part_block, piece)
    else:
        part_send = jnp.broadcast_to(
            pieces[source].reshape(p_groups, 1, part_block, piece),
            (p_groups, r_groups, part_block, piece),
        ).reshape(shards, part_block, piece)
        part_got = lax.all_to_all(part_send, "shard", 0, 0, tiled=True)
    spectra = part_got.transpose(1, 0, 2).reshape(part_block, -1)
    block_scores = score_block(spectra, contrast, energy_ref, refs_wide)

    targets = slot_target.reshape(shards, slots_here)
    in_block = (targets >= 0) & (targets // part_block == my_pblock)
    rows = block_scores[jnp.clip(targets - my_pblock * part_block, 0, part_block - 1)]
    back_send = jnp.where(in_block[:, :, None], rows, jnp.float32(0.0))
    back_got = lax.all_to_all(back_send, "shard", 0, 0, tiled=True)
    scores = (
        back_got.reshape(p_groups, r_groups, slots_here, ref_block)
        .sum(axis=0)
        .transpose(1, 0, 2)
        .reshape(slots_here, classes, rotations)
    )
    return (scores, jnp.max(scores, axis=2))


def solution(mesh):
    in_specs = (
        P(("groups", "shard"), None, None),
        P("groups"),
        P("groups"),
        P("groups"),
        P("groups", None, "shard"),
        P("groups", None),
    )
    out_specs = (P(("groups", "shard"), None, None), P(("groups", "shard"), None))
    return jax.shard_map(
        per_device, mesh=mesh, in_specs=in_specs, out_specs=out_specs, check_vma=False
    )
```

```python
import numpy as np
import jax
import jax.numpy as jnp
from jax import lax
from jax.experimental import pallas as pl
from jax.experimental.pallas import tpu as pltpu
from jax.sharding import PartitionSpec as P

BOX = 64
BAND = 32
SHIFTS = 8
PART_DEV = 1


def signed_band(band_size):
    return jnp.arange(band_size, dtype=jnp.int32) - band_size // 2


def table_pair(outer_loop_index, inner_index, box_edge):
    phase_index = outer_loop_index[:, None] * inner_index[None, :] % box_edge
    angles = phase_index.astype(jnp.float32) * (2.0 * jnp.pi / box_edge)
    return (jnp.cos(angles).astype(jnp.bfloat16), jnp.sin(angles).astype(jnp.bfloat16))


def spectral_product(form, left, right):
    return jnp.einsum(form, left, right, preferred_element_type=jnp.float32)


def forward_spectra(volumes):
    batch_size, box_edge = (volumes.shape[0], volumes.shape[1])
    cosine_forward, sine_forward = table_pair(
        signed_band(BAND), jnp.arange(box_edge, dtype=jnp.int32), box_edge
    )
    density_volume = volumes.astype(jnp.bfloat16)
    leading_real = spectral_product("qw,rwl->rql", cosine_forward, density_volume).astype(
        jnp.bfloat16
    )
    leading_imaginary = (-spectral_product("qw,rwl->rql", sine_forward, density_volume)).astype(
        jnp.bfloat16
    )
    leading_real = leading_real.reshape(batch_size, BAND, box_edge, box_edge)
    leading_imaginary = leading_imaginary.reshape(batch_size, BAND, box_edge, box_edge)
    second_real = (
        spectral_product("jy,nkyz->nkjz", cosine_forward, leading_real)
        + spectral_product("jy,nkyz->nkjz", sine_forward, leading_imaginary)
    ).astype(jnp.bfloat16)
    second_imag = (
        spectral_product("jy,nkyz->nkjz", cosine_forward, leading_imaginary)
        - spectral_product("jy,nkyz->nkjz", sine_forward, leading_real)
    ).astype(jnp.bfloat16)
    third_real = spectral_product("nkjz,lz->nkjl", second_real, cosine_forward) + spectral_product(
        "nkjz,lz->nkjl", second_imag, sine_forward
    )
    third_imag = spectral_product("nkjz,lz->nkjl", second_imag, cosine_forward) - spectral_product(
        "nkjz,lz->nkjl", second_real, sine_forward
    )
    spectrum = jnp.stack([third_real, third_imag], axis=1).astype(jnp.bfloat16)
    return spectrum.reshape(batch_size, 2, BAND * BAND * BAND)


def plane_table():
    k = np.arange(BAND) - BAND // 2
    t = np.arange(SHIFTS) - SHIFTS // 2
    phase = (
        t[None, None, :, None] * k[:, None, None, None]
        + t[None, None, None, :] * k[None, :, None, None]
    ) % BOX
    angles = phase.astype(np.float32) * np.float32(2.0 * np.pi / BOX)
    shape = (BAND * BAND, SHIFTS * SHIFTS)
    cosine = np.cos(angles).reshape(shape)
    sine = np.sin(angles).reshape(shape)
    upper = np.concatenate([cosine, sine], axis=1)
    lower = np.concatenate([-sine, cosine], axis=1)
    return jnp.asarray(np.concatenate([upper, lower], axis=0), dtype=jnp.bfloat16)


def shift_tables(n_ref):
    k = np.arange(BAND) - BAND // 2
    t = np.arange(SHIFTS) - SHIFTS // 2
    angles = ((t[:, None] * k[None, :]) % BOX).astype(np.float32) * np.float32(2.0 * np.pi / BOX)
    eye = np.eye(n_ref, dtype=np.float32)
    def rounded(x):
        return jnp.asarray(x, dtype=jnp.bfloat16).astype(jnp.float32)
    return rounded(np.kron(eye, np.cos(angles))), rounded(np.kron(eye, np.sin(angles)))


def correlation_kernel(s_ref, g_ref, c_ref, t_ref, ec_ref, es_ref, r_ref, o_ref, p_s):
    n_ref = c_ref.shape[0]
    plane = BAND * BAND
    contrast = g_ref[0]
    s_real = s_ref[0, 0].astype(jnp.float32)
    s_imag = s_ref[0, 1].astype(jnp.float32)
    w_real = (contrast * s_real).astype(jnp.bfloat16).astype(jnp.float32)
    w_imag = (-(contrast * s_imag)).astype(jnp.bfloat16).astype(jnp.float32)
    for j in range(n_ref):
        c_real = c_ref[j, 0]
        c_imag = c_ref[j, 1]
        rows = slice(j * BAND, (j + 1) * BAND)
        p_s[rows, :plane] = (w_real * c_real - w_imag * c_imag).astype(jnp.bfloat16)
        p_s[rows, plane:] = (w_real * c_imag + w_imag * c_real).astype(jnp.bfloat16)
    planes = jnp.dot(p_s[...], t_ref[...], preferred_element_type=jnp.float32)
    first = jnp.dot(ec_ref[...], planes, preferred_element_type=jnp.float32,
                    precision=lax.Precision.HIGHEST)
    second = jnp.dot(es_ref[...], planes, preferred_element_type=jnp.float32,
                     precision=lax.Precision.HIGHEST)
    half = SHIFTS * SHIFTS
    correlation = first - pltpu.roll(second, half, 1)
    lane = lax.broadcasted_iota(jnp.int32, correlation.shape, 1)
    correlation = jnp.where(lane < half, correlation, -jnp.inf)
    per_row = jnp.max(correlation.reshape(n_ref, SHIFTS, 2 * half), axis=1)
    peak = jnp.max(per_row, axis=1, keepdims=True)
    power = jnp.sum(s_real * s_real + s_imag * s_imag, axis=0, keepdims=True)
    energy_particle = jnp.sum(power, axis=1, keepdims=True)
    energy_ref = r_ref[0][:, 0:1]
    score = float(BAND) ** 1.5 * peak * lax.rsqrt(energy_particle * energy_ref + 1e-06)
    o_ref[0] = jnp.broadcast_to(score, (n_ref, 2 * half))


def peak_correlations(spectra, contrast, refs, energy_ref):
    n_part = spectra.shape[0]
    n_ref = refs.shape[0]
    plane = BAND * BAND
    e_cos, e_sin = shift_tables(n_ref)
    width = 2 * SHIFTS * SHIFTS
    scores = pl.pallas_call(
        correlation_kernel,
        grid=(n_part,),
        in_specs=[
            pl.BlockSpec((1, 2, BAND, plane), lambda i: (i, 0, 0, 0)),
            pl.BlockSpec((1, BAND, plane), lambda i: (i, 0, 0)),
            pl.BlockSpec((n_ref, 2, BAND, plane), lambda i: (0, 0, 0, 0)),
            pl.BlockSpec((2 * plane, width), lambda i: (0, 0)),
            pl.BlockSpec((n_ref * SHIFTS, n_ref * BAND), lambda i: (0, 0)),
            pl.BlockSpec((n_ref * SHIFTS, n_ref * BAND), lambda i: (0, 0)),
            pl.BlockSpec((1, n_ref, width), lambda i: (i, 0, 0)),
        ],
        out_specs=pl.BlockSpec((1, n_ref, width), lambda i: (i, 0, 0)),
        out_shape=jax.ShapeDtypeStruct((n_part, n_ref, width), jnp.float32),
        scratch_shapes=[pltpu.VMEM((n_ref * BAND, 2 * plane), jnp.bfloat16)],
        cost_estimate=pl.CostEstimate(
            flops=n_part * n_ref * (2 * BAND * 2 * plane * width + 8 * BAND * plane),
            transcendentals=0,
            bytes_accessed=n_part * 8 * BAND * plane + n_ref * 8 * BAND * plane,
        ),
    )(
        spectra, contrast, refs, plane_table(), e_cos, e_sin,
        energy_ref,
    )
    return scores


def particle_contrast(bin_ids, defocus):
    band_index = signed_band(BAND).astype(jnp.float32)
    radius = (
        band_index[:, None, None] ** 2
        + band_index[None, :, None] ** 2
        + band_index[None, None, :] ** 2
    ).reshape(-1) / (BAND / 2) ** 2
    chosen_defocus = jnp.sum(
        jnp.where(
            bin_ids[:, None] == jnp.arange(defocus.shape[0], dtype=jnp.int32)[None, :],
            defocus[None, :],
            jnp.float32(0.0),
        ),
        axis=1,
    )
    return -jnp.sin(chosen_defocus[:, None] * radius[None, :] + 0.07)


def reference_energy(contrast, refs):
    volume_size = BAND * BAND * BAND
    ref_real = refs[:, :volume_size].astype(jnp.float32)
    ref_imag = refs[:, volume_size:].astype(jnp.float32)
    magnitude = ref_real * ref_real + ref_imag * ref_imag
    energy = jnp.sum((contrast * contrast)[:, None, :] * magnitude[None, :, :], axis=2)
    return jnp.broadcast_to(energy[:, :, None], energy.shape + (2 * SHIFTS * SHIFTS,))


def score_block(spectra, contrast, energy_ref, refs):
    n_part = spectra.shape[0]
    n_ref = refs.shape[0]
    shape = (BAND, BAND * BAND)
    return peak_correlations(
        spectra.reshape(n_part, 2, *shape),
        contrast.reshape(n_part, *shape),
        refs,
        energy_ref,
    )


def ref_groups(shards, particles, refs):
    best = None
    for groups in range(1, shards + 1):
        if shards % groups or refs % groups or particles % (shards // groups):
            continue
        cost = particles * groups // shards + refs // groups
        if best is None or cost < best[0]:
            best = (cost, groups)
    return best[1]


def per_device(particles, slot_target, slot_defocus_level, defocus, ref_library, rotation_list):
    shards = lax.axis_size("shard")
    my_index = lax.axis_index("shard")
    slots_here = particles.shape[0]
    positions = PART_DEV * shards
    every_slot = slot_target.shape[0]
    classes, rotations = rotation_list.shape
    n_refs = classes * rotations
    r_groups = ref_groups(shards, positions, n_refs)
    p_groups = shards // r_groups
    part_block = positions // p_groups
    ref_block = n_refs // r_groups
    my_pblock = my_index // r_groups

    library = ref_library.shape[1]
    listed = (rotation_list[:, :, None] == jnp.arange(library, dtype=jnp.int32)).astype(jnp.bfloat16)
    chosen = jnp.einsum(
        "crl,clk->crk", listed, ref_library, preferred_element_type=jnp.float32
    ).astype(jnp.bfloat16)
    piece = chosen.shape[-1]
    ref_send = jnp.broadcast_to(
        chosen.reshape(1, r_groups, ref_block, piece), (p_groups, r_groups, ref_block, piece)
    ).reshape(shards, ref_block, piece)
    ref_got = lax.all_to_all(ref_send, "shard", 0, 0, tiled=True)
    flattened = forward_spectra(particles).reshape(slots_here, -1)
    source = (
        jnp.zeros((positions,), jnp.int32)
        .at[jnp.where(slot_target >= 0, slot_target, positions)]
        .set(jnp.arange(every_slot, dtype=jnp.int32), mode="drop")
    )
    my_sources = lax.dynamic_slice_in_dim(source, my_pblock * part_block, part_block, 0)
    flattened, ref_got, bin_ids = lax.optimization_barrier(
        (flattened, ref_got, slot_defocus_level[my_sources])
    )
    contrast = lax.optimization_barrier(particle_contrast(bin_ids, defocus))
    refs = ref_got.transpose(1, 0, 2).reshape(ref_block, shards * piece)
    pieces = lax.all_to_all(flattened, "shard", split_axis=1, concat_axis=0, tiled=True)

    energy_ref = reference_energy(contrast, refs)
    refs_wide = refs.reshape(ref_block, 2, BAND, BAND * BAND).astype(jnp.float32)
    if r_groups % 2 == 0:
        half = shards // 2
        core = my_index % 2
        groups = [[2 * m + q for m in range(half)] for q in range(2)]
        picked = pieces[source].reshape(p_groups, 1, part_block, piece)
        picked, contrast, energy_ref = lax.optimization_barrier(
            (picked, contrast.reshape(part_block, BAND, BAND * BAND), energy_ref)
        )
        part_send = jnp.broadcast_to(
            picked, (p_groups, r_groups // 2, part_block, piece)
        ).reshape(half, part_block, piece)
        mine = lax.all_to_all(part_send, "shard", 0, 0, tiled=True, axis_index_groups=groups)
        mine, refs_wide = lax.optimization_barrier((mine, refs_wide))
        other = lax.ppermute(mine, "shard", [(d, d ^ 1) for d in range(shards)])
        even = jnp.where(core == 0, mine, other)
        odd = jnp.where(core == 0, other, mine)
        part_got = jnp.stack([even, odd], axis=1).reshape(shards, part_block, piece)
    else:
        part_send = jnp.broadcast_to(
            pieces[source].reshape(p_groups, 1, part_block, piece),
            (p_groups, r_groups, part_block, piece),
        ).reshape(shards, part_block, piece)
        part_got = lax.all_to_all(part_send, "shard", 0, 0, tiled=True)
    spectra = part_got.transpose(1, 0, 2).reshape(part_block, -1)
    block_scores = score_block(spectra, contrast, energy_ref, refs_wide)

    targets = slot_target.reshape(shards, slots_here)
    in_block = (targets >= 0) & (targets // part_block == my_pblock)
    rows = block_scores[jnp.clip(targets - my_pblock * part_block, 0, part_block - 1)][..., 0]
    back_send = jnp.where(in_block[:, :, None], rows, jnp.float32(0.0))
    back_got = lax.all_to_all(back_send, "shard", 0, 0, tiled=True)
    scores = (
        back_got.reshape(p_groups, r_groups, slots_here, ref_block)
        .sum(axis=0)
        .transpose(1, 0, 2)
        .reshape(slots_here, classes, rotations)
    )
    return (scores, jnp.max(scores, axis=2))


def solution(mesh):
    in_specs = (
        P(("groups", "shard"), None, None),
        P("groups"),
        P("groups"),
        P("groups"),
        P("groups", None, "shard"),
        P("groups", None),
    )
    out_specs = (P(("groups", "shard"), None, None), P(("groups", "shard"), None))
    return jax.shard_map(
        per_device, mesh=mesh, in_specs=in_specs, out_specs=out_specs, check_vma=False
    )
```

```python
import numpy as np
import jax
import jax.numpy as jnp
from jax import lax
from jax.experimental import pallas as pl
from jax.experimental.pallas import tpu as pltpu
from jax.sharding import PartitionSpec as P

BOX = 64
BAND = 32
SHIFTS = 8
PART_DEV = 1


def signed_band(band_size):
    return jnp.arange(band_size, dtype=jnp.int32) - band_size // 2


def table_pair(outer_loop_index, inner_index, box_edge):
    phase_index = outer_loop_index[:, None] * inner_index[None, :] % box_edge
    angles = phase_index.astype(jnp.float32) * (2.0 * jnp.pi / box_edge)
    return (jnp.cos(angles).astype(jnp.bfloat16), jnp.sin(angles).astype(jnp.bfloat16))


def spectral_product(form, left, right):
    return jnp.einsum(form, left, right, preferred_element_type=jnp.float32)


def forward_spectra(volumes):
    batch_size, box_edge = (volumes.shape[0], volumes.shape[1])
    cosine_forward, sine_forward = table_pair(
        signed_band(BAND), jnp.arange(box_edge, dtype=jnp.int32), box_edge
    )
    density_volume = volumes.astype(jnp.bfloat16)
    leading_real = spectral_product("qw,rwl->rql", cosine_forward, density_volume).astype(
        jnp.bfloat16
    )
    leading_imaginary = (-spectral_product("qw,rwl->rql", sine_forward, density_volume)).astype(
        jnp.bfloat16
    )
    leading_real = leading_real.reshape(batch_size, BAND, box_edge, box_edge)
    leading_imaginary = leading_imaginary.reshape(batch_size, BAND, box_edge, box_edge)
    second_real = (
        spectral_product("jy,nkyz->nkjz", cosine_forward, leading_real)
        + spectral_product("jy,nkyz->nkjz", sine_forward, leading_imaginary)
    ).astype(jnp.bfloat16)
    second_imag = (
        spectral_product("jy,nkyz->nkjz", cosine_forward, leading_imaginary)
        - spectral_product("jy,nkyz->nkjz", sine_forward, leading_real)
    ).astype(jnp.bfloat16)
    third_real = spectral_product("nkjz,lz->nkjl", second_real, cosine_forward) + spectral_product(
        "nkjz,lz->nkjl", second_imag, sine_forward
    )
    third_imag = spectral_product("nkjz,lz->nkjl", second_imag, cosine_forward) - spectral_product(
        "nkjz,lz->nkjl", second_real, sine_forward
    )
    spectrum = jnp.stack([third_real, third_imag], axis=1).astype(jnp.bfloat16)
    return spectrum.reshape(batch_size, 2, BAND * BAND * BAND)


def plane_table():
    k = np.arange(BAND) - BAND // 2
    t = np.arange(SHIFTS) - SHIFTS // 2
    phase = (
        t[None, None, :, None] * k[:, None, None, None]
        + t[None, None, None, :] * k[None, :, None, None]
    ) % BOX
    angles = phase.astype(np.float32) * np.float32(2.0 * np.pi / BOX)
    shape = (BAND * BAND, SHIFTS * SHIFTS)
    cosine = np.cos(angles).reshape(shape)
    sine = np.sin(angles).reshape(shape)
    upper = np.concatenate([cosine, sine], axis=1)
    lower = np.concatenate([-sine, cosine], axis=1)
    return jnp.asarray(np.concatenate([upper, lower], axis=0), dtype=jnp.bfloat16)


def shift_tables(n_ref):
    k = np.arange(BAND) - BAND // 2
    t = np.arange(SHIFTS) - SHIFTS // 2
    angles = ((t[:, None] * k[None, :]) % BOX).astype(np.float32) * np.float32(2.0 * np.pi / BOX)
    eye = np.eye(n_ref, dtype=np.float32)
    def rounded(x):
        return jnp.asarray(x, dtype=jnp.bfloat16).astype(jnp.float32)
    return rounded(np.kron(eye, np.cos(angles))), rounded(np.kron(eye, np.sin(angles)))


def correlation_kernel(s_ref, g_ref, c_ref, t_ref, ec_ref, es_ref, r_ref, o_ref, p_s):
    n_ref = c_ref.shape[0]
    plane = BAND * BAND
    contrast = g_ref[0]
    s_real = s_ref[0, 0].astype(jnp.float32)
    s_imag = s_ref[0, 1].astype(jnp.float32)
    w_real = (contrast * s_real).astype(jnp.bfloat16).astype(jnp.float32)
    w_imag = (-(contrast * s_imag)).astype(jnp.bfloat16).astype(jnp.float32)
    for j in range(n_ref):
        c_real = c_ref[j, 0]
        c_imag = c_ref[j, 1]
        rows = slice(j * BAND, (j + 1) * BAND)
        p_s[rows, :plane] = (w_real * c_real - w_imag * c_imag).astype(jnp.bfloat16)
        p_s[rows, plane:] = (w_real * c_imag + w_imag * c_real).astype(jnp.bfloat16)
    planes = jnp.dot(p_s[...], t_ref[...], preferred_element_type=jnp.float32)
    first = jnp.dot(ec_ref[...], planes, preferred_element_type=jnp.float32,
                    precision=lax.Precision.HIGHEST)
    second = jnp.dot(es_ref[...], planes, preferred_element_type=jnp.float32,
                     precision=lax.Precision.HIGHEST)
    half = SHIFTS * SHIFTS
    correlation = first - pltpu.roll(second, half, 1)
    lane = lax.broadcasted_iota(jnp.int32, correlation.shape, 1)
    correlation = jnp.where(lane < half, correlation, -jnp.inf)
    per_row = jnp.max(correlation.reshape(n_ref, SHIFTS, 2 * half), axis=1)
    peak = jnp.max(per_row, axis=1, keepdims=True)
    power = jnp.sum(s_real * s_real + s_imag * s_imag, axis=0, keepdims=True)
    energy_particle = jnp.sum(power, axis=1, keepdims=True)
    energy_ref = r_ref[0][:, 0:1]
    score = float(BAND) ** 1.5 * peak * lax.rsqrt(energy_particle * energy_ref + 1e-06)
    o_ref[0] = jnp.broadcast_to(score, (n_ref, 2 * half))


def peak_correlations(spectra, contrast, refs, energy_ref):
    n_part = spectra.shape[0]
    n_ref = refs.shape[0]
    plane = BAND * BAND
    e_cos, e_sin = shift_tables(n_ref)
    width = 2 * SHIFTS * SHIFTS
    scores = pl.pallas_call(
        correlation_kernel,
        grid=(n_part,),
        in_specs=[
            pl.BlockSpec((1, 2, BAND, plane), lambda i: (i, 0, 0, 0)),
            pl.BlockSpec((1, BAND, plane), lambda i: (i, 0, 0)),
            pl.BlockSpec((n_ref, 2, BAND, plane), lambda i: (0, 0, 0, 0)),
            pl.BlockSpec((2 * plane, width), lambda i: (0, 0)),
            pl.BlockSpec((n_ref * SHIFTS, n_ref * BAND), lambda i: (0, 0)),
            pl.BlockSpec((n_ref * SHIFTS, n_ref * BAND), lambda i: (0, 0)),
            pl.BlockSpec((1, n_ref, width), lambda i: (i, 0, 0)),
        ],
        out_specs=pl.BlockSpec((1, n_ref, width), lambda i: (i, 0, 0)),
        out_shape=jax.ShapeDtypeStruct((n_part, n_ref, width), jnp.float32),
        scratch_shapes=[pltpu.VMEM((n_ref * BAND, 2 * plane), jnp.bfloat16)],
        cost_estimate=pl.CostEstimate(
            flops=n_part * n_ref * (2 * BAND * 2 * plane * width + 8 * BAND * plane),
            transcendentals=0,
            bytes_accessed=n_part * 8 * BAND * plane + n_ref * 8 * BAND * plane,
        ),
    )(
        spectra, contrast, refs, plane_table(), e_cos, e_sin,
        energy_ref,
    )
    return scores


def particle_contrast(bin_ids, defocus):
    band_index = signed_band(BAND).astype(jnp.float32)
    radius = (
        band_index[:, None, None] ** 2
        + band_index[None, :, None] ** 2
        + band_index[None, None, :] ** 2
    ).reshape(-1) / (BAND / 2) ** 2
    chosen_defocus = jnp.sum(
        jnp.where(
            bin_ids[:, None] == jnp.arange(defocus.shape[0], dtype=jnp.int32)[None, :],
            defocus[None, :],
            jnp.float32(0.0),
        ),
        axis=1,
    )
    return -jnp.sin(chosen_defocus[:, None] * radius[None, :] + 0.07)


def reference_energy(contrast, refs):
    volume_size = BAND * BAND * BAND
    ref_real = refs[:, :volume_size].astype(jnp.float32)
    ref_imag = refs[:, volume_size:].astype(jnp.float32)
    magnitude = ref_real * ref_real + ref_imag * ref_imag
    energy = jnp.sum((contrast * contrast)[:, None, :] * magnitude[None, :, :], axis=2)
    return jnp.broadcast_to(energy[:, :, None], energy.shape + (2 * SHIFTS * SHIFTS,))


def score_block(spectra, contrast, energy_ref, refs):
    n_part = spectra.shape[0]
    n_ref = refs.shape[0]
    shape = (BAND, BAND * BAND)
    return peak_correlations(
        spectra.reshape(n_part, 2, *shape),
        contrast.reshape(n_part, *shape),
        refs,
        energy_ref,
    )


def ref_groups(shards, particles, refs):
    best = None
    for groups in range(1, shards + 1):
        if shards % groups or refs % groups or particles % (shards // groups):
            continue
        cost = particles * groups // shards + refs // groups
        if best is None or cost < best[0]:
            best = (cost, groups)
    return best[1]


def per_device(particles, slot_target, slot_defocus_level, defocus, ref_library, rotation_list):
    shards = lax.axis_size("shard")
    my_index = lax.axis_index("shard")
    slots_here = particles.shape[0]
    positions = PART_DEV * shards
    every_slot = slot_target.shape[0]
    classes, rotations = rotation_list.shape
    n_refs = classes * rotations
    r_groups = ref_groups(shards, positions, n_refs)
    p_groups = shards // r_groups
    part_block = positions // p_groups
    ref_block = n_refs // r_groups
    my_pblock = my_index // r_groups

    library = ref_library.shape[1]
    listed = (rotation_list[:, :, None] == jnp.arange(library, dtype=jnp.int32)).astype(jnp.bfloat16)
    chosen = jnp.einsum(
        "crl,clk->crk", listed, ref_library, preferred_element_type=jnp.float32
    ).astype(jnp.bfloat16)
    piece = chosen.shape[-1]
    ref_send = jnp.broadcast_to(
        chosen.reshape(1, r_groups, ref_block, piece), (p_groups, r_groups, ref_block, piece)
    ).reshape(shards, ref_block, piece)
    ref_got = lax.all_to_all(ref_send, "shard", 0, 0, tiled=True)
    flattened = forward_spectra(particles).reshape(slots_here, -1)
    source = (
        jnp.zeros((positions,), jnp.int32)
        .at[jnp.where(slot_target >= 0, slot_target, positions)]
        .set(jnp.arange(every_slot, dtype=jnp.int32), mode="drop")
    )
    my_sources = lax.dynamic_slice_in_dim(source, my_pblock * part_block, part_block, 0)
    flattened, ref_got, bin_ids = lax.optimization_barrier(
        (flattened, ref_got, slot_defocus_level[my_sources])
    )
    contrast = lax.optimization_barrier(particle_contrast(bin_ids, defocus))
    refs = ref_got.transpose(1, 0, 2).reshape(ref_block, shards * piece)
    if r_groups % 2 == 0:
        half = shards // 2
        core = my_index % 2
        groups = [[2 * m + q for m in range(half)] for q in range(2)]
        partner_slots = lax.ppermute(flattened, "shard", [(d, d ^ 1) for d in range(shards)])
        chip_slots = jnp.concatenate(
            [
                jnp.where(core == 0, flattened, partner_slots),
                jnp.where(core == 0, partner_slots, flattened),
            ],
            axis=0,
        ).reshape(2 * slots_here, half, 2, piece)
        first_send = lax.dynamic_index_in_dim(chip_slots, core, axis=2, keepdims=False)
        first_got = lax.all_to_all(
            first_send.transpose(1, 0, 2), "shard", 0, 0, tiled=True, axis_index_groups=groups
        )
        pieces = first_got.reshape(shards * slots_here, piece)
    else:
        pieces = lax.all_to_all(flattened, "shard", split_axis=1, concat_axis=0, tiled=True)

    energy_ref = reference_energy(contrast, refs)
    refs_wide = refs.reshape(ref_block, 2, BAND, BAND * BAND).astype(jnp.float32)
    if r_groups % 2 == 0:
        half = shards // 2
        core = my_index % 2
        groups = [[2 * m + q for m in range(half)] for q in range(2)]
        picked = pieces[source].reshape(p_groups, 1, part_block, piece)
        picked, contrast, energy_ref = lax.optimization_barrier(
            (picked, contrast.reshape(part_block, BAND, BAND * BAND), energy_ref)
        )
        part_send = jnp.broadcast_to(
            picked, (p_groups, r_groups // 2, part_block, piece)
        ).reshape(half, part_block, piece)
        mine = lax.all_to_all(part_send, "shard", 0, 0, tiled=True, axis_index_groups=groups)
        mine, refs_wide = lax.optimization_barrier((mine, refs_wide))
        other = lax.ppermute(mine, "shard", [(d, d ^ 1) for d in range(shards)])
        even = jnp.where(core == 0, mine, other)
        odd = jnp.where(core == 0, other, mine)
        part_got = jnp.stack([even, odd], axis=1).reshape(shards, part_block, piece)
    else:
        part_send = jnp.broadcast_to(
            pieces[source].reshape(p_groups, 1, part_block, piece),
            (p_groups, r_groups, part_block, piece),
        ).reshape(shards, part_block, piece)
        part_got = lax.all_to_all(part_send, "shard", 0, 0, tiled=True)
    spectra = part_got.transpose(1, 0, 2).reshape(part_block, -1)
    block_scores = score_block(spectra, contrast, energy_ref, refs_wide)

    targets = slot_target.reshape(shards, slots_here)
    in_block = (targets >= 0) & (targets // part_block == my_pblock)
    rows = block_scores[jnp.clip(targets - my_pblock * part_block, 0, part_block - 1)][..., 0]
    back_send = jnp.where(in_block[:, :, None], rows, jnp.float32(0.0))
    back_got = lax.all_to_all(back_send, "shard", 0, 0, tiled=True)
    scores = (
        back_got.reshape(p_groups, r_groups, slots_here, ref_block)
        .sum(axis=0)
        .transpose(1, 0, 2)
        .reshape(slots_here, classes, rotations)
    )
    return (scores, jnp.max(scores, axis=2))


def solution(mesh):
    in_specs = (
        P(("groups", "shard"), None, None),
        P("groups"),
        P("groups"),
        P("groups"),
        P("groups", None, "shard"),
        P("groups", None),
    )
    out_specs = (P(("groups", "shard"), None, None), P(("groups", "shard"), None))
    return jax.shard_map(
        per_device, mesh=mesh, in_specs=in_specs, out_specs=out_specs, check_vma=False
    )
```

```python
import numpy as np
import jax
import jax.numpy as jnp
from jax import lax
from jax.experimental import pallas as pl
from jax.experimental.pallas import tpu as pltpu
from jax.sharding import PartitionSpec as P

BOX = 64
BAND = 32
SHIFTS = 8
PART_DEV = 1


def signed_band(band_size):
    return jnp.arange(band_size, dtype=jnp.int32) - band_size // 2


def table_pair(outer_loop_index, inner_index, box_edge):
    phase_index = outer_loop_index[:, None] * inner_index[None, :] % box_edge
    angles = phase_index.astype(jnp.float32) * (2.0 * jnp.pi / box_edge)
    return (jnp.cos(angles).astype(jnp.bfloat16), jnp.sin(angles).astype(jnp.bfloat16))


def spectral_product(form, left, right):
    return jnp.einsum(form, left, right, preferred_element_type=jnp.float32)


def forward_spectra(volumes):
    batch_size, box_edge = (volumes.shape[0], volumes.shape[1])
    cosine_forward, sine_forward = table_pair(
        signed_band(BAND), jnp.arange(box_edge, dtype=jnp.int32), box_edge
    )
    density_volume = volumes.astype(jnp.bfloat16)
    leading_real = spectral_product("qw,rwl->rql", cosine_forward, density_volume).astype(
        jnp.bfloat16
    )
    leading_imaginary = (-spectral_product("qw,rwl->rql", sine_forward, density_volume)).astype(
        jnp.bfloat16
    )
    leading_real = leading_real.reshape(batch_size, BAND, box_edge, box_edge)
    leading_imaginary = leading_imaginary.reshape(batch_size, BAND, box_edge, box_edge)
    second_real = (
        spectral_product("jy,nkyz->nkjz", cosine_forward, leading_real)
        + spectral_product("jy,nkyz->nkjz", sine_forward, leading_imaginary)
    ).astype(jnp.bfloat16)
    second_imag = (
        spectral_product("jy,nkyz->nkjz", cosine_forward, leading_imaginary)
        - spectral_product("jy,nkyz->nkjz", sine_forward, leading_real)
    ).astype(jnp.bfloat16)
    third_real = spectral_product("nkjz,lz->nkjl", second_real, cosine_forward) + spectral_product(
        "nkjz,lz->nkjl", second_imag, sine_forward
    )
    third_imag = spectral_product("nkjz,lz->nkjl", second_imag, cosine_forward) - spectral_product(
        "nkjz,lz->nkjl", second_real, sine_forward
    )
    spectrum = jnp.stack([third_real, third_imag], axis=1).astype(jnp.bfloat16)
    return spectrum.reshape(batch_size, 2, BAND * BAND * BAND)


def plane_table():
    k = np.arange(BAND) - BAND // 2
    t = np.arange(SHIFTS) - SHIFTS // 2
    phase = (
        t[None, None, :, None] * k[:, None, None, None]
        + t[None, None, None, :] * k[None, :, None, None]
    ) % BOX
    angles = phase.astype(np.float32) * np.float32(2.0 * np.pi / BOX)
    shape = (BAND * BAND, SHIFTS * SHIFTS)
    cosine = np.cos(angles).reshape(shape)
    sine = np.sin(angles).reshape(shape)
    upper = np.concatenate([cosine, sine], axis=1)
    lower = np.concatenate([-sine, cosine], axis=1)
    return jnp.asarray(np.concatenate([upper, lower], axis=0), dtype=jnp.bfloat16)


def shift_tables(n_ref):
    k = np.arange(BAND) - BAND // 2
    t = np.arange(SHIFTS) - SHIFTS // 2
    angles = ((t[:, None] * k[None, :]) % BOX).astype(np.float32) * np.float32(2.0 * np.pi / BOX)
    eye = np.eye(n_ref, dtype=np.float32)
    def rounded(x):
        return jnp.asarray(x, dtype=jnp.bfloat16).astype(jnp.float32)
    return rounded(np.kron(eye, np.cos(angles))), rounded(np.kron(eye, np.sin(angles)))


def correlation_kernel(s_ref, g_ref, c_ref, t_ref, ec_ref, es_ref, r_ref, o_ref, p_s):
    n_ref = c_ref.shape[0]
    plane = BAND * BAND
    contrast = g_ref[0]
    s_real = s_ref[0, 0].astype(jnp.float32)
    s_imag = s_ref[0, 1].astype(jnp.float32)
    w_real = (contrast * s_real).astype(jnp.bfloat16).astype(jnp.float32)
    w_imag = (-(contrast * s_imag)).astype(jnp.bfloat16).astype(jnp.float32)
    for j in range(n_ref):
        c_real = c_ref[j, 0]
        c_imag = c_ref[j, 1]
        rows = slice(j * BAND, (j + 1) * BAND)
        p_s[rows, :plane] = (w_real * c_real - w_imag * c_imag).astype(jnp.bfloat16)
        p_s[rows, plane:] = (w_real * c_imag + w_imag * c_real).astype(jnp.bfloat16)
    planes = jnp.dot(p_s[...], t_ref[...], preferred_element_type=jnp.float32)
    first = jnp.dot(ec_ref[...], planes, preferred_element_type=jnp.float32,
                    precision=lax.Precision.HIGHEST)
    second = jnp.dot(es_ref[...], planes, preferred_element_type=jnp.float32,
                     precision=lax.Precision.HIGHEST)
    half = SHIFTS * SHIFTS
    correlation = first - pltpu.roll(second, half, 1)
    lane = lax.broadcasted_iota(jnp.int32, correlation.shape, 1)
    correlation = jnp.where(lane < half, correlation, -jnp.inf)
    per_row = jnp.max(correlation.reshape(n_ref, SHIFTS, 2 * half), axis=1)
    peak = jnp.max(per_row, axis=1, keepdims=True)
    power = jnp.sum(s_real * s_real + s_imag * s_imag, axis=0, keepdims=True)
    energy_particle = jnp.sum(power, axis=1, keepdims=True)
    energy_ref = r_ref[0]
    score = float(BAND) ** 1.5 * peak * lax.rsqrt(energy_particle * energy_ref + 1e-06)
    o_ref[0] = jnp.broadcast_to(score, (n_ref, 2 * half))


def peak_correlations(spectra, contrast, refs, energy_ref):
    n_part = spectra.shape[0]
    n_ref = refs.shape[0]
    plane = BAND * BAND
    e_cos, e_sin = shift_tables(n_ref)
    width = 2 * SHIFTS * SHIFTS
    scores = pl.pallas_call(
        correlation_kernel,
        grid=(n_part,),
        in_specs=[
            pl.BlockSpec((1, 2, BAND, plane), lambda i: (i, 0, 0, 0)),
            pl.BlockSpec((1, BAND, plane), lambda i: (i, 0, 0)),
            pl.BlockSpec((n_ref, 2, BAND, plane), lambda i: (0, 0, 0, 0)),
            pl.BlockSpec((2 * plane, width), lambda i: (0, 0)),
            pl.BlockSpec((n_ref * SHIFTS, n_ref * BAND), lambda i: (0, 0)),
            pl.BlockSpec((n_ref * SHIFTS, n_ref * BAND), lambda i: (0, 0)),
            pl.BlockSpec((1, n_ref, 1), lambda i: (i, 0, 0)),
        ],
        out_specs=pl.BlockSpec((1, n_ref, width), lambda i: (i, 0, 0)),
        out_shape=jax.ShapeDtypeStruct((n_part, n_ref, width), jnp.float32),
        scratch_shapes=[pltpu.VMEM((n_ref * BAND, 2 * plane), jnp.bfloat16)],
        cost_estimate=pl.CostEstimate(
            flops=n_part * n_ref * (2 * BAND * 2 * plane * width + 8 * BAND * plane),
            transcendentals=0,
            bytes_accessed=n_part * 8 * BAND * plane + n_ref * 8 * BAND * plane,
        ),
    )(
        spectra, contrast, refs, plane_table(), e_cos, e_sin,
        energy_ref,
    )
    return scores


def particle_contrast(bin_ids, defocus):
    band_index = signed_band(BAND).astype(jnp.float32)
    radius = (
        band_index[:, None, None] ** 2
        + band_index[None, :, None] ** 2
        + band_index[None, None, :] ** 2
    ).reshape(-1) / (BAND / 2) ** 2
    chosen_defocus = jnp.sum(
        jnp.where(
            bin_ids[:, None] == jnp.arange(defocus.shape[0], dtype=jnp.int32)[None, :],
            defocus[None, :],
            jnp.float32(0.0),
        ),
        axis=1,
    )
    return -jnp.sin(chosen_defocus[:, None] * radius[None, :] + 0.07)


def reference_energy(contrast, refs):
    volume_size = BAND * BAND * BAND
    ref_real = refs[:, :volume_size].astype(jnp.float32)
    ref_imag = refs[:, volume_size:].astype(jnp.float32)
    magnitude = ref_real * ref_real + ref_imag * ref_imag
    energy = jnp.sum((contrast * contrast)[:, None, :] * magnitude[None, :, :], axis=2)
    return energy[:, :, None]


def score_block(spectra, contrast, energy_ref, refs):
    n_part = spectra.shape[0]
    n_ref = refs.shape[0]
    shape = (BAND, BAND * BAND)
    return peak_correlations(
        spectra.reshape(n_part, 2, *shape),
        contrast.reshape(n_part, *shape),
        refs,
        energy_ref,
    )


def ref_groups(shards, particles, refs):
    best = None
    for groups in range(1, shards + 1):
        if shards % groups or refs % groups or particles % (shards // groups):
            continue
        cost = particles * groups // shards + refs // groups
        if best is None or cost < best[0]:
            best = (cost, groups)
    return best[1]


def per_device(particles, slot_target, slot_defocus_level, defocus, ref_library, rotation_list):
    shards = lax.axis_size("shard")
    my_index = lax.axis_index("shard")
    slots_here = particles.shape[0]
    positions = PART_DEV * shards
    every_slot = slot_target.shape[0]
    classes, rotations = rotation_list.shape
    n_refs = classes * rotations
    r_groups = ref_groups(shards, positions, n_refs)
    p_groups = shards // r_groups
    part_block = positions // p_groups
    ref_block = n_refs // r_groups
    my_pblock = my_index // r_groups

    library = ref_library.shape[1]
    listed = (rotation_list[:, :, None] == jnp.arange(library, dtype=jnp.int32)).astype(jnp.bfloat16)
    chosen = jnp.einsum(
        "crl,clk->crk", listed, ref_library, preferred_element_type=jnp.float32
    ).astype(jnp.bfloat16)
    piece = chosen.shape[-1]
    ref_send = jnp.broadcast_to(
        chosen.reshape(1, r_groups, ref_block, piece), (p_groups, r_groups, ref_block, piece)
    ).reshape(shards, ref_block, piece)
    ref_got = lax.all_to_all(ref_send, "shard", 0, 0, tiled=True)
    flattened = forward_spectra(particles).reshape(slots_here, -1)
    source = (
        jnp.zeros((positions,), jnp.int32)
        .at[jnp.where(slot_target >= 0, slot_target, positions)]
        .set(jnp.arange(every_slot, dtype=jnp.int32), mode="drop")
    )
    my_sources = lax.dynamic_slice_in_dim(source, my_pblock * part_block, part_block, 0)
    flattened, ref_got, bin_ids = lax.optimization_barrier(
        (flattened, ref_got, slot_defocus_level[my_sources])
    )
    contrast = lax.optimization_barrier(particle_contrast(bin_ids, defocus))
    refs = ref_got.transpose(1, 0, 2).reshape(ref_block, shards * piece)
    pieces = lax.all_to_all(flattened, "shard", split_axis=1, concat_axis=0, tiled=True)

    energy_ref = reference_energy(contrast, refs)
    refs_wide = refs.reshape(ref_block, 2, BAND, BAND * BAND).astype(jnp.float32)
    if r_groups % 2 == 0:
        half = shards // 2
        core = my_index % 2
        groups = [[2 * m + q for m in range(half)] for q in range(2)]
        chosen_rows = jnp.broadcast_to(
            source.reshape(p_groups, 1, part_block), (p_groups, r_groups // 2, part_block)
        ).reshape(half, part_block)
        chosen_rows, contrast, energy_ref = lax.optimization_barrier(
            (chosen_rows, contrast.reshape(part_block, BAND, BAND * BAND), energy_ref)
        )
        picked = pieces[chosen_rows]
        mine = lax.all_to_all(picked, "shard", 0, 0, tiled=True, axis_index_groups=groups)
        mine, refs_wide = lax.optimization_barrier((mine, refs_wide))
        other = lax.ppermute(mine, "shard", [(d, d ^ 1) for d in range(shards)])
        even = jnp.where(core == 0, mine, other)
        odd = jnp.where(core == 0, other, mine)
        part_got = jnp.stack([even, odd], axis=1).reshape(shards, part_block, piece)
    else:
        part_send = jnp.broadcast_to(
            pieces[source].reshape(p_groups, 1, part_block, piece),
            (p_groups, r_groups, part_block, piece),
        ).reshape(shards, part_block, piece)
        part_got = lax.all_to_all(part_send, "shard", 0, 0, tiled=True)
    spectra = part_got.transpose(1, 0, 2).reshape(part_block, -1)
    block_scores = score_block(spectra, contrast, energy_ref, refs_wide)

    targets = slot_target.reshape(shards, slots_here)
    in_block = (targets >= 0) & (targets // part_block == my_pblock)
    rows = block_scores[jnp.clip(targets - my_pblock * part_block, 0, part_block - 1)][..., 0]
    back_send = jnp.where(in_block[:, :, None], rows, jnp.float32(0.0))
    back_got = lax.all_to_all(back_send, "shard", 0, 0, tiled=True)
    scores = (
        back_got.reshape(p_groups, r_groups, slots_here, ref_block)
        .sum(axis=0)
        .transpose(1, 0, 2)
        .reshape(slots_here, classes, rotations)
    )
    return (scores, jnp.max(scores, axis=2))


def solution(mesh):
    in_specs = (
        P(("groups", "shard"), None, None),
        P("groups"),
        P("groups"),
        P("groups"),
        P("groups", None, "shard"),
        P("groups", None),
    )
    out_specs = (P(("groups", "shard"), None, None), P(("groups", "shard"), None))
    return jax.shard_map(
        per_device, mesh=mesh, in_specs=in_specs, out_specs=out_specs, check_vma=False
    )
```

```python
import numpy as np
import jax
import jax.numpy as jnp
from jax import lax
from jax.experimental import pallas as pl
from jax.experimental.pallas import tpu as pltpu
from jax.sharding import PartitionSpec as P

BOX = 64
BAND = 32
SHIFTS = 8
PART_DEV = 1


def signed_band(band_size):
    return jnp.arange(band_size, dtype=jnp.int32) - band_size // 2


def table_pair(outer_loop_index, inner_index, box_edge):
    phase_index = outer_loop_index[:, None] * inner_index[None, :] % box_edge
    angles = phase_index.astype(jnp.float32) * (2.0 * jnp.pi / box_edge)
    return (jnp.cos(angles).astype(jnp.bfloat16), jnp.sin(angles).astype(jnp.bfloat16))


def spectral_product(form, left, right):
    return jnp.einsum(form, left, right, preferred_element_type=jnp.float32)


def forward_spectra(volumes):
    batch_size, box_edge = (volumes.shape[0], volumes.shape[1])
    cosine_forward, sine_forward = table_pair(
        signed_band(BAND), jnp.arange(box_edge, dtype=jnp.int32), box_edge
    )
    density_volume = volumes.astype(jnp.bfloat16)
    leading_real = spectral_product("qw,rwl->rql", cosine_forward, density_volume).astype(
        jnp.bfloat16
    )
    leading_imaginary = (-spectral_product("qw,rwl->rql", sine_forward, density_volume)).astype(
        jnp.bfloat16
    )
    leading_real = leading_real.reshape(batch_size, BAND, box_edge, box_edge)
    leading_imaginary = leading_imaginary.reshape(batch_size, BAND, box_edge, box_edge)
    second_real = (
        spectral_product("jy,nkyz->nkjz", cosine_forward, leading_real)
        + spectral_product("jy,nkyz->nkjz", sine_forward, leading_imaginary)
    ).astype(jnp.bfloat16)
    second_imag = (
        spectral_product("jy,nkyz->nkjz", cosine_forward, leading_imaginary)
        - spectral_product("jy,nkyz->nkjz", sine_forward, leading_real)
    ).astype(jnp.bfloat16)
    third_real = spectral_product("nkjz,lz->nkjl", second_real, cosine_forward) + spectral_product(
        "nkjz,lz->nkjl", second_imag, sine_forward
    )
    third_imag = spectral_product("nkjz,lz->nkjl", second_imag, cosine_forward) - spectral_product(
        "nkjz,lz->nkjl", second_real, sine_forward
    )
    spectrum = jnp.stack([third_real, third_imag], axis=1).astype(jnp.bfloat16)
    return spectrum.reshape(batch_size, 2, BAND * BAND * BAND)


def plane_table():
    k = np.arange(BAND) - BAND // 2
    t = np.arange(SHIFTS) - SHIFTS // 2
    phase = (
        t[None, None, :, None] * k[:, None, None, None]
        + t[None, None, None, :] * k[None, :, None, None]
    ) % BOX
    angles = phase.astype(np.float32) * np.float32(2.0 * np.pi / BOX)
    shape = (BAND * BAND, SHIFTS * SHIFTS)
    cosine = np.cos(angles).reshape(shape)
    sine = np.sin(angles).reshape(shape)
    upper = np.concatenate([cosine, sine], axis=1)
    lower = np.concatenate([-sine, cosine], axis=1)
    return jnp.asarray(np.concatenate([upper, lower], axis=0), dtype=jnp.bfloat16)


def shift_tables(n_ref):
    k = np.arange(BAND) - BAND // 2
    t = np.arange(SHIFTS) - SHIFTS // 2
    angles = ((t[:, None] * k[None, :]) % BOX).astype(np.float32) * np.float32(2.0 * np.pi / BOX)
    eye = np.eye(n_ref, dtype=np.float32)
    def rounded(x):
        return jnp.asarray(x, dtype=jnp.bfloat16).astype(jnp.float32)
    return rounded(np.kron(eye, np.cos(angles))), rounded(np.kron(eye, np.sin(angles)))


def correlation_kernel(s_ref, g_ref, c_ref, t_ref, ec_ref, es_ref, r_ref, o_ref, p_s):
    n_ref = c_ref.shape[0]
    plane = BAND * BAND
    contrast = g_ref[0]
    s_real = s_ref[0, 0].astype(jnp.float32)
    s_imag = s_ref[0, 1].astype(jnp.float32)
    w_real = (contrast * s_real).astype(jnp.bfloat16).astype(jnp.float32)
    w_imag = (-(contrast * s_imag)).astype(jnp.bfloat16).astype(jnp.float32)
    for j in range(n_ref):
        c_real = c_ref[j, 0]
        c_imag = c_ref[j, 1]
        rows = slice(j * BAND, (j + 1) * BAND)
        p_s[rows, :plane] = (w_real * c_real - w_imag * c_imag).astype(jnp.bfloat16)
        p_s[rows, plane:] = (w_real * c_imag + w_imag * c_real).astype(jnp.bfloat16)
    planes = jnp.dot(p_s[...], t_ref[...], preferred_element_type=jnp.float32)
    first = jnp.dot(ec_ref[...], planes, preferred_element_type=jnp.float32,
                    precision=lax.Precision.HIGHEST)
    second = jnp.dot(es_ref[...], planes, preferred_element_type=jnp.float32,
                     precision=lax.Precision.HIGHEST)
    half = SHIFTS * SHIFTS
    correlation = first - pltpu.roll(second, half, 1)
    lane = lax.broadcasted_iota(jnp.int32, correlation.shape, 1)
    correlation = jnp.where(lane < half, correlation, -jnp.inf)
    per_row = jnp.max(correlation.reshape(n_ref, SHIFTS, 2 * half), axis=1)
    peak = jnp.max(per_row, axis=1, keepdims=True)
    power = jnp.sum(s_real * s_real + s_imag * s_imag, axis=0, keepdims=True)
    energy_particle = jnp.sum(power, axis=1, keepdims=True)
    energy_ref = r_ref[0][:, 0:1]
    score = float(BAND) ** 1.5 * peak * lax.rsqrt(energy_particle * energy_ref + 1e-06)
    o_ref[0] = jnp.broadcast_to(score, (n_ref, 2 * half))


def peak_correlations(spectra, contrast, refs, energy_ref):
    n_part = spectra.shape[0]
    n_ref = refs.shape[0]
    plane = BAND * BAND
    e_cos, e_sin = shift_tables(n_ref)
    width = 2 * SHIFTS * SHIFTS
    scores = pl.pallas_call(
        correlation_kernel,
        grid=(n_part,),
        in_specs=[
            pl.BlockSpec((1, 2, BAND, plane), lambda i: (i, 0, 0, 0)),
            pl.BlockSpec((1, BAND, plane), lambda i: (i, 0, 0)),
            pl.BlockSpec((n_ref, 2, BAND, plane), lambda i: (0, 0, 0, 0)),
            pl.BlockSpec((2 * plane, width), lambda i: (0, 0)),
            pl.BlockSpec((n_ref * SHIFTS, n_ref * BAND), lambda i: (0, 0)),
            pl.BlockSpec((n_ref * SHIFTS, n_ref * BAND), lambda i: (0, 0)),
            pl.BlockSpec((1, n_ref, width), lambda i: (i, 0, 0)),
        ],
        out_specs=pl.BlockSpec((1, n_ref, width), lambda i: (i, 0, 0)),
        out_shape=jax.ShapeDtypeStruct((n_part, n_ref, width), jnp.float32),
        scratch_shapes=[pltpu.VMEM((n_ref * BAND, 2 * plane), jnp.bfloat16)],
        cost_estimate=pl.CostEstimate(
            flops=n_part * n_ref * (2 * BAND * 2 * plane * width + 8 * BAND * plane),
            transcendentals=0,
            bytes_accessed=n_part * 8 * BAND * plane + n_ref * 8 * BAND * plane,
        ),
    )(
        spectra, contrast, refs, plane_table(), e_cos, e_sin,
        energy_ref,
    )
    return scores


def particle_contrast(bin_ids, defocus):
    band_index = signed_band(BAND).astype(jnp.float32)
    radius = (
        band_index[:, None, None] ** 2
        + band_index[None, :, None] ** 2
        + band_index[None, None, :] ** 2
    ).reshape(-1) / (BAND / 2) ** 2
    chosen_defocus = jnp.sum(
        jnp.where(
            bin_ids[:, None] == jnp.arange(defocus.shape[0], dtype=jnp.int32)[None, :],
            defocus[None, :],
            jnp.float32(0.0),
        ),
        axis=1,
    )
    return -jnp.sin(chosen_defocus[:, None] * radius[None, :] + 0.07)


def reference_energy(contrast, refs):
    volume_size = BAND * BAND * BAND
    ref_real = refs[:, :volume_size].astype(jnp.float32)
    ref_imag = refs[:, volume_size:].astype(jnp.float32)
    magnitude = ref_real * ref_real + ref_imag * ref_imag
    energy = jnp.sum((contrast * contrast)[:, None, :] * magnitude[None, :, :], axis=2)
    return jnp.broadcast_to(energy[:, :, None], energy.shape + (2 * SHIFTS * SHIFTS,))


def score_block(spectra, contrast, energy_ref, refs):
    n_part = spectra.shape[0]
    n_ref = refs.shape[0]
    shape = (BAND, BAND * BAND)
    return peak_correlations(
        spectra.reshape(n_part, 2, *shape),
        contrast.reshape(n_part, *shape),
        refs,
        energy_ref,
    )


def ref_groups(shards, particles, refs):
    best = None
    for groups in range(1, shards + 1):
        if shards % groups or refs % groups or particles % (shards // groups):
            continue
        cost = particles * groups // shards + refs // groups
        if best is None or cost < best[0]:
            best = (cost, groups)
    return best[1]


def per_device(particles, slot_target, slot_defocus_level, defocus, ref_library, rotation_list):
    shards = lax.axis_size("shard")
    my_index = lax.axis_index("shard")
    slots_here = particles.shape[0]
    positions = PART_DEV * shards
    every_slot = slot_target.shape[0]
    classes, rotations = rotation_list.shape
    n_refs = classes * rotations
    r_groups = ref_groups(shards, positions, n_refs)
    p_groups = shards // r_groups
    part_block = positions // p_groups
    ref_block = n_refs // r_groups
    my_pblock = my_index // r_groups

    library = ref_library.shape[1]
    listed = (rotation_list[:, :, None] == jnp.arange(library, dtype=jnp.int32)).astype(jnp.bfloat16)
    listed = jnp.broadcast_to(listed[None], (p_groups,) + listed.shape)
    chosen = jnp.einsum(
        "gcrl,clk->gcrk", listed, ref_library, preferred_element_type=jnp.float32
    ).astype(jnp.bfloat16)
    piece = chosen.shape[-1]
    ref_send = chosen.reshape(shards, ref_block, piece)
    ref_got = lax.all_to_all(ref_send, "shard", 0, 0, tiled=True)
    flattened = forward_spectra(particles).reshape(slots_here, -1)
    source = (
        jnp.zeros((positions,), jnp.int32)
        .at[jnp.where(slot_target >= 0, slot_target, positions)]
        .set(jnp.arange(every_slot, dtype=jnp.int32), mode="drop")
    )
    my_sources = lax.dynamic_slice_in_dim(source, my_pblock * part_block, part_block, 0)
    flattened, ref_got, bin_ids = lax.optimization_barrier(
        (flattened, ref_got, slot_defocus_level[my_sources])
    )
    contrast = lax.optimization_barrier(particle_contrast(bin_ids, defocus))
    refs = ref_got.transpose(1, 0, 2).reshape(ref_block, shards * piece)
    pieces = lax.all_to_all(flattened, "shard", split_axis=1, concat_axis=0, tiled=True)

    energy_ref = reference_energy(contrast, refs)
    refs_wide = refs.reshape(ref_block, 2, BAND, BAND * BAND).astype(jnp.float32)
    if r_groups % 2 == 0:
        half = shards // 2
        core = my_index % 2
        groups = [[2 * m + q for m in range(half)] for q in range(2)]
        picked = pieces[source].reshape(p_groups, 1, part_block, piece)
        picked, contrast, energy_ref = lax.optimization_barrier(
            (picked, contrast.reshape(part_block, BAND, BAND * BAND), energy_ref)
        )
        part_send = jnp.broadcast_to(
            picked, (p_groups, r_groups // 2, part_block, piece)
        ).reshape(half, part_block, piece)
        mine = lax.all_to_all(part_send, "shard", 0, 0, tiled=True, axis_index_groups=groups)
        mine, refs_wide = lax.optimization_barrier((mine, refs_wide))
        other = lax.ppermute(mine, "shard", [(d, d ^ 1) for d in range(shards)])
        even = jnp.where(core == 0, mine, other)
        odd = jnp.where(core == 0, other, mine)
        part_got = jnp.stack([even, odd], axis=1).reshape(shards, part_block, piece)
    else:
        part_send = jnp.broadcast_to(
            pieces[source].reshape(p_groups, 1, part_block, piece),
            (p_groups, r_groups, part_block, piece),
        ).reshape(shards, part_block, piece)
        part_got = lax.all_to_all(part_send, "shard", 0, 0, tiled=True)
    spectra = part_got.transpose(1, 0, 2).reshape(part_block, -1)
    block_scores = score_block(spectra, contrast, energy_ref, refs_wide)

    targets = slot_target.reshape(shards, slots_here)
    in_block = (targets >= 0) & (targets // part_block == my_pblock)
    rows = block_scores[jnp.clip(targets - my_pblock * part_block, 0, part_block - 1)][..., 0]
    back_send = jnp.where(in_block[:, :, None], rows, jnp.float32(0.0))
    back_got = lax.all_to_all(back_send, "shard", 0, 0, tiled=True)
    scores = (
        back_got.reshape(p_groups, r_groups, slots_here, ref_block)
        .sum(axis=0)
        .transpose(1, 0, 2)
        .reshape(slots_here, classes, rotations)
    )
    return (scores, jnp.max(scores, axis=2))


def solution(mesh):
    in_specs = (
        P(("groups", "shard"), None, None),
        P("groups"),
        P("groups"),
        P("groups"),
        P("groups", None, "shard"),
        P("groups", None),
    )
    out_specs = (P(("groups", "shard"), None, None), P(("groups", "shard"), None))
    return jax.shard_map(
        per_device, mesh=mesh, in_specs=in_specs, out_specs=out_specs, check_vma=False
    )
```

```python
import numpy as np
import jax
import jax.numpy as jnp
from jax import lax
from jax.experimental import pallas as pl
from jax.experimental.pallas import tpu as pltpu
from jax.sharding import PartitionSpec as P

BOX = 64
BAND = 32
SHIFTS = 8
PART_DEV = 1


def signed_band(band_size):
    return jnp.arange(band_size, dtype=jnp.int32) - band_size // 2


def table_pair(outer_loop_index, inner_index, box_edge):
    phase_index = outer_loop_index[:, None] * inner_index[None, :] % box_edge
    angles = phase_index.astype(jnp.float32) * (2.0 * jnp.pi / box_edge)
    return (jnp.cos(angles).astype(jnp.bfloat16), jnp.sin(angles).astype(jnp.bfloat16))


def spectral_product(form, left, right):
    return jnp.einsum(form, left, right, preferred_element_type=jnp.float32)


def forward_spectra(volumes):
    batch_size, box_edge = (volumes.shape[0], volumes.shape[1])
    cosine_forward, sine_forward = table_pair(
        signed_band(BAND), jnp.arange(box_edge, dtype=jnp.int32), box_edge
    )
    density_volume = volumes.astype(jnp.bfloat16)
    leading_real = spectral_product("qw,rwl->rql", cosine_forward, density_volume).astype(
        jnp.bfloat16
    )
    leading_imaginary = (-spectral_product("qw,rwl->rql", sine_forward, density_volume)).astype(
        jnp.bfloat16
    )
    leading_real = leading_real.reshape(batch_size, BAND, box_edge, box_edge)
    leading_imaginary = leading_imaginary.reshape(batch_size, BAND, box_edge, box_edge)
    second_real = (
        spectral_product("jy,nkyz->nkjz", cosine_forward, leading_real)
        + spectral_product("jy,nkyz->nkjz", sine_forward, leading_imaginary)
    ).astype(jnp.bfloat16)
    second_imag = (
        spectral_product("jy,nkyz->nkjz", cosine_forward, leading_imaginary)
        - spectral_product("jy,nkyz->nkjz", sine_forward, leading_real)
    ).astype(jnp.bfloat16)
    third_real = spectral_product("nkjz,lz->nkjl", second_real, cosine_forward) + spectral_product(
        "nkjz,lz->nkjl", second_imag, sine_forward
    )
    third_imag = spectral_product("nkjz,lz->nkjl", second_imag, cosine_forward) - spectral_product(
        "nkjz,lz->nkjl", second_real, sine_forward
    )
    spectrum = jnp.stack([third_real, third_imag], axis=1).astype(jnp.bfloat16)
    return spectrum.reshape(batch_size, 2, BAND * BAND * BAND)


def plane_table():
    k = np.arange(BAND) - BAND // 2
    t = np.arange(SHIFTS) - SHIFTS // 2
    phase = (
        t[None, None, :, None] * k[:, None, None, None]
        + t[None, None, None, :] * k[None, :, None, None]
    ) % BOX
    angles = phase.astype(np.float32) * np.float32(2.0 * np.pi / BOX)
    shape = (BAND * BAND, SHIFTS * SHIFTS)
    cosine = np.cos(angles).reshape(shape)
    sine = np.sin(angles).reshape(shape)
    upper = np.concatenate([cosine, sine], axis=1)
    lower = np.concatenate([-sine, cosine], axis=1)
    return jnp.asarray(np.concatenate([upper, lower], axis=0), dtype=jnp.bfloat16)


def shift_tables(n_ref):
    k = np.arange(BAND) - BAND // 2
    t = np.arange(SHIFTS) - SHIFTS // 2
    angles = ((t[:, None] * k[None, :]) % BOX).astype(np.float32) * np.float32(2.0 * np.pi / BOX)
    eye = np.eye(n_ref, dtype=np.float32)
    def rounded(x):
        return jnp.asarray(x, dtype=jnp.bfloat16).astype(jnp.float32)
    return rounded(np.kron(eye, np.cos(angles))), rounded(np.kron(eye, np.sin(angles)))


def correlation_kernel(s_ref, g_ref, c_ref, t_ref, ec_ref, es_ref, r_ref, o_ref, p_s):
    n_ref = c_ref.shape[0]
    plane = BAND * BAND
    contrast = g_ref[0]
    s_real = s_ref[0, 0].astype(jnp.float32)
    s_imag = s_ref[0, 1].astype(jnp.float32)
    w_real = (contrast * s_real).astype(jnp.bfloat16).astype(jnp.float32)
    w_imag = (-(contrast * s_imag)).astype(jnp.bfloat16).astype(jnp.float32)
    for j in range(n_ref):
        c_real = c_ref[j, 0]
        c_imag = c_ref[j, 1]
        rows = slice(j * BAND, (j + 1) * BAND)
        p_s[rows, :plane] = (w_real * c_real - w_imag * c_imag).astype(jnp.bfloat16)
        p_s[rows, plane:] = (w_real * c_imag + w_imag * c_real).astype(jnp.bfloat16)
    planes = jnp.dot(p_s[...], t_ref[...], preferred_element_type=jnp.float32)
    first = jnp.dot(ec_ref[...], planes, preferred_element_type=jnp.float32,
                    precision=lax.Precision.HIGHEST)
    second = jnp.dot(es_ref[...], planes, preferred_element_type=jnp.float32,
                     precision=lax.Precision.HIGHEST)
    half = SHIFTS * SHIFTS
    correlation = first - pltpu.roll(second, half, 1)
    lane = lax.broadcasted_iota(jnp.int32, correlation.shape, 1)
    correlation = jnp.where(lane < half, correlation, -jnp.inf)
    per_row = jnp.max(correlation.reshape(n_ref, SHIFTS, 2 * half), axis=1)
    peak = jnp.max(per_row, axis=1, keepdims=True)
    power = jnp.sum(s_real * s_real + s_imag * s_imag, axis=0, keepdims=True)
    energy_particle = jnp.sum(power, axis=1, keepdims=True)
    energy_ref = r_ref[0][:, 0:1]
    score = float(BAND) ** 1.5 * peak * lax.rsqrt(energy_particle * energy_ref + 1e-06)
    o_ref[0] = jnp.broadcast_to(score, (n_ref, 2 * half))


def peak_correlations(spectra, contrast, refs, energy_ref):
    n_part = spectra.shape[0]
    n_ref = refs.shape[0]
    plane = BAND * BAND
    e_cos, e_sin = shift_tables(n_ref)
    width = 2 * SHIFTS * SHIFTS
    scores = pl.pallas_call(
        correlation_kernel,
        grid=(n_part,),
        in_specs=[
            pl.BlockSpec((1, 2, BAND, plane), lambda i: (i, 0, 0, 0)),
            pl.BlockSpec((1, BAND, plane), lambda i: (i, 0, 0)),
            pl.BlockSpec((n_ref, 2, BAND, plane), lambda i: (0, 0, 0, 0)),
            pl.BlockSpec((2 * plane, width), lambda i: (0, 0)),
            pl.BlockSpec((n_ref * SHIFTS, n_ref * BAND), lambda i: (0, 0)),
            pl.BlockSpec((n_ref * SHIFTS, n_ref * BAND), lambda i: (0, 0)),
            pl.BlockSpec((1, n_ref, width), lambda i: (i, 0, 0)),
        ],
        out_specs=pl.BlockSpec((1, n_ref, width), lambda i: (i, 0, 0)),
        out_shape=jax.ShapeDtypeStruct((n_part, n_ref, width), jnp.float32),
        scratch_shapes=[pltpu.VMEM((n_ref * BAND, 2 * plane), jnp.bfloat16)],
        cost_estimate=pl.CostEstimate(
            flops=n_part * n_ref * (2 * BAND * 2 * plane * width + 8 * BAND * plane),
            transcendentals=0,
            bytes_accessed=n_part * 8 * BAND * plane + n_ref * 8 * BAND * plane,
        ),
    )(
        spectra, contrast, refs, plane_table(), e_cos, e_sin,
        energy_ref,
    )
    return scores


def particle_contrast(bin_ids, defocus):
    band_index = signed_band(BAND).astype(jnp.float32)
    radius = (
        band_index[:, None, None] ** 2
        + band_index[None, :, None] ** 2
        + band_index[None, None, :] ** 2
    ).reshape(-1) / (BAND / 2) ** 2
    chosen_defocus = jnp.sum(
        jnp.where(
            bin_ids[:, None] == jnp.arange(defocus.shape[0], dtype=jnp.int32)[None, :],
            defocus[None, :],
            jnp.float32(0.0),
        ),
        axis=1,
    )
    return -jnp.sin(chosen_defocus[:, None] * radius[None, :] + 0.07)


def reference_energy(contrast, refs):
    volume_size = BAND * BAND * BAND
    ref_real = refs[:, :volume_size].astype(jnp.float32)
    ref_imag = refs[:, volume_size:].astype(jnp.float32)
    magnitude = ref_real * ref_real + ref_imag * ref_imag
    energy = jnp.sum((contrast * contrast)[:, None, :] * magnitude[None, :, :], axis=2)
    return jnp.broadcast_to(energy[:, :, None], energy.shape + (2 * SHIFTS * SHIFTS,))


def score_block(spectra, contrast, energy_ref, refs):
    n_part = spectra.shape[0]
    n_ref = refs.shape[0]
    shape = (BAND, BAND * BAND)
    return peak_correlations(
        spectra.reshape(n_part, 2, *shape),
        contrast.reshape(n_part, *shape),
        refs,
        energy_ref,
    )


def ref_groups(shards, particles, refs):
    best = None
    for groups in range(1, shards + 1):
        if shards % groups or refs % groups or particles % (shards // groups):
            continue
        cost = particles * groups // shards + refs // groups
        if best is None or cost < best[0]:
            best = (cost, groups)
    return best[1]


def per_device(particles, slot_target, slot_defocus_level, defocus, ref_library, rotation_list):
    shards = lax.axis_size("shard")
    my_index = lax.axis_index("shard")
    slots_here = particles.shape[0]
    positions = PART_DEV * shards
    every_slot = slot_target.shape[0]
    classes, rotations = rotation_list.shape
    n_refs = classes * rotations
    r_groups = ref_groups(shards, positions, n_refs)
    p_groups = shards // r_groups
    part_block = positions // p_groups
    ref_block = n_refs // r_groups
    my_pblock = my_index // r_groups

    library = ref_library.shape[1]
    listed = (rotation_list[:, :, None] == jnp.arange(library, dtype=jnp.int32)).astype(jnp.bfloat16)
    listed = jnp.broadcast_to(listed[None], (p_groups,) + listed.shape)
    copies = jnp.broadcast_to(ref_library[None], (p_groups,) + ref_library.shape)
    chosen = jnp.einsum(
        "gcrl,gclk->gcrk", listed, copies, preferred_element_type=jnp.float32
    ).astype(jnp.bfloat16)
    piece = chosen.shape[-1]
    ref_send = chosen.reshape(shards, ref_block, piece)
    ref_got = lax.all_to_all(ref_send, "shard", 0, 0, tiled=True)
    flattened = forward_spectra(particles).reshape(slots_here, -1)
    source = (
        jnp.zeros((positions,), jnp.int32)
        .at[jnp.where(slot_target >= 0, slot_target, positions)]
        .set(jnp.arange(every_slot, dtype=jnp.int32), mode="drop")
    )
    my_sources = lax.dynamic_slice_in_dim(source, my_pblock * part_block, part_block, 0)
    flattened, ref_got, bin_ids = lax.optimization_barrier(
        (flattened, ref_got, slot_defocus_level[my_sources])
    )
    contrast = lax.optimization_barrier(particle_contrast(bin_ids, defocus))
    refs = ref_got.transpose(1, 0, 2).reshape(ref_block, shards * piece)
    pieces = lax.all_to_all(flattened, "shard", split_axis=1, concat_axis=0, tiled=True)

    energy_ref = reference_energy(contrast, refs)
    refs_wide = refs.reshape(ref_block, 2, BAND, BAND * BAND).astype(jnp.float32)
    if r_groups % 2 == 0:
        half = shards // 2
        core = my_index % 2
        groups = [[2 * m + q for m in range(half)] for q in range(2)]
        picked = pieces[source].reshape(p_groups, 1, part_block, piece)
        picked, contrast, energy_ref = lax.optimization_barrier(
            (picked, contrast.reshape(part_block, BAND, BAND * BAND), energy_ref)
        )
        part_send = jnp.broadcast_to(
            picked, (p_groups, r_groups // 2, part_block, piece)
        ).reshape(half, part_block, piece)
        mine = lax.all_to_all(part_send, "shard", 0, 0, tiled=True, axis_index_groups=groups)
        mine, refs_wide = lax.optimization_barrier((mine, refs_wide))
        other = lax.ppermute(mine, "shard", [(d, d ^ 1) for d in range(shards)])
        even = jnp.where(core == 0, mine, other)
        odd = jnp.where(core == 0, other, mine)
        part_got = jnp.stack([even, odd], axis=1).reshape(shards, part_block, piece)
    else:
        part_send = jnp.broadcast_to(
            pieces[source].reshape(p_groups, 1, part_block, piece),
            (p_groups, r_groups, part_block, piece),
        ).reshape(shards, part_block, piece)
        part_got = lax.all_to_all(part_send, "shard", 0, 0, tiled=True)
    spectra = part_got.transpose(1, 0, 2).reshape(part_block, -1)
    block_scores = score_block(spectra, contrast, energy_ref, refs_wide)

    targets = slot_target.reshape(shards, slots_here)
    in_block = (targets >= 0) & (targets // part_block == my_pblock)
    rows = block_scores[jnp.clip(targets - my_pblock * part_block, 0, part_block - 1)][..., 0]
    back_send = jnp.where(in_block[:, :, None], rows, jnp.float32(0.0))
    back_got = lax.all_to_all(back_send, "shard", 0, 0, tiled=True)
    scores = (
        back_got.reshape(p_groups, r_groups, slots_here, ref_block)
        .sum(axis=0)
        .transpose(1, 0, 2)
        .reshape(slots_here, classes, rotations)
    )
    return (scores, jnp.max(scores, axis=2))


def solution(mesh):
    in_specs = (
        P(("groups", "shard"), None, None),
        P("groups"),
        P("groups"),
        P("groups"),
        P("groups", None, "shard"),
        P("groups", None),
    )
    out_specs = (P(("groups", "shard"), None, None), P(("groups", "shard"), None))
    return jax.shard_map(
        per_device, mesh=mesh, in_specs=in_specs, out_specs=out_specs, check_vma=False
    )
```

```python
import numpy as np
import jax
import jax.numpy as jnp
from jax import lax
from jax.experimental import pallas as pl
from jax.experimental.pallas import tpu as pltpu
from jax.sharding import PartitionSpec as P

BOX = 64
BAND = 32
SHIFTS = 8
PART_DEV = 1


def signed_band(band_size):
    return jnp.arange(band_size, dtype=jnp.int32) - band_size // 2


def table_pair(outer_loop_index, inner_index, box_edge):
    phase_index = outer_loop_index[:, None] * inner_index[None, :] % box_edge
    angles = phase_index.astype(jnp.float32) * (2.0 * jnp.pi / box_edge)
    return (jnp.cos(angles).astype(jnp.bfloat16), jnp.sin(angles).astype(jnp.bfloat16))


def spectral_product(form, left, right):
    return jnp.einsum(form, left, right, preferred_element_type=jnp.float32)


def forward_spectra(volumes):
    batch_size, box_edge = (volumes.shape[0], volumes.shape[1])
    cosine_forward, sine_forward = table_pair(
        signed_band(BAND), jnp.arange(box_edge, dtype=jnp.int32), box_edge
    )
    density_volume = volumes.astype(jnp.bfloat16)
    leading_real = spectral_product("qw,rwl->rql", cosine_forward, density_volume).astype(
        jnp.bfloat16
    )
    leading_imaginary = (-spectral_product("qw,rwl->rql", sine_forward, density_volume)).astype(
        jnp.bfloat16
    )
    leading_real = leading_real.reshape(batch_size, BAND, box_edge, box_edge)
    leading_imaginary = leading_imaginary.reshape(batch_size, BAND, box_edge, box_edge)
    second_real = (
        spectral_product("jy,nkyz->nkjz", cosine_forward, leading_real)
        + spectral_product("jy,nkyz->nkjz", sine_forward, leading_imaginary)
    ).astype(jnp.bfloat16)
    second_imag = (
        spectral_product("jy,nkyz->nkjz", cosine_forward, leading_imaginary)
        - spectral_product("jy,nkyz->nkjz", sine_forward, leading_real)
    ).astype(jnp.bfloat16)
    third_real = spectral_product("nkjz,lz->nkjl", second_real, cosine_forward) + spectral_product(
        "nkjz,lz->nkjl", second_imag, sine_forward
    )
    third_imag = spectral_product("nkjz,lz->nkjl", second_imag, cosine_forward) - spectral_product(
        "nkjz,lz->nkjl", second_real, sine_forward
    )
    spectrum = jnp.stack([third_real, third_imag], axis=1).astype(jnp.bfloat16)
    return spectrum.reshape(batch_size, 2, BAND * BAND * BAND)


def plane_table():
    k = np.arange(BAND) - BAND // 2
    t = np.arange(SHIFTS) - SHIFTS // 2
    phase = (
        t[None, None, :, None] * k[:, None, None, None]
        + t[None, None, None, :] * k[None, :, None, None]
    ) % BOX
    angles = phase.astype(np.float32) * np.float32(2.0 * np.pi / BOX)
    shape = (BAND * BAND, SHIFTS * SHIFTS)
    cosine = np.cos(angles).reshape(shape)
    sine = np.sin(angles).reshape(shape)
    upper = np.concatenate([cosine, sine], axis=1)
    lower = np.concatenate([-sine, cosine], axis=1)
    return jnp.asarray(np.concatenate([upper, lower], axis=0), dtype=jnp.bfloat16)


def shift_tables(n_ref):
    k = np.arange(BAND) - BAND // 2
    t = np.arange(SHIFTS) - SHIFTS // 2
    angles = ((t[:, None] * k[None, :]) % BOX).astype(np.float32) * np.float32(2.0 * np.pi / BOX)
    eye = np.eye(n_ref, dtype=np.float32)
    def rounded(x):
        return jnp.asarray(x, dtype=jnp.bfloat16).astype(jnp.float32)
    return rounded(np.kron(eye, np.cos(angles))), rounded(np.kron(eye, np.sin(angles)))


def correlation_kernel(s_ref, g_ref, c_ref, t_ref, ec_ref, es_ref, r_ref, o_ref, p_s):
    per_step = s_ref.shape[0]
    n_ref = c_ref.shape[0]
    plane = BAND * BAND
    half = SHIFTS * SHIFTS
    power = []
    for p in range(per_step):
        contrast = g_ref[p]
        s_real = s_ref[p, 0].astype(jnp.float32)
        s_imag = s_ref[p, 1].astype(jnp.float32)
        w_real = (contrast * s_real).astype(jnp.bfloat16).astype(jnp.float32)
        w_imag = (-(contrast * s_imag)).astype(jnp.bfloat16).astype(jnp.float32)
        for j in range(n_ref):
            c_real = c_ref[j, 0]
            c_imag = c_ref[j, 1]
            rows = slice((p * n_ref + j) * BAND, (p * n_ref + j + 1) * BAND)
            p_s[rows, :plane] = (w_real * c_real - w_imag * c_imag).astype(jnp.bfloat16)
            p_s[rows, plane:] = (w_real * c_imag + w_imag * c_real).astype(jnp.bfloat16)
        rowsum = jnp.sum(s_real * s_real + s_imag * s_imag, axis=0, keepdims=True)
        power.append(jnp.sum(rowsum, axis=1, keepdims=True))
    planes = jnp.dot(p_s[...], t_ref[...], preferred_element_type=jnp.float32)
    first = jnp.dot(ec_ref[...], planes, preferred_element_type=jnp.float32,
                    precision=lax.Precision.HIGHEST)
    second = jnp.dot(es_ref[...], planes, preferred_element_type=jnp.float32,
                     precision=lax.Precision.HIGHEST)
    correlation = first - pltpu.roll(second, half, 1)
    lane = lax.broadcasted_iota(jnp.int32, correlation.shape, 1)
    correlation = jnp.where(lane < half, correlation, -jnp.inf)
    per_row = jnp.max(correlation.reshape(per_step * n_ref, SHIFTS, 2 * half), axis=1)
    peak = jnp.max(per_row, axis=1, keepdims=True)
    for p in range(per_step):
        energy_ref = r_ref[p][:, 0:1]
        score = float(BAND) ** 1.5 * peak[p * n_ref:(p + 1) * n_ref] * lax.rsqrt(
            power[p] * energy_ref + 1e-06
        )
        o_ref[p] = jnp.broadcast_to(score, (n_ref, 2 * half))


def peak_correlations(spectra, contrast, refs, energy_ref):
    n_part = spectra.shape[0]
    n_ref = refs.shape[0]
    plane = BAND * BAND
    per_step = 2 if n_part % 2 == 0 else 1
    e_cos, e_sin = shift_tables(per_step * n_ref)
    width = 2 * SHIFTS * SHIFTS
    scores = pl.pallas_call(
        correlation_kernel,
        grid=(n_part // per_step,),
        in_specs=[
            pl.BlockSpec((per_step, 2, BAND, plane), lambda i: (i, 0, 0, 0)),
            pl.BlockSpec((per_step, BAND, plane), lambda i: (i, 0, 0)),
            pl.BlockSpec((n_ref, 2, BAND, plane), lambda i: (0, 0, 0, 0)),
            pl.BlockSpec((2 * plane, width), lambda i: (0, 0)),
            pl.BlockSpec((per_step * n_ref * SHIFTS, per_step * n_ref * BAND), lambda i: (0, 0)),
            pl.BlockSpec((per_step * n_ref * SHIFTS, per_step * n_ref * BAND), lambda i: (0, 0)),
            pl.BlockSpec((per_step, n_ref, width), lambda i: (i, 0, 0)),
        ],
        out_specs=pl.BlockSpec((per_step, n_ref, width), lambda i: (i, 0, 0)),
        out_shape=jax.ShapeDtypeStruct((n_part, n_ref, width), jnp.float32),
        scratch_shapes=[pltpu.VMEM((per_step * n_ref * BAND, 2 * plane), jnp.bfloat16)],
        cost_estimate=pl.CostEstimate(
            flops=n_part * n_ref * (2 * BAND * 2 * plane * width + 8 * BAND * plane),
            transcendentals=0,
            bytes_accessed=n_part * 8 * BAND * plane + n_ref * 8 * BAND * plane,
        ),
    )(
        spectra, contrast, refs, plane_table(), e_cos, e_sin,
        energy_ref,
    )
    return scores


def particle_contrast(bin_ids, defocus):
    band_index = signed_band(BAND).astype(jnp.float32)
    radius = (
        band_index[:, None, None] ** 2
        + band_index[None, :, None] ** 2
        + band_index[None, None, :] ** 2
    ).reshape(-1) / (BAND / 2) ** 2
    chosen_defocus = jnp.sum(
        jnp.where(
            bin_ids[:, None] == jnp.arange(defocus.shape[0], dtype=jnp.int32)[None, :],
            defocus[None, :],
            jnp.float32(0.0),
        ),
        axis=1,
    )
    return -jnp.sin(chosen_defocus[:, None] * radius[None, :] + 0.07)


def reference_energy(contrast, refs):
    volume_size = BAND * BAND * BAND
    ref_real = refs[:, :volume_size].astype(jnp.float32)
    ref_imag = refs[:, volume_size:].astype(jnp.float32)
    magnitude = ref_real * ref_real + ref_imag * ref_imag
    energy = jnp.sum((contrast * contrast)[:, None, :] * magnitude[None, :, :], axis=2)
    return jnp.broadcast_to(energy[:, :, None], energy.shape + (2 * SHIFTS * SHIFTS,))


def score_block(spectra, contrast, energy_ref, refs):
    n_part = spectra.shape[0]
    n_ref = refs.shape[0]
    shape = (BAND, BAND * BAND)
    return peak_correlations(
        spectra.reshape(n_part, 2, *shape),
        contrast.reshape(n_part, *shape),
        refs,
        energy_ref,
    )


def ref_groups(shards, particles, refs):
    best = None
    for groups in range(1, shards + 1):
        if shards % groups or refs % groups or particles % (shards // groups):
            continue
        cost = particles * groups // shards + refs // groups
        if best is None or cost < best[0]:
            best = (cost, groups)
    return best[1]


def per_device(particles, slot_target, slot_defocus_level, defocus, ref_library, rotation_list):
    shards = lax.axis_size("shard")
    my_index = lax.axis_index("shard")
    slots_here = particles.shape[0]
    positions = PART_DEV * shards
    every_slot = slot_target.shape[0]
    classes, rotations = rotation_list.shape
    n_refs = classes * rotations
    r_groups = ref_groups(shards, positions, n_refs)
    p_groups = shards // r_groups
    part_block = positions // p_groups
    ref_block = n_refs // r_groups
    my_pblock = my_index // r_groups

    library = ref_library.shape[1]
    listed = (rotation_list[:, :, None] == jnp.arange(library, dtype=jnp.int32)).astype(jnp.bfloat16)
    listed = jnp.broadcast_to(listed[None], (p_groups,) + listed.shape)
    chosen = jnp.einsum(
        "gcrl,clk->gcrk", listed, ref_library, preferred_element_type=jnp.float32
    ).astype(jnp.bfloat16)
    piece = chosen.shape[-1]
    ref_send = chosen.reshape(shards, ref_block, piece)
    ref_got = lax.all_to_all(ref_send, "shard", 0, 0, tiled=True)
    flattened = forward_spectra(particles).reshape(slots_here, -1)
    source = (
        jnp.zeros((positions,), jnp.int32)
        .at[jnp.where(slot_target >= 0, slot_target, positions)]
        .set(jnp.arange(every_slot, dtype=jnp.int32), mode="drop")
    )
    my_sources = lax.dynamic_slice_in_dim(source, my_pblock * part_block, part_block, 0)
    flattened, ref_got, bin_ids = lax.optimization_barrier(
        (flattened, ref_got, slot_defocus_level[my_sources])
    )
    contrast = lax.optimization_barrier(particle_contrast(bin_ids, defocus))
    refs = ref_got.transpose(1, 0, 2).reshape(ref_block, shards * piece)
    pieces = lax.all_to_all(flattened, "shard", split_axis=1, concat_axis=0, tiled=True)

    energy_ref = reference_energy(contrast, refs)
    refs_wide = refs.reshape(ref_block, 2, BAND, BAND * BAND).astype(jnp.float32)
    if r_groups % 2 == 0:
        half = shards // 2
        core = my_index % 2
        groups = [[2 * m + q for m in range(half)] for q in range(2)]
        picked = pieces[source].reshape(p_groups, 1, part_block, piece)
        picked, contrast, energy_ref = lax.optimization_barrier(
            (picked, contrast.reshape(part_block, BAND, BAND * BAND), energy_ref)
        )
        part_send = jnp.broadcast_to(
            picked, (p_groups, r_groups // 2, part_block, piece)
        ).reshape(half, part_block, piece)
        mine = lax.all_to_all(part_send, "shard", 0, 0, tiled=True, axis_index_groups=groups)
        mine, refs_wide = lax.optimization_barrier((mine, refs_wide))
        other = lax.ppermute(mine, "shard", [(d, d ^ 1) for d in range(shards)])
        even = jnp.where(core == 0, mine, other)
        odd = jnp.where(core == 0, other, mine)
        part_got = jnp.stack([even, odd], axis=1).reshape(shards, part_block, piece)
    else:
        part_send = jnp.broadcast_to(
            pieces[source].reshape(p_groups, 1, part_block, piece),
            (p_groups, r_groups, part_block, piece),
        ).reshape(shards, part_block, piece)
        part_got = lax.all_to_all(part_send, "shard", 0, 0, tiled=True)
    spectra = part_got.transpose(1, 0, 2).reshape(part_block, -1)
    block_scores = score_block(spectra, contrast, energy_ref, refs_wide)

    targets = slot_target.reshape(shards, slots_here)
    in_block = (targets >= 0) & (targets // part_block == my_pblock)
    rows = block_scores[jnp.clip(targets - my_pblock * part_block, 0, part_block - 1)][..., 0]
    back_send = jnp.where(in_block[:, :, None], rows, jnp.float32(0.0))
    back_got = lax.all_to_all(back_send, "shard", 0, 0, tiled=True)
    scores = (
        back_got.reshape(p_groups, r_groups, slots_here, ref_block)
        .sum(axis=0)
        .transpose(1, 0, 2)
        .reshape(slots_here, classes, rotations)
    )
    return (scores, jnp.max(scores, axis=2))


def solution(mesh):
    in_specs = (
        P(("groups", "shard"), None, None),
        P("groups"),
        P("groups"),
        P("groups"),
        P("groups", None, "shard"),
        P("groups", None),
    )
    out_specs = (P(("groups", "shard"), None, None), P(("groups", "shard"), None))
    return jax.shard_map(
        per_device, mesh=mesh, in_specs=in_specs, out_specs=out_specs, check_vma=False
    )
```

```python
import numpy as np
import jax
import jax.numpy as jnp
from jax import lax
from jax.experimental import pallas as pl
from jax.experimental.pallas import tpu as pltpu
from jax.sharding import PartitionSpec as P

BOX = 64
BAND = 32
SHIFTS = 8
PART_DEV = 1


def signed_band(band_size):
    return jnp.arange(band_size, dtype=jnp.int32) - band_size // 2


def table_pair(outer_loop_index, inner_index, box_edge):
    phase_index = outer_loop_index[:, None] * inner_index[None, :] % box_edge
    angles = phase_index.astype(jnp.float32) * (2.0 * jnp.pi / box_edge)
    return (jnp.cos(angles).astype(jnp.bfloat16), jnp.sin(angles).astype(jnp.bfloat16))


def spectral_product(form, left, right):
    return jnp.einsum(form, left, right, preferred_element_type=jnp.float32)


def forward_spectra(volumes):
    batch_size, box_edge = (volumes.shape[0], volumes.shape[1])
    cosine_forward, sine_forward = table_pair(
        signed_band(BAND), jnp.arange(box_edge, dtype=jnp.int32), box_edge
    )
    density_volume = volumes.astype(jnp.bfloat16)
    leading_real = spectral_product("qw,rwl->rql", cosine_forward, density_volume).astype(
        jnp.bfloat16
    )
    leading_imaginary = (-spectral_product("qw,rwl->rql", sine_forward, density_volume)).astype(
        jnp.bfloat16
    )
    leading_real = leading_real.reshape(batch_size, BAND, box_edge, box_edge)
    leading_imaginary = leading_imaginary.reshape(batch_size, BAND, box_edge, box_edge)
    second_real = (
        spectral_product("jy,nkyz->nkjz", cosine_forward, leading_real)
        + spectral_product("jy,nkyz->nkjz", sine_forward, leading_imaginary)
    ).astype(jnp.bfloat16)
    second_imag = (
        spectral_product("jy,nkyz->nkjz", cosine_forward, leading_imaginary)
        - spectral_product("jy,nkyz->nkjz", sine_forward, leading_real)
    ).astype(jnp.bfloat16)
    third_real = spectral_product("nkjz,lz->nkjl", second_real, cosine_forward) + spectral_product(
        "nkjz,lz->nkjl", second_imag, sine_forward
    )
    third_imag = spectral_product("nkjz,lz->nkjl", second_imag, cosine_forward) - spectral_product(
        "nkjz,lz->nkjl", second_real, sine_forward
    )
    spectrum = jnp.stack([third_real, third_imag], axis=1).astype(jnp.bfloat16)
    return spectrum.reshape(batch_size, 2, BAND * BAND * BAND)


def plane_table():
    k = np.arange(BAND) - BAND // 2
    t = np.arange(SHIFTS) - SHIFTS // 2
    phase = (
        t[None, None, :, None] * k[:, None, None, None]
        + t[None, None, None, :] * k[None, :, None, None]
    ) % BOX
    angles = phase.astype(np.float32) * np.float32(2.0 * np.pi / BOX)
    shape = (BAND * BAND, SHIFTS * SHIFTS)
    cosine = np.cos(angles).reshape(shape)
    sine = np.sin(angles).reshape(shape)
    upper = np.concatenate([cosine, sine], axis=1)
    lower = np.concatenate([-sine, cosine], axis=1)
    return jnp.asarray(np.concatenate([upper, lower], axis=0), dtype=jnp.bfloat16)


def shift_tables(n_ref):
    k = np.arange(BAND) - BAND // 2
    t = np.arange(SHIFTS) - SHIFTS // 2
    angles = ((t[:, None] * k[None, :]) % BOX).astype(np.float32) * np.float32(2.0 * np.pi / BOX)
    eye = np.eye(n_ref, dtype=np.float32)
    def rounded(x):
        return jnp.asarray(x, dtype=jnp.bfloat16).astype(jnp.float32)
    return rounded(np.kron(eye, np.cos(angles))), rounded(np.kron(eye, np.sin(angles)))


def correlation_kernel(s_ref, g_ref, c_ref, t_ref, ec_ref, es_ref, r_ref, o_ref, p_s):
    n_ref = c_ref.shape[0]
    plane = BAND * BAND
    contrast = g_ref[0]
    s_real = s_ref[0, 0].astype(jnp.float32)
    s_imag = s_ref[0, 1].astype(jnp.float32)
    w_real = (contrast * s_real).astype(jnp.bfloat16).astype(jnp.float32)
    w_imag = (-(contrast * s_imag)).astype(jnp.bfloat16).astype(jnp.float32)
    for j in range(n_ref):
        c_real = c_ref[j, 0]
        c_imag = c_ref[j, 1]
        rows = slice(j * BAND, (j + 1) * BAND)
        p_s[rows, :plane] = (w_real * c_real - w_imag * c_imag).astype(jnp.bfloat16)
        p_s[rows, plane:] = (w_real * c_imag + w_imag * c_real).astype(jnp.bfloat16)
    planes = jnp.dot(p_s[...], t_ref[...], preferred_element_type=jnp.float32)
    first = jnp.dot(ec_ref[...], planes, preferred_element_type=jnp.float32,
                    precision=lax.Precision.HIGH)
    second = jnp.dot(es_ref[...], planes, preferred_element_type=jnp.float32,
                     precision=lax.Precision.HIGH)
    half = SHIFTS * SHIFTS
    correlation = first - pltpu.roll(second, half, 1)
    lane = lax.broadcasted_iota(jnp.int32, correlation.shape, 1)
    correlation = jnp.where(lane < half, correlation, -jnp.inf)
    per_row = jnp.max(correlation.reshape(n_ref, SHIFTS, 2 * half), axis=1)
    peak = jnp.max(per_row, axis=1, keepdims=True)
    power = jnp.sum(s_real * s_real + s_imag * s_imag, axis=0, keepdims=True)
    energy_particle = jnp.sum(power, axis=1, keepdims=True)
    energy_ref = r_ref[0][:, 0:1]
    score = float(BAND) ** 1.5 * peak * lax.rsqrt(energy_particle * energy_ref + 1e-06)
    o_ref[0] = jnp.broadcast_to(score, (n_ref, 2 * half))


def peak_correlations(spectra, contrast, refs, energy_ref):
    n_part = spectra.shape[0]
    n_ref = refs.shape[0]
    plane = BAND * BAND
    e_cos, e_sin = shift_tables(n_ref)
    width = 2 * SHIFTS * SHIFTS
    scores = pl.pallas_call(
        correlation_kernel,
        grid=(n_part,),
        in_specs=[
            pl.BlockSpec((1, 2, BAND, plane), lambda i: (i, 0, 0, 0)),
            pl.BlockSpec((1, BAND, plane), lambda i: (i, 0, 0)),
            pl.BlockSpec((n_ref, 2, BAND, plane), lambda i: (0, 0, 0, 0)),
            pl.BlockSpec((2 * plane, width), lambda i: (0, 0)),
            pl.BlockSpec((n_ref * SHIFTS, n_ref * BAND), lambda i: (0, 0)),
            pl.BlockSpec((n_ref * SHIFTS, n_ref * BAND), lambda i: (0, 0)),
            pl.BlockSpec((1, n_ref, width), lambda i: (i, 0, 0)),
        ],
        out_specs=pl.BlockSpec((1, n_ref, width), lambda i: (i, 0, 0)),
        out_shape=jax.ShapeDtypeStruct((n_part, n_ref, width), jnp.float32),
        scratch_shapes=[pltpu.VMEM((n_ref * BAND, 2 * plane), jnp.bfloat16)],
        cost_estimate=pl.CostEstimate(
            flops=n_part * n_ref * (2 * BAND * 2 * plane * width + 8 * BAND * plane),
            transcendentals=0,
            bytes_accessed=n_part * 8 * BAND * plane + n_ref * 8 * BAND * plane,
        ),
    )(
        spectra, contrast, refs, plane_table(), e_cos, e_sin,
        energy_ref,
    )
    return scores


def particle_contrast(bin_ids, defocus):
    band_index = signed_band(BAND).astype(jnp.float32)
    radius = (
        band_index[:, None, None] ** 2
        + band_index[None, :, None] ** 2
        + band_index[None, None, :] ** 2
    ).reshape(-1) / (BAND / 2) ** 2
    chosen_defocus = jnp.sum(
        jnp.where(
            bin_ids[:, None] == jnp.arange(defocus.shape[0], dtype=jnp.int32)[None, :],
            defocus[None, :],
            jnp.float32(0.0),
        ),
        axis=1,
    )
    return -jnp.sin(chosen_defocus[:, None] * radius[None, :] + 0.07)


def reference_energy(contrast, refs):
    volume_size = BAND * BAND * BAND
    ref_real = refs[:, :volume_size].astype(jnp.float32)
    ref_imag = refs[:, volume_size:].astype(jnp.float32)
    magnitude = ref_real * ref_real + ref_imag * ref_imag
    energy = jnp.sum((contrast * contrast)[:, None, :] * magnitude[None, :, :], axis=2)
    return jnp.broadcast_to(energy[:, :, None], energy.shape + (2 * SHIFTS * SHIFTS,))


def score_block(spectra, contrast, energy_ref, refs):
    n_part = spectra.shape[0]
    n_ref = refs.shape[0]
    shape = (BAND, BAND * BAND)
    return peak_correlations(
        spectra.reshape(n_part, 2, *shape),
        contrast.reshape(n_part, *shape),
        refs,
        energy_ref,
    )


def ref_groups(shards, particles, refs):
    best = None
    for groups in range(1, shards + 1):
        if shards % groups or refs % groups or particles % (shards // groups):
            continue
        cost = particles * groups // shards + refs // groups
        if best is None or cost < best[0]:
            best = (cost, groups)
    return best[1]


def per_device(particles, slot_target, slot_defocus_level, defocus, ref_library, rotation_list):
    shards = lax.axis_size("shard")
    my_index = lax.axis_index("shard")
    slots_here = particles.shape[0]
    positions = PART_DEV * shards
    every_slot = slot_target.shape[0]
    classes, rotations = rotation_list.shape
    n_refs = classes * rotations
    r_groups = ref_groups(shards, positions, n_refs)
    p_groups = shards // r_groups
    part_block = positions // p_groups
    ref_block = n_refs // r_groups
    my_pblock = my_index // r_groups

    library = ref_library.shape[1]
    listed = (rotation_list[:, :, None] == jnp.arange(library, dtype=jnp.int32)).astype(jnp.bfloat16)
    listed = jnp.broadcast_to(listed[None], (p_groups,) + listed.shape)
    chosen = jnp.einsum(
        "gcrl,clk->gcrk", listed, ref_library, preferred_element_type=jnp.float32
    ).astype(jnp.bfloat16)
    piece = chosen.shape[-1]
    ref_send = chosen.reshape(shards, ref_block, piece)
    ref_got = lax.all_to_all(ref_send, "shard", 0, 0, tiled=True)
    flattened = forward_spectra(particles).reshape(slots_here, -1)
    source = (
        jnp.zeros((positions,), jnp.int32)
        .at[jnp.where(slot_target >= 0, slot_target, positions)]
        .set(jnp.arange(every_slot, dtype=jnp.int32), mode="drop")
    )
    my_sources = lax.dynamic_slice_in_dim(source, my_pblock * part_block, part_block, 0)
    flattened, ref_got, bin_ids = lax.optimization_barrier(
        (flattened, ref_got, slot_defocus_level[my_sources])
    )
    contrast = lax.optimization_barrier(particle_contrast(bin_ids, defocus))
    refs = ref_got.transpose(1, 0, 2).reshape(ref_block, shards * piece)
    pieces = lax.all_to_all(flattened, "shard", split_axis=1, concat_axis=0, tiled=True)

    energy_ref = reference_energy(contrast, refs)
    refs_wide = refs.reshape(ref_block, 2, BAND, BAND * BAND).astype(jnp.float32)
    if r_groups % 2 == 0:
        half = shards // 2
        core = my_index % 2
        groups = [[2 * m + q for m in range(half)] for q in range(2)]
        picked = pieces[source].reshape(p_groups, 1, part_block, piece)
        picked, contrast, energy_ref = lax.optimization_barrier(
            (picked, contrast.reshape(part_block, BAND, BAND * BAND), energy_ref)
        )
        part_send = jnp.broadcast_to(
            picked, (p_groups, r_groups // 2, part_block, piece)
        ).reshape(half, part_block, piece)
        mine = lax.all_to_all(part_send, "shard", 0, 0, tiled=True, axis_index_groups=groups)
        mine, refs_wide = lax.optimization_barrier((mine, refs_wide))
        other = lax.ppermute(mine, "shard", [(d, d ^ 1) for d in range(shards)])
        even = jnp.where(core == 0, mine, other)
        odd = jnp.where(core == 0, other, mine)
        part_got = jnp.stack([even, odd], axis=1).reshape(shards, part_block, piece)
    else:
        part_send = jnp.broadcast_to(
            pieces[source].reshape(p_groups, 1, part_block, piece),
            (p_groups, r_groups, part_block, piece),
        ).reshape(shards, part_block, piece)
        part_got = lax.all_to_all(part_send, "shard", 0, 0, tiled=True)
    spectra = part_got.transpose(1, 0, 2).reshape(part_block, -1)
    block_scores = score_block(spectra, contrast, energy_ref, refs_wide)

    targets = slot_target.reshape(shards, slots_here)
    in_block = (targets >= 0) & (targets // part_block == my_pblock)
    rows = block_scores[jnp.clip(targets - my_pblock * part_block, 0, part_block - 1)][..., 0]
    back_send = jnp.where(in_block[:, :, None], rows, jnp.float32(0.0))
    back_got = lax.all_to_all(back_send, "shard", 0, 0, tiled=True)
    scores = (
        back_got.reshape(p_groups, r_groups, slots_here, ref_block)
        .sum(axis=0)
        .transpose(1, 0, 2)
        .reshape(slots_here, classes, rotations)
    )
    return (scores, jnp.max(scores, axis=2))


def solution(mesh):
    in_specs = (
        P(("groups", "shard"), None, None),
        P("groups"),
        P("groups"),
        P("groups"),
        P("groups", None, "shard"),
        P("groups", None),
    )
    out_specs = (P(("groups", "shard"), None, None), P(("groups", "shard"), None))
    return jax.shard_map(
        per_device, mesh=mesh, in_specs=in_specs, out_specs=out_specs, check_vma=False
    )
```

```python
import numpy as np
import jax
import jax.numpy as jnp
from jax import lax
from jax.experimental import pallas as pl
from jax.experimental.pallas import tpu as pltpu
from jax.sharding import PartitionSpec as P

BOX = 64
BAND = 32
SHIFTS = 8
PART_DEV = 1


def signed_band(band_size):
    return jnp.arange(band_size, dtype=jnp.int32) - band_size // 2


def table_pair(outer_loop_index, inner_index, box_edge):
    phase_index = outer_loop_index[:, None] * inner_index[None, :] % box_edge
    angles = phase_index.astype(jnp.float32) * (2.0 * jnp.pi / box_edge)
    return (jnp.cos(angles).astype(jnp.bfloat16), jnp.sin(angles).astype(jnp.bfloat16))


def spectral_product(form, left, right):
    return jnp.einsum(form, left, right, preferred_element_type=jnp.float32)


def forward_spectra(volumes):
    batch_size, box_edge = (volumes.shape[0], volumes.shape[1])
    cosine_forward, sine_forward = table_pair(
        signed_band(BAND), jnp.arange(box_edge, dtype=jnp.int32), box_edge
    )
    density_volume = volumes.astype(jnp.bfloat16)
    leading_real = spectral_product("qw,rwl->rql", cosine_forward, density_volume).astype(
        jnp.bfloat16
    )
    leading_imaginary = (-spectral_product("qw,rwl->rql", sine_forward, density_volume)).astype(
        jnp.bfloat16
    )
    leading_real = leading_real.reshape(batch_size, BAND, box_edge, box_edge)
    leading_imaginary = leading_imaginary.reshape(batch_size, BAND, box_edge, box_edge)
    second_real = (
        spectral_product("jy,nkyz->nkjz", cosine_forward, leading_real)
        + spectral_product("jy,nkyz->nkjz", sine_forward, leading_imaginary)
    ).astype(jnp.bfloat16)
    second_imag = (
        spectral_product("jy,nkyz->nkjz", cosine_forward, leading_imaginary)
        - spectral_product("jy,nkyz->nkjz", sine_forward, leading_real)
    ).astype(jnp.bfloat16)
    third_real = spectral_product("nkjz,lz->nkjl", second_real, cosine_forward) + spectral_product(
        "nkjz,lz->nkjl", second_imag, sine_forward
    )
    third_imag = spectral_product("nkjz,lz->nkjl", second_imag, cosine_forward) - spectral_product(
        "nkjz,lz->nkjl", second_real, sine_forward
    )
    spectrum = jnp.stack([third_real, third_imag], axis=1).astype(jnp.bfloat16)
    return spectrum.reshape(batch_size, 2, BAND * BAND * BAND)


def plane_table():
    k = np.arange(BAND) - BAND // 2
    t = np.arange(SHIFTS) - SHIFTS // 2
    phase = (
        t[None, None, :, None] * k[:, None, None, None]
        + t[None, None, None, :] * k[None, :, None, None]
    ) % BOX
    angles = phase.astype(np.float32) * np.float32(2.0 * np.pi / BOX)
    shape = (BAND * BAND, SHIFTS * SHIFTS)
    cosine = np.cos(angles).reshape(shape)
    sine = np.sin(angles).reshape(shape)
    upper = np.concatenate([cosine, sine], axis=1)
    lower = np.concatenate([-sine, cosine], axis=1)
    return jnp.asarray(np.concatenate([upper, lower], axis=0), dtype=jnp.bfloat16)


def shift_tables(n_ref):
    k = np.arange(BAND) - BAND // 2
    t = np.arange(SHIFTS) - SHIFTS // 2
    angles = ((t[:, None] * k[None, :]) % BOX).astype(np.float32) * np.float32(2.0 * np.pi / BOX)
    eye = np.eye(n_ref, dtype=np.float32)
    def rounded(x):
        return jnp.asarray(x, dtype=jnp.bfloat16).astype(jnp.float32)
    return rounded(np.kron(eye, np.cos(angles))), rounded(np.kron(eye, np.sin(angles)))


def correlation_kernel(s_ref, g_ref, c_ref, t_ref, ec_ref, es_ref, r_ref, o_ref, p_s):
    n_ref = c_ref.shape[0]
    plane = BAND * BAND
    contrast = g_ref[0]
    s_real = s_ref[0, 0].astype(jnp.float32)
    s_imag = s_ref[0, 1].astype(jnp.float32)
    w_real = (contrast * s_real).astype(jnp.bfloat16).astype(jnp.float32)
    w_imag = (-(contrast * s_imag)).astype(jnp.bfloat16).astype(jnp.float32)
    for j in range(n_ref):
        c_real = c_ref[j, 0]
        c_imag = c_ref[j, 1]
        rows = slice(j * BAND, (j + 1) * BAND)
        p_s[rows, :plane] = (w_real * c_real - w_imag * c_imag).astype(jnp.bfloat16)
        p_s[rows, plane:] = (w_real * c_imag + w_imag * c_real).astype(jnp.bfloat16)
    planes = jnp.dot(p_s[...], t_ref[...], preferred_element_type=jnp.float32)
    first = jnp.dot(ec_ref[...], planes, preferred_element_type=jnp.float32,
                    precision=lax.Precision.DEFAULT)
    second = jnp.dot(es_ref[...], planes, preferred_element_type=jnp.float32,
                     precision=lax.Precision.DEFAULT)
    half = SHIFTS * SHIFTS
    correlation = first - pltpu.roll(second, half, 1)
    lane = lax.broadcasted_iota(jnp.int32, correlation.shape, 1)
    correlation = jnp.where(lane < half, correlation, -jnp.inf)
    per_row = jnp.max(correlation.reshape(n_ref, SHIFTS, 2 * half), axis=1)
    peak = jnp.max(per_row, axis=1, keepdims=True)
    power = jnp.sum(s_real * s_real + s_imag * s_imag, axis=0, keepdims=True)
    energy_particle = jnp.sum(power, axis=1, keepdims=True)
    energy_ref = r_ref[0][:, 0:1]
    score = float(BAND) ** 1.5 * peak * lax.rsqrt(energy_particle * energy_ref + 1e-06)
    o_ref[0] = jnp.broadcast_to(score, (n_ref, 2 * half))


def peak_correlations(spectra, contrast, refs, energy_ref):
    n_part = spectra.shape[0]
    n_ref = refs.shape[0]
    plane = BAND * BAND
    e_cos, e_sin = shift_tables(n_ref)
    width = 2 * SHIFTS * SHIFTS
    scores = pl.pallas_call(
        correlation_kernel,
        grid=(n_part,),
        in_specs=[
            pl.BlockSpec((1, 2, BAND, plane), lambda i: (i, 0, 0, 0)),
            pl.BlockSpec((1, BAND, plane), lambda i: (i, 0, 0)),
            pl.BlockSpec((n_ref, 2, BAND, plane), lambda i: (0, 0, 0, 0)),
            pl.BlockSpec((2 * plane, width), lambda i: (0, 0)),
            pl.BlockSpec((n_ref * SHIFTS, n_ref * BAND), lambda i: (0, 0)),
            pl.BlockSpec((n_ref * SHIFTS, n_ref * BAND), lambda i: (0, 0)),
            pl.BlockSpec((1, n_ref, width), lambda i: (i, 0, 0)),
        ],
        out_specs=pl.BlockSpec((1, n_ref, width), lambda i: (i, 0, 0)),
        out_shape=jax.ShapeDtypeStruct((n_part, n_ref, width), jnp.float32),
        scratch_shapes=[pltpu.VMEM((n_ref * BAND, 2 * plane), jnp.bfloat16)],
        cost_estimate=pl.CostEstimate(
            flops=n_part * n_ref * (2 * BAND * 2 * plane * width + 8 * BAND * plane),
            transcendentals=0,
            bytes_accessed=n_part * 8 * BAND * plane + n_ref * 8 * BAND * plane,
        ),
    )(
        spectra, contrast, refs, plane_table(), e_cos, e_sin,
        energy_ref,
    )
    return scores


def particle_contrast(bin_ids, defocus):
    band_index = signed_band(BAND).astype(jnp.float32)
    radius = (
        band_index[:, None, None] ** 2
        + band_index[None, :, None] ** 2
        + band_index[None, None, :] ** 2
    ).reshape(-1) / (BAND / 2) ** 2
    chosen_defocus = jnp.sum(
        jnp.where(
            bin_ids[:, None] == jnp.arange(defocus.shape[0], dtype=jnp.int32)[None, :],
            defocus[None, :],
            jnp.float32(0.0),
        ),
        axis=1,
    )
    return -jnp.sin(chosen_defocus[:, None] * radius[None, :] + 0.07)


def reference_energy(contrast, refs):
    volume_size = BAND * BAND * BAND
    ref_real = refs[:, :volume_size].astype(jnp.float32)
    ref_imag = refs[:, volume_size:].astype(jnp.float32)
    magnitude = ref_real * ref_real + ref_imag * ref_imag
    energy = jnp.sum((contrast * contrast)[:, None, :] * magnitude[None, :, :], axis=2)
    return jnp.broadcast_to(energy[:, :, None], energy.shape + (2 * SHIFTS * SHIFTS,))


def score_block(spectra, contrast, energy_ref, refs):
    n_part = spectra.shape[0]
    n_ref = refs.shape[0]
    shape = (BAND, BAND * BAND)
    return peak_correlations(
        spectra.reshape(n_part, 2, *shape),
        contrast.reshape(n_part, *shape),
        refs,
        energy_ref,
    )


def ref_groups(shards, particles, refs):
    best = None
    for groups in range(1, shards + 1):
        if shards % groups or refs % groups or particles % (shards // groups):
            continue
        cost = particles * groups // shards + refs // groups
        if best is None or cost < best[0]:
            best = (cost, groups)
    return best[1]


def per_device(particles, slot_target, slot_defocus_level, defocus, ref_library, rotation_list):
    shards = lax.axis_size("shard")
    my_index = lax.axis_index("shard")
    slots_here = particles.shape[0]
    positions = PART_DEV * shards
    every_slot = slot_target.shape[0]
    classes, rotations = rotation_list.shape
    n_refs = classes * rotations
    r_groups = ref_groups(shards, positions, n_refs)
    p_groups = shards // r_groups
    part_block = positions // p_groups
    ref_block = n_refs // r_groups
    my_pblock = my_index // r_groups

    library = ref_library.shape[1]
    listed = (rotation_list[:, :, None] == jnp.arange(library, dtype=jnp.int32)).astype(jnp.bfloat16)
    listed = jnp.broadcast_to(listed[None], (p_groups,) + listed.shape)
    chosen = jnp.einsum(
        "gcrl,clk->gcrk", listed, ref_library, preferred_element_type=jnp.float32
    ).astype(jnp.bfloat16)
    piece = chosen.shape[-1]
    ref_send = chosen.reshape(shards, ref_block, piece)
    ref_got = lax.all_to_all(ref_send, "shard", 0, 0, tiled=True)
    flattened = forward_spectra(particles).reshape(slots_here, -1)
    source = (
        jnp.zeros((positions,), jnp.int32)
        .at[jnp.where(slot_target >= 0, slot_target, positions)]
        .set(jnp.arange(every_slot, dtype=jnp.int32), mode="drop")
    )
    my_sources = lax.dynamic_slice_in_dim(source, my_pblock * part_block, part_block, 0)
    flattened, ref_got, bin_ids = lax.optimization_barrier(
        (flattened, ref_got, slot_defocus_level[my_sources])
    )
    contrast = lax.optimization_barrier(particle_contrast(bin_ids, defocus))
    refs = ref_got.transpose(1, 0, 2).reshape(ref_block, shards * piece)
    pieces = lax.all_to_all(flattened, "shard", split_axis=1, concat_axis=0, tiled=True)

    energy_ref = reference_energy(contrast, refs)
    refs_wide = refs.reshape(ref_block, 2, BAND, BAND * BAND).astype(jnp.float32)
    if r_groups % 2 == 0:
        half = shards // 2
        core = my_index % 2
        groups = [[2 * m + q for m in range(half)] for q in range(2)]
        picked = pieces[source].reshape(p_groups, 1, part_block, piece)
        picked, contrast, energy_ref = lax.optimization_barrier(
            (picked, contrast.reshape(part_block, BAND, BAND * BAND), energy_ref)
        )
        part_send = jnp.broadcast_to(
            picked, (p_groups, r_groups // 2, part_block, piece)
        ).reshape(half, part_block, piece)
        mine = lax.all_to_all(part_send, "shard", 0, 0, tiled=True, axis_index_groups=groups)
        mine, refs_wide = lax.optimization_barrier((mine, refs_wide))
        other = lax.ppermute(mine, "shard", [(d, d ^ 1) for d in range(shards)])
        even = jnp.where(core == 0, mine, other)
        odd = jnp.where(core == 0, other, mine)
        part_got = jnp.stack([even, odd], axis=1).reshape(shards, part_block, piece)
    else:
        part_send = jnp.broadcast_to(
            pieces[source].reshape(p_groups, 1, part_block, piece),
            (p_groups, r_groups, part_block, piece),
        ).reshape(shards, part_block, piece)
        part_got = lax.all_to_all(part_send, "shard", 0, 0, tiled=True)
    spectra = part_got.transpose(1, 0, 2).reshape(part_block, -1)
    block_scores = score_block(spectra, contrast, energy_ref, refs_wide)

    targets = slot_target.reshape(shards, slots_here)
    in_block = (targets >= 0) & (targets // part_block == my_pblock)
    rows = block_scores[jnp.clip(targets - my_pblock * part_block, 0, part_block - 1)][..., 0]
    back_send = jnp.where(in_block[:, :, None], rows, jnp.float32(0.0))
    back_got = lax.all_to_all(back_send, "shard", 0, 0, tiled=True)
    scores = (
        back_got.reshape(p_groups, r_groups, slots_here, ref_block)
        .sum(axis=0)
        .transpose(1, 0, 2)
        .reshape(slots_here, classes, rotations)
    )
    return (scores, jnp.max(scores, axis=2))


def solution(mesh):
    in_specs = (
        P(("groups", "shard"), None, None),
        P("groups"),
        P("groups"),
        P("groups"),
        P("groups", None, "shard"),
        P("groups", None),
    )
    out_specs = (P(("groups", "shard"), None, None), P(("groups", "shard"), None))
    return jax.shard_map(
        per_device, mesh=mesh, in_specs=in_specs, out_specs=out_specs, check_vma=False
    )
```

```python
import numpy as np
import jax
import jax.numpy as jnp
from jax import lax
from jax.experimental import pallas as pl
from jax.experimental.pallas import tpu as pltpu
from jax.sharding import PartitionSpec as P

BOX = 64
BAND = 32
SHIFTS = 8
PART_DEV = 1


def signed_band(band_size):
    return jnp.arange(band_size, dtype=jnp.int32) - band_size // 2


def table_pair(outer_loop_index, inner_index, box_edge):
    phase_index = outer_loop_index[:, None] * inner_index[None, :] % box_edge
    angles = phase_index.astype(jnp.float32) * (2.0 * jnp.pi / box_edge)
    return (jnp.cos(angles).astype(jnp.bfloat16), jnp.sin(angles).astype(jnp.bfloat16))


def spectral_product(form, left, right):
    return jnp.einsum(form, left, right, preferred_element_type=jnp.float32)


def forward_spectra(volumes):
    batch_size, box_edge = (volumes.shape[0], volumes.shape[1])
    cosine_forward, sine_forward = table_pair(
        signed_band(BAND), jnp.arange(box_edge, dtype=jnp.int32), box_edge
    )
    density_volume = volumes.astype(jnp.bfloat16)
    leading_real = spectral_product("qw,rwl->rql", cosine_forward, density_volume).astype(
        jnp.bfloat16
    )
    leading_imaginary = (-spectral_product("qw,rwl->rql", sine_forward, density_volume)).astype(
        jnp.bfloat16
    )
    leading_real = leading_real.reshape(batch_size, BAND, box_edge, box_edge)
    leading_imaginary = leading_imaginary.reshape(batch_size, BAND, box_edge, box_edge)
    second_real = (
        spectral_product("jy,nkyz->nkjz", cosine_forward, leading_real)
        + spectral_product("jy,nkyz->nkjz", sine_forward, leading_imaginary)
    ).astype(jnp.bfloat16)
    second_imag = (
        spectral_product("jy,nkyz->nkjz", cosine_forward, leading_imaginary)
        - spectral_product("jy,nkyz->nkjz", sine_forward, leading_real)
    ).astype(jnp.bfloat16)
    third_real = spectral_product("nkjz,lz->nkjl", second_real, cosine_forward) + spectral_product(
        "nkjz,lz->nkjl", second_imag, sine_forward
    )
    third_imag = spectral_product("nkjz,lz->nkjl", second_imag, cosine_forward) - spectral_product(
        "nkjz,lz->nkjl", second_real, sine_forward
    )
    spectrum = jnp.stack([third_real, third_imag], axis=1).astype(jnp.bfloat16)
    return spectrum.reshape(batch_size, 2, BAND * BAND * BAND)


def plane_table():
    k = np.arange(BAND) - BAND // 2
    t = np.arange(SHIFTS) - SHIFTS // 2
    phase = (
        t[None, None, :, None] * k[:, None, None, None]
        + t[None, None, None, :] * k[None, :, None, None]
    ) % BOX
    angles = phase.astype(np.float32) * np.float32(2.0 * np.pi / BOX)
    shape = (BAND * BAND, SHIFTS * SHIFTS)
    cosine = np.cos(angles).reshape(shape)
    sine = np.sin(angles).reshape(shape)
    upper = np.concatenate([cosine, sine], axis=1)
    lower = np.concatenate([-sine, cosine], axis=1)
    return jnp.asarray(np.concatenate([upper, lower], axis=0), dtype=jnp.bfloat16)


def shift_tables(n_ref):
    k = np.arange(BAND) - BAND // 2
    t = np.arange(SHIFTS) - SHIFTS // 2
    angles = ((t[:, None] * k[None, :]) % BOX).astype(np.float32) * np.float32(2.0 * np.pi / BOX)
    eye = np.eye(n_ref, dtype=np.float32)
    def rounded(x):
        return jnp.asarray(x, dtype=jnp.bfloat16).astype(jnp.float32)
    return rounded(np.kron(eye, np.cos(angles))), rounded(np.kron(eye, np.sin(angles)))


def correlation_kernel(s_ref, g_ref, c_ref, t_ref, ec_ref, es_ref, r_ref, o_ref, p_s):
    n_ref = c_ref.shape[0]
    plane = BAND * BAND
    contrast = g_ref[0]
    s_real = s_ref[0, 0].astype(jnp.float32)
    s_imag = s_ref[0, 1].astype(jnp.float32)
    w_real = (contrast * s_real).astype(jnp.bfloat16).astype(jnp.float32)
    w_imag = (-(contrast * s_imag)).astype(jnp.bfloat16).astype(jnp.float32)
    for j in range(n_ref):
        c_real = c_ref[j, 0]
        c_imag = c_ref[j, 1]
        rows = slice(j * BAND, (j + 1) * BAND)
        p_s[rows, :plane] = (w_real * c_real - w_imag * c_imag).astype(jnp.bfloat16)
        p_s[rows, plane:] = (w_real * c_imag + w_imag * c_real).astype(jnp.bfloat16)
    planes = jnp.dot(p_s[...], t_ref[...], preferred_element_type=jnp.float32)
    first = jnp.dot(ec_ref[...], planes, preferred_element_type=jnp.float32,
                    precision=lax.Precision.DEFAULT)
    second = jnp.dot(es_ref[...], planes, preferred_element_type=jnp.float32,
                     precision=lax.Precision.DEFAULT)
    half = SHIFTS * SHIFTS
    correlation = first - pltpu.roll(second, half, 1)
    lane = lax.broadcasted_iota(jnp.int32, correlation.shape, 1)
    correlation = jnp.where(lane < half, correlation, -jnp.inf)
    per_row = jnp.max(correlation.reshape(n_ref, SHIFTS, 2 * half), axis=1)
    peak = jnp.max(per_row, axis=1, keepdims=True)
    power = jnp.sum(s_real * s_real + s_imag * s_imag, axis=0, keepdims=True)
    energy_particle = jnp.sum(power, axis=1, keepdims=True)
    energy_ref = r_ref[0][:, 0:1]
    score = float(BAND) ** 1.5 * peak * lax.rsqrt(energy_particle * energy_ref + 1e-06)
    o_ref[0] = jnp.broadcast_to(score, (n_ref, 2 * half))


def peak_correlations(spectra, contrast, refs, energy_ref):
    n_part = spectra.shape[0]
    n_ref = refs.shape[0]
    plane = BAND * BAND
    e_cos, e_sin = shift_tables(n_ref)
    width = 2 * SHIFTS * SHIFTS
    scores = pl.pallas_call(
        correlation_kernel,
        grid=(n_part,),
        in_specs=[
            pl.BlockSpec((1, 2, BAND, plane), lambda i: (i, 0, 0, 0)),
            pl.BlockSpec((1, BAND, plane), lambda i: (i, 0, 0)),
            pl.BlockSpec((n_ref, 2, BAND, plane), lambda i: (0, 0, 0, 0)),
            pl.BlockSpec((2 * plane, width), lambda i: (0, 0)),
            pl.BlockSpec((n_ref * SHIFTS, n_ref * BAND), lambda i: (0, 0)),
            pl.BlockSpec((n_ref * SHIFTS, n_ref * BAND), lambda i: (0, 0)),
            pl.BlockSpec((1, n_ref, width), lambda i: (i, 0, 0)),
        ],
        out_specs=pl.BlockSpec((1, n_ref, width), lambda i: (i, 0, 0)),
        out_shape=jax.ShapeDtypeStruct((n_part, n_ref, width), jnp.float32),
        scratch_shapes=[pltpu.VMEM((n_ref * BAND, 2 * plane), jnp.bfloat16)],
        cost_estimate=pl.CostEstimate(
            flops=n_part * n_ref * (2 * BAND * 2 * plane * width + 8 * BAND * plane),
            transcendentals=0,
            bytes_accessed=n_part * 8 * BAND * plane + n_ref * 8 * BAND * plane,
        ),
    )(
        spectra, contrast, refs, plane_table(), e_cos, e_sin,
        energy_ref,
    )
    return scores


def particle_contrast(bin_ids, defocus):
    band_index = signed_band(BAND).astype(jnp.float32)
    radius = (
        band_index[:, None, None] ** 2
        + band_index[None, :, None] ** 2
        + band_index[None, None, :] ** 2
    ).reshape(-1) / (BAND / 2) ** 2
    chosen_defocus = jnp.sum(
        jnp.where(
            bin_ids[:, None] == jnp.arange(defocus.shape[0], dtype=jnp.int32)[None, :],
            defocus[None, :],
            jnp.float32(0.0),
        ),
        axis=1,
    )
    return -jnp.sin(chosen_defocus[:, None] * radius[None, :] + 0.07)


def reference_energy(contrast, refs):
    volume_size = BAND * BAND * BAND
    ref_real = refs[:, :volume_size].astype(jnp.float32)
    ref_imag = refs[:, volume_size:].astype(jnp.float32)
    magnitude = ref_real * ref_real + ref_imag * ref_imag
    energy = jnp.sum((contrast * contrast)[:, None, :] * magnitude[None, :, :], axis=2)
    return jnp.broadcast_to(energy[:, :, None], energy.shape + (2 * SHIFTS * SHIFTS,))


def score_block(spectra, contrast, energy_ref, refs):
    n_part = spectra.shape[0]
    n_ref = refs.shape[0]
    shape = (BAND, BAND * BAND)
    return peak_correlations(
        spectra.reshape(n_part, 2, *shape),
        contrast.reshape(n_part, *shape),
        refs,
        energy_ref,
    )


def ref_groups(shards, particles, refs):
    best = None
    for groups in range(1, shards + 1):
        if shards % groups or refs % groups or particles % (shards // groups):
            continue
        cost = particles * groups // shards + refs // groups
        if best is None or cost < best[0]:
            best = (cost, groups)
    return best[1]


def per_device(particles, slot_target, slot_defocus_level, defocus, ref_library, rotation_list):
    shards = lax.axis_size("shard")
    my_index = lax.axis_index("shard")
    slots_here = particles.shape[0]
    positions = PART_DEV * shards
    every_slot = slot_target.shape[0]
    classes, rotations = rotation_list.shape
    n_refs = classes * rotations
    r_groups = ref_groups(shards, positions, n_refs)
    p_groups = shards // r_groups
    part_block = positions // p_groups
    ref_block = n_refs // r_groups
    my_pblock = my_index // r_groups

    library = ref_library.shape[1]
    listed = (rotation_list[:, :, None] == jnp.arange(library, dtype=jnp.int32)).astype(jnp.bfloat16)
    listed = jnp.broadcast_to(listed[None], (p_groups,) + listed.shape)
    chosen = jnp.einsum(
        "gcrl,clk->gcrk", listed, ref_library, preferred_element_type=jnp.float32
    ).astype(jnp.bfloat16)
    piece = chosen.shape[-1]
    ref_send = chosen.reshape(shards, ref_block, piece)
    ref_got = lax.all_to_all(ref_send, "shard", 0, 0, tiled=True)
    flattened = forward_spectra(particles).reshape(slots_here, -1)
    source = (
        jnp.zeros((positions,), jnp.int32)
        .at[jnp.where(slot_target >= 0, slot_target, positions)]
        .set(jnp.arange(every_slot, dtype=jnp.int32), mode="drop")
    )
    my_sources = lax.dynamic_slice_in_dim(source, my_pblock * part_block, part_block, 0)
    flattened, ref_got, bin_ids = lax.optimization_barrier(
        (flattened, ref_got, slot_defocus_level[my_sources])
    )
    contrast = lax.optimization_barrier(particle_contrast(bin_ids, defocus))
    refs = ref_got.transpose(1, 0, 2).reshape(ref_block, shards * piece)
    pieces = lax.all_to_all(flattened, "shard", split_axis=1, concat_axis=0, tiled=True)

    energy_ref = reference_energy(contrast, refs)
    refs_wide = refs.reshape(ref_block, 2, BAND, BAND * BAND).astype(jnp.float32)
    if r_groups % 2 == 0:
        half = shards // 2
        core = my_index % 2
        groups = [[2 * m + q for m in range(half)] for q in range(2)]
        picked = pieces[source].reshape(p_groups, 1, part_block, piece)
        picked, contrast, energy_ref = lax.optimization_barrier(
            (picked, contrast.reshape(part_block, BAND, BAND * BAND), energy_ref)
        )
        part_send = jnp.broadcast_to(
            picked, (p_groups, r_groups // 2, part_block, piece)
        ).reshape(half, part_block, piece)
        mine = lax.all_to_all(part_send, "shard", 0, 0, tiled=True, axis_index_groups=groups)
        mine, refs_wide = lax.optimization_barrier((mine, refs_wide))
        other = lax.ppermute(mine, "shard", [(d, d ^ 1) for d in range(shards)])
        pair = lax.dynamic_slice_in_dim(jnp.stack([mine, other, mine], axis=1), core, 2, 1)
        part_got = pair.reshape(shards, part_block, piece)
    else:
        part_send = jnp.broadcast_to(
            pieces[source].reshape(p_groups, 1, part_block, piece),
            (p_groups, r_groups, part_block, piece),
        ).reshape(shards, part_block, piece)
        part_got = lax.all_to_all(part_send, "shard", 0, 0, tiled=True)
    spectra = part_got.transpose(1, 0, 2).reshape(part_block, -1)
    block_scores = score_block(spectra, contrast, energy_ref, refs_wide)

    targets = slot_target.reshape(shards, slots_here)
    in_block = (targets >= 0) & (targets // part_block == my_pblock)
    rows = block_scores[jnp.clip(targets - my_pblock * part_block, 0, part_block - 1)][..., 0]
    back_send = jnp.where(in_block[:, :, None], rows, jnp.float32(0.0))
    back_got = lax.all_to_all(back_send, "shard", 0, 0, tiled=True)
    scores = (
        back_got.reshape(p_groups, r_groups, slots_here, ref_block)
        .sum(axis=0)
        .transpose(1, 0, 2)
        .reshape(slots_here, classes, rotations)
    )
    return (scores, jnp.max(scores, axis=2))


def solution(mesh):
    in_specs = (
        P(("groups", "shard"), None, None),
        P("groups"),
        P("groups"),
        P("groups"),
        P("groups", None, "shard"),
        P("groups", None),
    )
    out_specs = (P(("groups", "shard"), None, None), P(("groups", "shard"), None))
    return jax.shard_map(
        per_device, mesh=mesh, in_specs=in_specs, out_specs=out_specs, check_vma=False
    )
```
